128 devices in a mesh: segment: 8 (over x, core), blk: 16 (over y, z).
Axes of the slice: x: 4, y: 4, z: 4, core: 2. Of those that a mesh axis runs over, the one named last changes fastest.
Arguments:
- fresh: bfloat16 [256, 4096], replicated, may hold values from -6 to 6
- previous: bfloat16 [8, 256, 4096], P('segment'), may hold values from -6 to 6
- span_index: int32 [8], P('segment'), may hold values from 0 to 7
- cache_counts: int32 [8, 16], P('segment'), may hold values from 1 to 2048, 16384 in all within a row
- norm_gain: float32 [8, 4096], P('segment'), may hold values from 0.1 to 1.9
- w_query: bfloat16 [8, 4096, 4096], P('segment', None, 'blk'), may hold values from -0.375 to 0.375
- w_keyval: bfloat16 [8, 4096, 2048], P('segment', None, 'blk'), may hold values from -0.09375 to 0.09375
- w_out: bfloat16 [8, 4096, 4096], P('segment', 'blk'), may hold values from -0.09375 to 0.09375
- cache_keys: bfloat16 [8, 32768, 1024], P('segment', 'blk'), may hold values from -220 to 220
- cache_values: bfloat16 [8, 32768, 1024], P('segment', 'blk'), may hold values from -6 to 6
Outputs:
- mixed: bfloat16 [8, 256, 4096], P('segment')
The draws below stay inside these ranges and needn't reach their ends.
Inputs may be any that keep to these rules, and one draw needn't show every extreme that they name: Each row of cache_counts sums to 16384 and its largest entry is 2048.
All inputs are finite; a program needn't handle non-finite values.
Results may differ from the reference program's by a relative error of at most 0.012.
Values may be sent and summed in bfloat16 or wider, within the bound.
No kernel may reach another device: no remote copies, remote signals or barrier semaphores. Data moves between devices by JAX's collectives and lax.ppermute only.
A program may use at most 128 MiB of HBM per device.

```python
import math
import jax
import jax.numpy as jnp
import numpy as np
from jax import lax

D = 4096
HEADS = 32
KVH = 8
HD = 128
SPAN = 256
CACHE_DEV = 2048
LAYERS = 8
CACHE = 32768
N_BLK = 16


def draw_cache_keys(key, part):
    base_key = jax.random.fold_in(key, 0)
    key_rows = jnp.clip(jax.random.normal(base_key, (LAYERS, CACHE, KVH * HD), jnp.float32), -6.0, 6.0)
    return key_rows.astype(jnp.bfloat16)


def plant(entries, own_key, low, largest):
    longest = entries.shape.index(max(entries.shape))
    spots = []
    for shift in (0, 1):
        where = [jax.random.randint(jax.random.fold_in(own_key, axis), (), 0, length) for axis, length in enumerate(entries.shape)]
        where[longest] = (where[longest] + shift) % entries.shape[longest]
        spots.append(tuple(where))
    return entries.at[spots[0]].set(low).at[spots[1]].set(largest)


def steps_of(key, dims, pieces, least, largest):
    def one(position, blocks):
        heights = jax.random.uniform(jax.random.fold_in(jax.random.fold_in(key, 6), position), (blocks,), jnp.float32, least / len(pieces), largest / len(pieces))
        return jnp.repeat(jnp.exp(heights), dims[position] // blocks).reshape((-1,) + (1,) * (len(dims) - position - 1))

    factor_of = one(*pieces[0])
    for cut in pieces[1:]:
        factor_of = factor_of * one(*cut)
    return factor_of


def profile(count, total, most, lean):
    portions = [(1 << 20) // math.isqrt(grade ** lean) + 1 for grade in range(2, count + 1)]
    rest, given = total - most - (count - 1), [1] * (count - 1)
    while rest > 0:
        candidates = [i for i in range(count - 1) if given[i] < most]
        whole, budget = sum([portions[i] for i in candidates]), rest
        for i in candidates:
            extra = min(most - given[i], max(1, budget * portions[i] // whole), rest)
            given[i] = given[i] + extra
            rest = rest - extra
    return np.array([most] + given)


def ragged(own_key, count, total, limit, lean):
    if count == 2:
        one = jax.random.randint(own_key, (), max(1, total - limit), min(limit, total - 1) + 1)
        return jnp.stack([one, total - one])
    lengths = jnp.asarray(profile(count, total, limit, lean), jnp.int32)
    couples = (count - 1) // 2
    donor, taker = lengths[1:1 + 2 * couples:2], lengths[2:2 + 2 * couples:2]
    room = jnp.minimum(donor - 1, limit - taker)
    shifted = jax.random.randint(jax.random.fold_in(own_key, 1), (couples,), 0, 1 << 20) % (room + 1)
    lengths = lengths.at[1:1 + 2 * couples:2].set(donor - shifted).at[2:2 + 2 * couples:2].set(taker + shifted)
    return lengths[jax.random.permutation(jax.random.fold_in(own_key, 2), count)]


def normal_values(own_key, shape, spread, most, shards=(), kind=jnp.bfloat16):
    array = jax.random.normal(own_key, shape, jnp.float32) * spread
    if len(shards) > 0:
        array = steps_of(own_key, shape, shards, -0.22, 0.18) * array
    return jnp.clip(array, min=-most, max=most).astype(kind)


def setup_inputs(seed: int = 0) -> dict:
    seeds = jax.random.split(jax.random.key(seed), 11)
    return {
        "fresh": normal_values(seeds[0], (SPAN, D), 1.0, 6.0),
        "previous": normal_values(seeds[1], (LAYERS, SPAN, D), 1.0, 6.0, ((0, 8),)),
        "span_index": plant(jax.random.randint(seeds[2], (LAYERS,), 0, 8), jax.random.fold_in(seeds[2], 1), 0, 7).astype(jnp.int32),
        "cache_counts": jax.vmap(lambda own: ragged(own, N_BLK, CACHE_DEV * N_BLK // 2, CACHE_DEV, 2))(jax.random.split(seeds[3], LAYERS)).reshape((LAYERS, N_BLK)).astype(jnp.int32),
        "norm_gain": jnp.clip(1.0 + 0.18 * jax.random.normal(seeds[4], (LAYERS, D), jnp.float32), 0.1, 1.9),
        "w_query": normal_values(seeds[5], (LAYERS, D, HEADS * HD), (D // 16) ** -0.5, 0.375, ((0, 8), (2, 16))),
        "w_keyval": normal_values(seeds[6], (LAYERS, D, 2 * KVH * HD), D ** -0.5, 0.09375, ((0, 8), (2, 16))),
        "w_out": normal_values(seeds[7], (LAYERS, HEADS * HD, D), (HEADS * HD) ** -0.5, 0.09375, ((0, 8), (1, 16))),
        "cache_keys": draw_cache_keys(jax.random.fold_in(seeds[10], 71), 0),
        "cache_values": normal_values(seeds[9], (LAYERS, CACHE, KVH * HD), 1.0, 6.0, ((0, 8), (1, 16))),
    }


ROPE_BASE = 500000.0
EPSILON = 1e-05

def rotate(projected, first_span):
    length = projected.shape[0]
    half_width = projected.shape[-1] // 2
    positions = (first_span * length + jnp.arange(length, dtype=jnp.int32)).astype(jnp.float32)
    inverse = ROPE_BASE ** (-(jnp.arange(half_width, dtype=jnp.float32) * 2.0) / projected.shape[-1])
    angles = positions[:, None] * inverse[None, :]
    cosine = jnp.cos(angles)[:, None, :]
    sine_table = jnp.sin(angles)[:, None, :]
    left_part = projected[..., :half_width]
    right_part = projected[..., half_width:]
    return jnp.concatenate([left_part * cosine - right_part * sine_table, right_part * cosine + left_part * sine_table], axis=-1)

def attend(queries, key_rows, value_rows, allowed):
    scores = jnp.einsum('grd,gcd->grc', queries, key_rows) * HD ** (-0.5)
    scores = jnp.where(allowed[None], scores, -jnp.inf)
    highest = lax.optimization_barrier(jnp.max(scores, axis=-1, keepdims=True))
    weights = jnp.exp(scores - highest)
    totals = lax.optimization_barrier(jnp.sum(weights, axis=-1, keepdims=True))
    rounded = lax.optimization_barrier(weights.astype(jnp.bfloat16)).astype(jnp.float32)
    partial_out = (jnp.einsum('grc,gcd->grd', rounded, value_rows) / totals).astype(jnp.bfloat16)
    return (partial_out, (highest + jnp.log(totals))[..., 0])

def layer_step(current, first_span, counts, gain, query_weight, keyval_weight, out_weight, cached_keys, cached_values):
    widened = current.astype(jnp.float32)
    span_rows = current.shape[0]
    width = current.shape[1]
    group_size = HEADS // KVH
    normed = (widened * lax.rsqrt(lax.optimization_barrier(jnp.mean(widened * widened, axis=-1, keepdims=True)) + EPSILON) * gain.astype(jnp.float32)).astype(jnp.bfloat16)
    queries = jnp.dot(normed, query_weight, preferred_element_type=jnp.float32).reshape(span_rows, HEADS, HD)
    queries = rotate(queries, first_span).astype(jnp.bfloat16)
    projected = jnp.dot(normed, keyval_weight, preferred_element_type=jnp.float32).reshape(span_rows, KVH, 2, HD)
    own_keys = rotate(projected[:, :, 0, :], first_span).astype(jnp.bfloat16)
    own_values = projected[:, :, 1, :].astype(jnp.bfloat16)
    grouped = queries.astype(jnp.float32).reshape(span_rows, KVH, group_size, HD).transpose(1, 0, 2, 3).reshape(KVH, span_rows * group_size, HD)
    row_tokens = jnp.arange(span_rows * group_size, dtype=jnp.int32) // group_size
    causal = row_tokens[:, None] >= jnp.arange(span_rows, dtype=jnp.int32)[None, :]
    own_out, own_log = attend(grouped, own_keys.astype(jnp.float32).transpose(1, 0, 2), own_values.astype(jnp.float32).transpose(1, 0, 2), causal)

    def shard_part(shard):
        start = (shard * CACHE_DEV).astype(jnp.int32)
        block_keys = lax.dynamic_slice_in_dim(cached_keys, start, CACHE_DEV, 0).astype(jnp.float32).reshape(CACHE_DEV, KVH, HD).transpose(1, 0, 2)
        block_values = lax.dynamic_slice_in_dim(cached_values, start, CACHE_DEV, 0).astype(jnp.float32).reshape(CACHE_DEV, KVH, HD).transpose(1, 0, 2)
        allowed = (jnp.arange(CACHE_DEV, dtype=jnp.int32) < counts[shard])[None, :]
        return attend(grouped, block_keys, block_values, allowed)
    shard_outs, shard_logs = lax.map(shard_part, jnp.arange(N_BLK, dtype=jnp.int32))
    all_outs = jnp.concatenate([own_out[None], shard_outs], axis=0).astype(jnp.float32)
    all_logs = jnp.concatenate([own_log[None], shard_logs], axis=0)
    ceiling = lax.optimization_barrier(jnp.max(all_logs, axis=0))
    factors = jnp.exp(all_logs - ceiling)
    attended = (lax.optimization_barrier(jnp.sum(factors[..., None] * all_outs, axis=0)) / lax.optimization_barrier(jnp.sum(factors, axis=0))[..., None]).astype(jnp.bfloat16)
    attended = attended.reshape(KVH, span_rows, group_size, HD).transpose(1, 0, 2, 3).reshape(span_rows, HEADS * HD)
    per_group = HEADS // N_BLK * HD
    head_terms = jnp.einsum('tnp,npd->ntd', attended.astype(jnp.float32).reshape(span_rows, N_BLK, per_group), out_weight.astype(jnp.float32).reshape(N_BLK, per_group, width))
    head_terms = lax.optimization_barrier(head_terms.astype(jnp.bfloat16)).astype(jnp.float32)
    return (widened + lax.optimization_barrier(jnp.sum(head_terms, axis=0))).astype(jnp.bfloat16)

def reference(fresh, previous, span_index, cache_counts, norm_gain, w_query, w_keyval, w_out, cache_keys, cache_values):
    results = []
    for segment_no in range(LAYERS):
        current = fresh if segment_no == 0 else previous[segment_no - 1]
        results.append(layer_step(current, span_index[segment_no], cache_counts[segment_no], norm_gain[segment_no], w_query[segment_no], w_keyval[segment_no], w_out[segment_no], cache_keys[segment_no], cache_values[segment_no]))
    return jnp.stack(results)
```

```python
import jax
import jax.numpy as jnp
from jax import lax
from jax.sharding import PartitionSpec as P
from jax.experimental import pallas as pl
from jax.experimental.pallas import tpu as pltpu

KVH = 8
HD = 128


ROPE_BASE = 500000.0
EPSILON = 1e-05


def passed_along(block, axis, distance):
    devices = range(lax.axis_size(axis))
    route = [(i - distance, i) for i in devices if i - distance in devices]
    return lax.ppermute(block, axis, route)


def swapped(block, axis, distance):
    count = lax.axis_size(axis)
    route = []
    for low in range(count):
        high = low | 1 << distance
        if high != low and high < count:
            route += [(low, high), (high, low)]
    return lax.ppermute(block, axis, route)


def rotate(projected, first_span):
    length = projected.shape[0]
    half_width = projected.shape[-1] // 2
    positions = (first_span * length + jnp.arange(length, dtype=jnp.int32)).astype(jnp.float32)
    inverse = ROPE_BASE ** (
        -(jnp.arange(half_width, dtype=jnp.float32) * 2.0) / projected.shape[-1]
    )
    angles = positions[:, None] * inverse[None, :]
    cosine = jnp.cos(angles)[:, None, :]
    sine_table = jnp.sin(angles)[:, None, :]
    left_part = projected[..., :half_width]
    right_part = projected[..., half_width:]
    return jnp.concatenate(
        [
            left_part * cosine - right_part * sine_table,
            right_part * cosine + left_part * sine_table,
        ],
        axis=-1,
    )


def attend_rows(query_rows, key_rows, value_rows, allowed):
    scores = lax.dot_general(
        query_rows, key_rows, (((1,), (1,)), ((), ())), preferred_element_type=jnp.float32
    ) * query_rows.shape[-1] ** (-0.5)
    scores = jnp.where(allowed, scores, -jnp.inf)
    highest = jnp.max(scores, axis=-1, keepdims=True)
    weights = jnp.exp(scores - highest)
    totals = jnp.sum(weights, axis=-1, keepdims=True)
    partial_out = (
        jnp.dot(weights.astype(jnp.bfloat16), value_rows, preferred_element_type=jnp.float32)
        / totals
    ).astype(jnp.bfloat16)
    return (partial_out, (highest + jnp.log(totals))[:, 0])


def cache_kernel(live_ref, q_ref, k_ref, v_ref, out_ref, log_ref):
    live = live_ref[0]
    keys = k_ref[...]
    values = v_ref[...]
    visible = lax.broadcasted_iota(jnp.int32, (1, keys.shape[0]), 1) < live
    for src in range(q_ref.shape[0]):
        for h in range(q_ref.shape[2] // HD):
            q = q_ref[src, :, h * HD:(h + 1) * HD]
            scores = lax.dot_general(
                q, keys, (((1,), (1,)), ((), ())), preferred_element_type=jnp.float32
            ) * HD ** (-0.5)
            scores = jnp.where(visible, scores, -jnp.inf)
            highest = jnp.max(scores, axis=-1, keepdims=True)
            weights = jnp.exp(scores - highest)
            totals = jnp.sum(weights, axis=-1, keepdims=True)
            part = jnp.dot(weights.astype(jnp.bfloat16), values, preferred_element_type=jnp.float32)
            out_ref[src, :, h * HD:(h + 1) * HD] = (part / totals).astype(out_ref.dtype)
            log_ref[src, :, h:h + 1] = highest + jnp.log(totals)


def cache_attention(live, every_query, cached_keys, cached_values):
    sources, span_rows, width = every_query.shape
    heads_here = width // HD
    kv_heads = cached_keys.shape[1] // HD
    per_head = sources // kv_heads
    rows = cached_keys.shape[0]
    grid_spec = pltpu.PrefetchScalarGridSpec(
        num_scalar_prefetch=1,
        grid=(kv_heads,),
        in_specs=[
            pl.BlockSpec((per_head, span_rows, width), lambda g, live: (g, 0, 0)),
            pl.BlockSpec((rows, HD), lambda g, live: (0, g)),
            pl.BlockSpec((rows, HD), lambda g, live: (0, g)),
        ],
        out_specs=[
            pl.BlockSpec((per_head, span_rows, width), lambda g, live: (g, 0, 0)),
            pl.BlockSpec((per_head, span_rows, heads_here), lambda g, live: (g, 0, 0)),
        ],
    )
    return pl.pallas_call(
        cache_kernel,
        grid_spec=grid_spec,
        out_shape=[
            jax.ShapeDtypeStruct((sources, span_rows, width), jnp.bfloat16),
            jax.ShapeDtypeStruct((sources, span_rows, heads_here), jnp.float32),
        ],
    )(live, every_query, cached_keys, cached_values)


def shards(
    fresh,
    previous,
    span_index,
    cache_counts,
    norm_gain,
    w_query,
    w_keyval,
    w_out,
    cache_keys,
    cache_values,
):
    blocks = lax.axis_size("blk")
    position = lax.axis_index("blk")
    span_rows = fresh.shape[0]
    arrived = passed_along(previous[0], "segment", 1)
    current = jnp.where(lax.axis_index("segment") == 0, fresh, arrived)
    widened = current.astype(jnp.float32)
    normed = (
        widened
        * lax.rsqrt(jnp.mean(widened * widened, axis=-1, keepdims=True) + EPSILON)
        * norm_gain[0]
    ).astype(jnp.bfloat16)
    first_span = span_index[0]
    heads_here = w_query.shape[2] // HD
    ratio = blocks // KVH
    queries = jnp.dot(normed, w_query[0], preferred_element_type=jnp.float32).reshape(
        span_rows, heads_here, HD
    )
    queries = rotate(queries, first_span).astype(jnp.bfloat16).reshape(span_rows, heads_here * HD)
    projected = jnp.dot(normed, w_keyval[0], preferred_element_type=jnp.float32)
    odd_member = position % 2 == 1
    as_key = rotate(projected[:, None, :], first_span)[:, 0, :].astype(jnp.bfloat16)
    mine = jnp.where(odd_member, projected.astype(jnp.bfloat16), as_key)
    partner = swapped(mine, "blk", 0)
    own_keys = jnp.where(odd_member, partner, mine)
    own_values = jnp.where(odd_member, mine, partner)
    query_rows = queries.reshape(span_rows * heads_here, HD)
    row_tokens = jnp.arange(span_rows * heads_here, dtype=jnp.int32) // heads_here
    causal = row_tokens[:, None] >= jnp.arange(span_rows, dtype=jnp.int32)[None, :]
    own_out, own_log = attend_rows(query_rows, own_keys, own_values, causal)
    own_out = own_out.reshape(span_rows, heads_here * HD)
    own_log = own_log.reshape(span_rows, heads_here)
    every_query = lax.all_to_all(
        jnp.broadcast_to(queries[None], (blocks,) + queries.shape), "blk", 0, 0, tiled=True
    ).reshape(blocks, span_rows, heads_here * HD)
    live = cache_counts[0, position].reshape(1)
    held_outs, held_logs = cache_attention(live, every_query, cache_keys[0], cache_values[0])
    shard_outs = lax.all_to_all(held_outs, "blk", split_axis=0, concat_axis=0, tiled=True)
    shard_logs = lax.all_to_all(held_logs, "blk", split_axis=0, concat_axis=0, tiled=True)
    all_outs = (
        jnp.concatenate([own_out[None], shard_outs], axis=0)
        .astype(jnp.float32)
        .reshape(blocks + 1, span_rows, heads_here, HD)
    )
    all_logs = jnp.concatenate([own_log[None], shard_logs], axis=0)
    ceiling = jnp.max(all_logs, axis=0)
    factors = jnp.exp(all_logs - ceiling)
    attended = (
        jnp.sum(factors[..., None] * all_outs, axis=0) / jnp.sum(factors, axis=0)[..., None]
    ).astype(jnp.bfloat16)
    attended = attended.reshape(span_rows, heads_here * HD)
    head_terms = jnp.dot(attended, w_out[0], preferred_element_type=jnp.float32).astype(jnp.bfloat16)
    chunk = span_rows // blocks
    gathered_terms = lax.all_to_all(
        head_terms.reshape(blocks, chunk, -1), "blk", 0, 0, tiled=True
    )
    own_rows = lax.dynamic_slice_in_dim(widened, position * chunk, chunk, 0)
    mixed_rows = (own_rows + jnp.sum(gathered_terms.astype(jnp.float32), axis=0)).astype(jnp.bfloat16)
    mixed = lax.all_to_all(
        jnp.broadcast_to(mixed_rows[None], (blocks,) + mixed_rows.shape), "blk", 0, 0, tiled=True
    ).reshape(span_rows, -1)
    return mixed[None]


def solution(mesh):
    placed = (
        P(),
        P("segment", None, None),
        P("segment"),
        P("segment", None),
        P("segment", None),
        P("segment", None, "blk"),
        P("segment", None, "blk"),
        P("segment", "blk", None),
        P("segment", "blk", None),
        P("segment", "blk", None),
    )
    return jax.shard_map(
        shards, mesh=mesh, in_specs=placed, out_specs=P("segment", None, None), check_vma=False
    )
```

```python
import jax
import jax.numpy as jnp
from jax import lax
from jax.sharding import PartitionSpec as P
from jax.experimental import pallas as pl
from jax.experimental.pallas import tpu as pltpu

KVH = 8
HD = 128


ROPE_BASE = 500000.0
EPSILON = 1e-05


def passed_along(block, axis, distance):
    devices = range(lax.axis_size(axis))
    route = [(i - distance, i) for i in devices if i - distance in devices]
    return lax.ppermute(block, axis, route)


def swapped(block, axis, distance):
    count = lax.axis_size(axis)
    route = []
    for low in range(count):
        high = low | 1 << distance
        if high != low and high < count:
            route += [(low, high), (high, low)]
    return lax.ppermute(block, axis, route)


def rotate(projected, first_span):
    length = projected.shape[0]
    half_width = projected.shape[-1] // 2
    positions = (first_span * length + jnp.arange(length, dtype=jnp.int32)).astype(jnp.float32)
    inverse = ROPE_BASE ** (
        -(jnp.arange(half_width, dtype=jnp.float32) * 2.0) / projected.shape[-1]
    )
    angles = positions[:, None] * inverse[None, :]
    cosine = jnp.cos(angles)[:, None, :]
    sine_table = jnp.sin(angles)[:, None, :]
    left_part = projected[..., :half_width]
    right_part = projected[..., half_width:]
    return jnp.concatenate(
        [
            left_part * cosine - right_part * sine_table,
            right_part * cosine + left_part * sine_table,
        ],
        axis=-1,
    )


def attend_rows(query_rows, key_rows, value_rows, allowed):
    scores = lax.dot_general(
        query_rows, key_rows, (((1,), (1,)), ((), ())), preferred_element_type=jnp.float32
    ) * query_rows.shape[-1] ** (-0.5)
    scores = jnp.where(allowed, scores, -jnp.inf)
    highest = jnp.max(scores, axis=-1, keepdims=True)
    weights = jnp.exp(scores - highest)
    totals = jnp.sum(weights, axis=-1, keepdims=True)
    partial_out = (
        jnp.dot(weights.astype(jnp.bfloat16), value_rows, preferred_element_type=jnp.float32)
        / totals
    ).astype(jnp.bfloat16)
    return (partial_out, (highest + jnp.log(totals))[:, 0])


def cache_kernel(live_ref, q_ref, k_ref, v_ref, out_ref):
    live = live_ref[0]
    keys = k_ref[...]
    values = v_ref[...]
    rows = q_ref.shape[1]
    width = out_ref.shape[2]
    visible = lax.broadcasted_iota(jnp.int32, (1, keys.shape[0]), 1) < live
    for src in range(q_ref.shape[0]):
        log_rows = []
        for h in range(q_ref.shape[2] // HD):
            q = q_ref[src, :, h * HD:(h + 1) * HD]
            scores = lax.dot_general(
                q, keys, (((1,), (1,)), ((), ())), preferred_element_type=jnp.float32
            ) * HD ** (-0.5)
            scores = jnp.where(visible, scores, -jnp.inf)
            highest = jnp.max(scores, axis=-1, keepdims=True)
            weights = jnp.exp(scores - highest)
            totals = jnp.sum(weights, axis=-1, keepdims=True)
            part = jnp.dot(weights.astype(jnp.bfloat16), values, preferred_element_type=jnp.float32)
            out_ref[src, :rows, h * HD:(h + 1) * HD] = (part / totals).astype(out_ref.dtype)
            log_col = jnp.broadcast_to(highest + jnp.log(totals), (rows, HD))
            rest = jnp.transpose(log_col)[0:1, :]
            for _ in range(3):
                piece = rest.astype(jnp.bfloat16).astype(jnp.float32)
                log_rows.append(piece)
                rest = rest - piece
        if rows < width:
            log_rows = [jnp.concatenate([r, jnp.zeros((1, width - rows), jnp.float32)], axis=1) for r in log_rows]
        log_rows += [jnp.zeros((1, width), jnp.float32)] * (out_ref.shape[1] - rows - len(log_rows))
        out_ref[src, rows:, :] = jnp.concatenate(log_rows, axis=0).astype(out_ref.dtype)


LOG_ROWS = 8


def cache_attention(live, every_query, cached_keys, cached_values):
    sources, span_rows, width = every_query.shape
    kv_heads = cached_keys.shape[1] // HD
    per_head = sources // kv_heads
    rows = cached_keys.shape[0]
    grid_spec = pltpu.PrefetchScalarGridSpec(
        num_scalar_prefetch=1,
        grid=(kv_heads,),
        in_specs=[
            pl.BlockSpec((per_head, span_rows, width), lambda g, live: (g, 0, 0)),
            pl.BlockSpec((rows, HD), lambda g, live: (0, g)),
            pl.BlockSpec((rows, HD), lambda g, live: (0, g)),
        ],
        out_specs=pl.BlockSpec((per_head, span_rows + LOG_ROWS, width), lambda g, live: (g, 0, 0)),
    )
    return pl.pallas_call(
        cache_kernel,
        grid_spec=grid_spec,
        out_shape=jax.ShapeDtypeStruct((sources, span_rows + LOG_ROWS, width), jnp.bfloat16),
    )(live, every_query, cached_keys, cached_values)


def shards(
    fresh,
    previous,
    span_index,
    cache_counts,
    norm_gain,
    w_query,
    w_keyval,
    w_out,
    cache_keys,
    cache_values,
):
    blocks = lax.axis_size("blk")
    position = lax.axis_index("blk")
    span_rows = fresh.shape[0]
    chunks = 2
    rows = span_rows // chunks
    first_span = span_index[0]
    heads_here = w_query.shape[2] // HD
    odd_member = position % 2 == 1
    live = cache_counts[0, position].reshape(1)
    first_segment = lax.axis_index("segment") == 0
    key_parts, value_parts, results = [], [], []
    for c in range(chunks):
        arrived = passed_along(previous[0, c * rows:(c + 1) * rows], "segment", 1)
        current = jnp.where(first_segment, fresh[c * rows:(c + 1) * rows], arrived)
        widened = current.astype(jnp.float32)
        normed = (
            widened
            * lax.rsqrt(jnp.mean(widened * widened, axis=-1, keepdims=True) + EPSILON)
            * norm_gain[0]
        ).astype(jnp.bfloat16)
        chunk_span = first_span * chunks + c
        queries = jnp.dot(normed, w_query[0], preferred_element_type=jnp.float32).reshape(
            rows, heads_here, HD
        )
        queries = rotate(queries, chunk_span).astype(jnp.bfloat16).reshape(rows, heads_here * HD)
        projected = jnp.dot(normed, w_keyval[0], preferred_element_type=jnp.float32)
        as_key = rotate(projected[:, None, :], chunk_span)[:, 0, :].astype(jnp.bfloat16)
        mine = jnp.where(odd_member, projected.astype(jnp.bfloat16), as_key)
        partner = swapped(mine, "blk", 0)
        key_parts.append(jnp.where(odd_member, partner, mine))
        value_parts.append(jnp.where(odd_member, mine, partner))
        every_query = lax.all_to_all(
            jnp.broadcast_to(queries[None], (blocks,) + queries.shape), "blk", 0, 0, tiled=True
        )
        held = cache_attention(live, every_query, cache_keys[0], cache_values[0])
        arrived_parts = lax.all_to_all(held, "blk", split_axis=0, concat_axis=0, tiled=True)
        shard_outs = arrived_parts[:, :rows].astype(jnp.float32).reshape(blocks, rows, heads_here, HD)
        log_parts = arrived_parts[:, rows:rows + 3 * heads_here, :rows].astype(jnp.float32)
        shard_logs = sum(
            log_parts[:, i::3] for i in (2, 1, 0)
        ).transpose(0, 2, 1)
        own_keys = jnp.concatenate(key_parts, axis=0)
        own_values = jnp.concatenate(value_parts, axis=0)
        query_rows = queries.reshape(rows * heads_here, HD)
        row_tokens = c * rows + jnp.arange(rows * heads_here, dtype=jnp.int32) // heads_here
        causal = row_tokens[:, None] >= jnp.arange(own_keys.shape[0], dtype=jnp.int32)[None, :]
        own_out, own_log = attend_rows(query_rows, own_keys, own_values, causal)
        own_out = own_out.reshape(rows, heads_here * HD)
        own_log = own_log.reshape(rows, heads_here)
        all_outs = (
            jnp.concatenate([own_out[None].astype(jnp.float32).reshape(1, rows, heads_here, HD), shard_outs], axis=0)
        )
        all_logs = jnp.concatenate([own_log[None], shard_logs], axis=0)
        ceiling = jnp.max(all_logs, axis=0)
        factors = jnp.exp(all_logs - ceiling)
        attended = (
            jnp.sum(factors[..., None] * all_outs, axis=0) / jnp.sum(factors, axis=0)[..., None]
        ).astype(jnp.bfloat16)
        attended = attended.reshape(rows, heads_here * HD)
        head_terms = jnp.dot(attended, w_out[0], preferred_element_type=jnp.float32).astype(jnp.bfloat16)
        chunk = rows // blocks
        gathered_terms = lax.all_to_all(
            head_terms.reshape(blocks, chunk, -1), "blk", 0, 0, tiled=True
        )
        own_rows = lax.dynamic_slice_in_dim(widened, position * chunk, chunk, 0)
        mixed_rows = (own_rows + jnp.sum(gathered_terms.astype(jnp.float32), axis=0)).astype(jnp.bfloat16)
        results.append(lax.all_to_all(
            jnp.broadcast_to(mixed_rows[None], (blocks,) + mixed_rows.shape), "blk", 0, 0, tiled=True
        ).reshape(rows, -1))
    return jnp.concatenate(results, axis=0)[None]


def solution(mesh):
    placed = (
        P(),
        P("segment", None, None),
        P("segment"),
        P("segment", None),
        P("segment", None),
        P("segment", None, "blk"),
        P("segment", None, "blk"),
        P("segment", "blk", None),
        P("segment", "blk", None),
        P("segment", "blk", None),
    )
    return jax.shard_map(
        shards, mesh=mesh, in_specs=placed, out_specs=P("segment", None, None), check_vma=False
    )
```

```python
import jax
import jax.numpy as jnp
from jax import lax
from jax.sharding import PartitionSpec as P
from jax.experimental import pallas as pl
from jax.experimental.pallas import tpu as pltpu

KVH = 8
HD = 128


ROPE_BASE = 500000.0
EPSILON = 1e-05


def passed_along(block, axis, distance):
    devices = range(lax.axis_size(axis))
    route = [(i - distance, i) for i in devices if i - distance in devices]
    return lax.ppermute(block, axis, route)


def swapped(block, axis, distance):
    count = lax.axis_size(axis)
    route = []
    for low in range(count):
        high = low | 1 << distance
        if high != low and high < count:
            route += [(low, high), (high, low)]
    return lax.ppermute(block, axis, route)


def rotate(projected, first_span):
    length = projected.shape[0]
    half_width = projected.shape[-1] // 2
    positions = (first_span * length + jnp.arange(length, dtype=jnp.int32)).astype(jnp.float32)
    inverse = ROPE_BASE ** (
        -(jnp.arange(half_width, dtype=jnp.float32) * 2.0) / projected.shape[-1]
    )
    angles = positions[:, None] * inverse[None, :]
    cosine = jnp.cos(angles)[:, None, :]
    sine_table = jnp.sin(angles)[:, None, :]
    left_part = projected[..., :half_width]
    right_part = projected[..., half_width:]
    return jnp.concatenate(
        [
            left_part * cosine - right_part * sine_table,
            right_part * cosine + left_part * sine_table,
        ],
        axis=-1,
    )


def attend_rows(query_rows, key_rows, value_rows, allowed):
    scores = lax.dot_general(
        query_rows, key_rows, (((1,), (1,)), ((), ())), preferred_element_type=jnp.float32
    ) * query_rows.shape[-1] ** (-0.5)
    scores = jnp.where(allowed, scores, -jnp.inf)
    highest = jnp.max(scores, axis=-1, keepdims=True)
    weights = jnp.exp(scores - highest)
    totals = jnp.sum(weights, axis=-1, keepdims=True)
    partial_out = (
        jnp.dot(weights.astype(jnp.bfloat16), value_rows, preferred_element_type=jnp.float32)
        / totals
    ).astype(jnp.bfloat16)
    return (partial_out, (highest + jnp.log(totals))[:, 0])


def cache_kernel(live_ref, q_ref, k_ref, v_ref, out_ref):
    live = live_ref[0]
    keys = k_ref[...]
    values = v_ref[...]
    rows = q_ref.shape[1]
    width = out_ref.shape[2]
    visible = lax.broadcasted_iota(jnp.int32, (1, keys.shape[0]), 1) < live
    for src in range(q_ref.shape[0]):
        log_rows = []
        for h in range(q_ref.shape[2] // HD):
            q = q_ref[src, :, h * HD:(h + 1) * HD]
            scores = lax.dot_general(
                q, keys, (((1,), (1,)), ((), ())), preferred_element_type=jnp.float32
            ) * HD ** (-0.5)
            scores = jnp.where(visible, scores, -jnp.inf)
            highest = jnp.max(scores, axis=-1, keepdims=True)
            weights = jnp.exp(scores - highest)
            totals = jnp.sum(weights, axis=-1, keepdims=True)
            part = jnp.dot(weights.astype(jnp.bfloat16), values, preferred_element_type=jnp.float32)
            out_ref[src, :rows, h * HD:(h + 1) * HD] = (part / totals).astype(out_ref.dtype)
            log_col = jnp.broadcast_to(highest + jnp.log(totals), (rows, HD))
            rest = jnp.transpose(log_col)[0:1, :]
            for _ in range(3):
                piece = rest.astype(jnp.bfloat16).astype(jnp.float32)
                log_rows.append(piece)
                rest = rest - piece
        if rows < width:
            log_rows = [jnp.concatenate([r, jnp.zeros((1, width - rows), jnp.float32)], axis=1) for r in log_rows]
        log_rows += [jnp.zeros((1, width), jnp.float32)] * (out_ref.shape[1] - rows - len(log_rows))
        out_ref[src, rows:, :] = jnp.concatenate(log_rows, axis=0).astype(out_ref.dtype)


LOG_ROWS = 8


def cache_attention(live, every_query, cached_keys, cached_values):
    sources, span_rows, width = every_query.shape
    kv_heads = cached_keys.shape[1] // HD
    per_head = sources // kv_heads
    rows = cached_keys.shape[0]
    grid_spec = pltpu.PrefetchScalarGridSpec(
        num_scalar_prefetch=1,
        grid=(kv_heads,),
        in_specs=[
            pl.BlockSpec((per_head, span_rows, width), lambda g, live: (g, 0, 0)),
            pl.BlockSpec((rows, HD), lambda g, live: (0, g)),
            pl.BlockSpec((rows, HD), lambda g, live: (0, g)),
        ],
        out_specs=pl.BlockSpec((per_head, span_rows + LOG_ROWS, width), lambda g, live: (g, 0, 0)),
    )
    return pl.pallas_call(
        cache_kernel,
        grid_spec=grid_spec,
        out_shape=jax.ShapeDtypeStruct((sources, span_rows + LOG_ROWS, width), jnp.bfloat16),
    )(live, every_query, cached_keys, cached_values)


def shards(
    fresh,
    previous,
    span_index,
    cache_counts,
    norm_gain,
    w_query,
    w_keyval,
    w_out,
    cache_keys,
    cache_values,
):
    blocks = lax.axis_size("blk")
    position = lax.axis_index("blk")
    span_rows = fresh.shape[0]
    first_span = span_index[0]
    heads_here = w_query.shape[2] // HD
    odd_member = position % 2 == 1
    live = cache_counts[0, position].reshape(1)
    arrived = passed_along(previous[0], "segment", 1)
    current = jnp.where(lax.axis_index("segment") == 0, fresh, arrived)
    widened = current.astype(jnp.float32)
    normed = (
        widened
        * lax.rsqrt(jnp.mean(widened * widened, axis=-1, keepdims=True) + EPSILON)
        * norm_gain[0]
    ).astype(jnp.bfloat16)
    queries = jnp.dot(normed, w_query[0], preferred_element_type=jnp.float32).reshape(
        span_rows, heads_here, HD
    )
    queries = rotate(queries, first_span).astype(jnp.bfloat16).reshape(span_rows, heads_here * HD)
    projected = jnp.dot(normed, w_keyval[0], preferred_element_type=jnp.float32)
    as_key = rotate(projected[:, None, :], first_span)[:, 0, :].astype(jnp.bfloat16)
    mine = jnp.where(odd_member, projected.astype(jnp.bfloat16), as_key)
    partner = swapped(mine, "blk", 0)
    own_keys = jnp.where(odd_member, partner, mine)
    own_values = jnp.where(odd_member, mine, partner)
    every_query = lax.all_to_all(
        jnp.broadcast_to(queries[None], (blocks,) + queries.shape), "blk", 0, 0, tiled=True
    )
    held = cache_attention(live, every_query, cache_keys[0], cache_values[0])
    arrived_parts = lax.all_to_all(held, "blk", split_axis=0, concat_axis=0, tiled=True)
    log_parts = arrived_parts[:, span_rows:span_rows + 3 * heads_here].astype(jnp.float32)
    shard_logs = sum(log_parts[:, i::3] for i in (2, 1, 0))
    query_rows = queries.reshape(span_rows * heads_here, HD)
    row_tokens = jnp.arange(span_rows * heads_here, dtype=jnp.int32) // heads_here
    causal = row_tokens[:, None] >= jnp.arange(span_rows, dtype=jnp.int32)[None, :]
    own_out, own_log = attend_rows(query_rows, own_keys, own_values, causal)
    own_out = own_out.reshape(span_rows, heads_here * HD)
    own_log = own_log.reshape(span_rows, heads_here).T
    ceiling = jnp.maximum(own_log, jnp.max(shard_logs, axis=0))
    own_factor = jnp.exp(own_log - ceiling)
    factors = jnp.exp(shard_logs - ceiling)
    spread = lambda f: jnp.repeat(jnp.swapaxes(f, -1, -2), HD, axis=-1)
    weighted = spread(own_factor) * own_out.astype(jnp.float32) + jnp.sum(
        spread(factors) * arrived_parts[:, :span_rows].astype(jnp.float32), axis=0
    )
    attended = (weighted / spread(own_factor + jnp.sum(factors, axis=0))).astype(jnp.bfloat16)
    head_terms = jnp.dot(attended, w_out[0], preferred_element_type=jnp.float32).astype(jnp.bfloat16)
    chunk = span_rows // blocks
    gathered_terms = lax.all_to_all(
        head_terms.reshape(blocks, chunk, -1), "blk", 0, 0, tiled=True
    )
    own_rows = lax.dynamic_slice_in_dim(widened, position * chunk, chunk, 0)
    mixed_rows = (own_rows + jnp.sum(gathered_terms.astype(jnp.float32), axis=0)).astype(jnp.bfloat16)
    mixed = lax.all_to_all(
        jnp.broadcast_to(mixed_rows[None], (blocks,) + mixed_rows.shape), "blk", 0, 0, tiled=True
    ).reshape(span_rows, -1)
    return mixed[None]


def solution(mesh):
    placed = (
        P(),
        P("segment", None, None),
        P("segment"),
        P("segment", None),
        P("segment", None),
        P("segment", None, "blk"),
        P("segment", None, "blk"),
        P("segment", "blk", None),
        P("segment", "blk", None),
        P("segment", "blk", None),
    )
    return jax.shard_map(
        shards, mesh=mesh, in_specs=placed, out_specs=P("segment", None, None), check_vma=False
    )
```

```python
import jax
import jax.numpy as jnp
from jax import lax
from jax.sharding import PartitionSpec as P
from jax.experimental import pallas as pl
from jax.experimental.pallas import tpu as pltpu

KVH = 8
HD = 128


ROPE_BASE = 500000.0
EPSILON = 1e-05


def passed_along(block, axis, distance):
    devices = range(lax.axis_size(axis))
    route = [(i - distance, i) for i in devices if i - distance in devices]
    return lax.ppermute(block, axis, route)


def swapped(block, axis, distance):
    count = lax.axis_size(axis)
    route = []
    for low in range(count):
        high = low | 1 << distance
        if high != low and high < count:
            route += [(low, high), (high, low)]
    return lax.ppermute(block, axis, route)


def rotate(projected, first_span):
    length = projected.shape[0]
    half_width = projected.shape[-1] // 2
    positions = (first_span * length + jnp.arange(length, dtype=jnp.int32)).astype(jnp.float32)
    inverse = ROPE_BASE ** (
        -(jnp.arange(half_width, dtype=jnp.float32) * 2.0) / projected.shape[-1]
    )
    angles = positions[:, None] * inverse[None, :]
    cosine = jnp.cos(angles)[:, None, :]
    sine_table = jnp.sin(angles)[:, None, :]
    left_part = projected[..., :half_width]
    right_part = projected[..., half_width:]
    return jnp.concatenate(
        [
            left_part * cosine - right_part * sine_table,
            right_part * cosine + left_part * sine_table,
        ],
        axis=-1,
    )


def attend_rows(query_rows, key_rows, value_rows, allowed):
    scores = lax.dot_general(
        query_rows, key_rows, (((1,), (1,)), ((), ())), preferred_element_type=jnp.float32
    ) * query_rows.shape[-1] ** (-0.5)
    scores = jnp.where(allowed, scores, -jnp.inf)
    highest = jnp.max(scores, axis=-1, keepdims=True)
    weights = jnp.exp(scores - highest)
    totals = jnp.sum(weights, axis=-1, keepdims=True)
    partial_out = (
        jnp.dot(weights.astype(jnp.bfloat16), value_rows, preferred_element_type=jnp.float32)
        / totals
    ).astype(jnp.bfloat16)
    return (partial_out, (highest + jnp.log(totals))[:, 0])


def cache_kernel(live_ref, q_ref, k_ref, v_ref, out_ref):
    live = live_ref[0]
    keys = k_ref[...]
    values = v_ref[...]
    rows = q_ref.shape[1]
    width = out_ref.shape[2]
    visible = lax.broadcasted_iota(jnp.int32, (1, keys.shape[0]), 1) < live
    for src in range(q_ref.shape[0]):
        log_rows = []
        for h in range(q_ref.shape[2] // HD):
            q = q_ref[src, :, h * HD:(h + 1) * HD]
            scores = lax.dot_general(
                q, keys, (((1,), (1,)), ((), ())), preferred_element_type=jnp.float32
            ) * HD ** (-0.5)
            scores = jnp.where(visible, scores, -jnp.inf)
            highest = jnp.max(scores, axis=-1, keepdims=True)
            weights = jnp.exp(scores - highest)
            totals = jnp.sum(weights, axis=-1, keepdims=True)
            part = jnp.dot(weights.astype(jnp.bfloat16), values, preferred_element_type=jnp.float32)
            out_ref[src, :rows, h * HD:(h + 1) * HD] = (part / totals).astype(out_ref.dtype)
            log_col = jnp.broadcast_to(highest + jnp.log(totals), (rows, HD))
            rest = jnp.transpose(log_col)[0:1, :]
            for _ in range(3):
                piece = rest.astype(jnp.bfloat16).astype(jnp.float32)
                log_rows.append(piece)
                rest = rest - piece
        if rows < width:
            log_rows = [jnp.concatenate([r, jnp.zeros((1, width - rows), jnp.float32)], axis=1) for r in log_rows]
        log_rows += [jnp.zeros((1, width), jnp.float32)] * (out_ref.shape[1] - rows - len(log_rows))
        out_ref[src, rows:, :] = jnp.concatenate(log_rows, axis=0).astype(out_ref.dtype)


LOG_ROWS = 8


def cache_attention(live, every_query, cached_keys, cached_values):
    sources, span_rows, width = every_query.shape
    kv_heads = cached_keys.shape[1] // HD
    per_head = sources // kv_heads
    rows = cached_keys.shape[0]
    grid_spec = pltpu.PrefetchScalarGridSpec(
        num_scalar_prefetch=1,
        grid=(kv_heads,),
        in_specs=[
            pl.BlockSpec((per_head, span_rows, width), lambda g, live: (g, 0, 0)),
            pl.BlockSpec((rows, HD), lambda g, live: (0, g)),
            pl.BlockSpec((rows, HD), lambda g, live: (0, g)),
        ],
        out_specs=pl.BlockSpec((per_head, span_rows + LOG_ROWS, width), lambda g, live: (g, 0, 0)),
    )
    return pl.pallas_call(
        cache_kernel,
        grid_spec=grid_spec,
        out_shape=jax.ShapeDtypeStruct((sources, span_rows + LOG_ROWS, width), jnp.bfloat16),
    )(live, every_query, cached_keys, cached_values)


def combine_kernel(parts_ref, own_out_ref, own_log_ref, out_ref):
    sources = parts_ref.shape[0]
    rows = out_ref.shape[0]
    heads_here = out_ref.shape[1] // HD
    log_rows = []
    for b in range(sources):
        packed = parts_ref[b, rows:rows + LOG_ROWS, :].astype(jnp.float32)
        for h in range(heads_here):
            log_rows.append((packed[3 * h + 2:3 * h + 3] + packed[3 * h + 1:3 * h + 2]) + packed[3 * h:3 * h + 1])
    table_rows = 128 * pl.cdiv(len(log_rows), 128)
    which = lax.broadcasted_iota(jnp.int32, (table_rows, rows), 0)
    table = jnp.zeros((table_rows, rows), jnp.float32)
    for j, row in enumerate(log_rows):
        table = jnp.where(which == j, jnp.broadcast_to(row, (table_rows, rows)), table)
    columns = jnp.transpose(table)
    for h in range(heads_here):
        own_log = own_log_ref[:, h:h + 1]
        logs = [columns[:, b * heads_here + h:b * heads_here + h + 1] for b in range(sources)]
        ceiling = own_log
        for lg in logs:
            ceiling = jnp.maximum(ceiling, lg)
        own_factor = jnp.exp(own_log - ceiling)
        weighted = own_factor * own_out_ref[:, h * HD:(h + 1) * HD].astype(jnp.float32)
        total = own_factor
        for b, lg in enumerate(logs):
            factor = jnp.exp(lg - ceiling)
            weighted = weighted + factor * parts_ref[b, :rows, h * HD:(h + 1) * HD].astype(jnp.float32)
            total = total + factor
        out_ref[:, h * HD:(h + 1) * HD] = (weighted / total).astype(out_ref.dtype)


def combine(arrived_parts, own_out, own_log):
    return pl.pallas_call(
        combine_kernel,
        out_shape=jax.ShapeDtypeStruct(own_out.shape, jnp.bfloat16),
    )(arrived_parts, own_out, own_log)


def shards(
    fresh,
    previous,
    span_index,
    cache_counts,
    norm_gain,
    w_query,
    w_keyval,
    w_out,
    cache_keys,
    cache_values,
):
    blocks = lax.axis_size("blk")
    position = lax.axis_index("blk")
    span_rows = fresh.shape[0]
    first_span = span_index[0]
    heads_here = w_query.shape[2] // HD
    odd_member = position % 2 == 1
    live = cache_counts[0, position].reshape(1)
    arrived = passed_along(previous[0], "segment", 1)
    current = jnp.where(lax.axis_index("segment") == 0, fresh, arrived)
    widened = current.astype(jnp.float32)
    normed = (
        widened
        * lax.rsqrt(jnp.mean(widened * widened, axis=-1, keepdims=True) + EPSILON)
        * norm_gain[0]
    ).astype(jnp.bfloat16)
    queries = jnp.dot(normed, w_query[0], preferred_element_type=jnp.float32).reshape(
        span_rows, heads_here, HD
    )
    queries = rotate(queries, first_span).astype(jnp.bfloat16).reshape(span_rows, heads_here * HD)
    projected = jnp.dot(normed, w_keyval[0], preferred_element_type=jnp.float32)
    as_key = rotate(projected[:, None, :], first_span)[:, 0, :].astype(jnp.bfloat16)
    mine = jnp.where(odd_member, projected.astype(jnp.bfloat16), as_key)
    partner = swapped(mine, "blk", 0)
    own_keys = jnp.where(odd_member, partner, mine)
    own_values = jnp.where(odd_member, mine, partner)
    every_query = lax.all_to_all(
        jnp.broadcast_to(queries[None], (blocks,) + queries.shape), "blk", 0, 0, tiled=True
    )
    held = cache_attention(live, every_query, cache_keys[0], cache_values[0])
    arrived_parts = lax.all_to_all(held, "blk", split_axis=0, concat_axis=0, tiled=True)
    query_rows = queries.reshape(span_rows * heads_here, HD)
    row_tokens = jnp.arange(span_rows * heads_here, dtype=jnp.int32) // heads_here
    causal = row_tokens[:, None] >= jnp.arange(span_rows, dtype=jnp.int32)[None, :]
    own_out, own_log = attend_rows(query_rows, own_keys, own_values, causal)
    own_out = own_out.reshape(span_rows, heads_here * HD)
    own_log = own_log.reshape(span_rows, heads_here)
    attended = combine(arrived_parts, own_out, own_log)
    head_terms = jnp.dot(attended, w_out[0], preferred_element_type=jnp.float32).astype(jnp.bfloat16)
    chunk = span_rows // blocks
    gathered_terms = lax.all_to_all(
        head_terms.reshape(blocks, chunk, -1), "blk", 0, 0, tiled=True
    )
    own_rows = lax.dynamic_slice_in_dim(widened, position * chunk, chunk, 0)
    mixed_rows = (own_rows + jnp.sum(gathered_terms.astype(jnp.float32), axis=0)).astype(jnp.bfloat16)
    mixed = lax.all_to_all(
        jnp.broadcast_to(mixed_rows[None], (blocks,) + mixed_rows.shape), "blk", 0, 0, tiled=True
    ).reshape(span_rows, -1)
    return mixed[None]


def solution(mesh):
    placed = (
        P(),
        P("segment", None, None),
        P("segment"),
        P("segment", None),
        P("segment", None),
        P("segment", None, "blk"),
        P("segment", None, "blk"),
        P("segment", "blk", None),
        P("segment", "blk", None),
        P("segment", "blk", None),
    )
    return jax.shard_map(
        shards, mesh=mesh, in_specs=placed, out_specs=P("segment", None, None), check_vma=False
    )
```

```python
import jax
import jax.numpy as jnp
from jax import lax
from jax.sharding import PartitionSpec as P
from jax.experimental import pallas as pl
from jax.experimental.pallas import tpu as pltpu

KVH = 8
HD = 128


ROPE_BASE = 500000.0
EPSILON = 1e-05


def passed_along(block, axis, distance):
    devices = range(lax.axis_size(axis))
    route = [(i - distance, i) for i in devices if i - distance in devices]
    return lax.ppermute(block, axis, route)


def swapped(block, axis, distance):
    count = lax.axis_size(axis)
    route = []
    for low in range(count):
        high = low | 1 << distance
        if high != low and high < count:
            route += [(low, high), (high, low)]
    return lax.ppermute(block, axis, route)


def rotate(projected, first_span):
    length = projected.shape[0]
    half_width = projected.shape[-1] // 2
    positions = (first_span * length + jnp.arange(length, dtype=jnp.int32)).astype(jnp.float32)
    inverse = ROPE_BASE ** (
        -(jnp.arange(half_width, dtype=jnp.float32) * 2.0) / projected.shape[-1]
    )
    angles = positions[:, None] * inverse[None, :]
    cosine = jnp.cos(angles)[:, None, :]
    sine_table = jnp.sin(angles)[:, None, :]
    left_part = projected[..., :half_width]
    right_part = projected[..., half_width:]
    return jnp.concatenate(
        [
            left_part * cosine - right_part * sine_table,
            right_part * cosine + left_part * sine_table,
        ],
        axis=-1,
    )


def attend_rows(query_rows, key_rows, value_rows, allowed):
    scores = lax.dot_general(
        query_rows, key_rows, (((1,), (1,)), ((), ())), preferred_element_type=jnp.float32
    ) * query_rows.shape[-1] ** (-0.5)
    scores = jnp.where(allowed, scores, -jnp.inf)
    highest = jnp.max(scores, axis=-1, keepdims=True)
    weights = jnp.exp(scores - highest)
    totals = jnp.sum(weights, axis=-1, keepdims=True)
    partial_out = (
        jnp.dot(weights.astype(jnp.bfloat16), value_rows, preferred_element_type=jnp.float32)
        / totals
    ).astype(jnp.bfloat16)
    return (partial_out, (highest + jnp.log(totals))[:, 0])


def cache_kernel(live_ref, q_ref, k_ref, v_ref, out_ref, score_ref, high_ref, sum_ref, acc_ref):
    live = live_ref[0]
    rows = q_ref.shape[1]
    width = out_ref.shape[2]
    pieces, piece = score_ref.shape[0], score_ref.shape[2]
    for src in range(q_ref.shape[0]):
        log_rows = []
        for h in range(q_ref.shape[2] // HD):
            q = q_ref[src, :, h * HD:(h + 1) * HD]
            high_ref[...] = jnp.full(high_ref.shape, -jnp.inf, jnp.float32)
            sum_ref[...] = jnp.zeros(sum_ref.shape, jnp.float32)
            acc_ref[...] = jnp.zeros(acc_ref.shape, jnp.float32)
            for c in range(pieces):
                start = c * piece

                def scores_of():
                    return lax.dot_general(
                        q, k_ref[start:start + piece, :], (((1,), (1,)), ((), ())),
                        preferred_element_type=jnp.float32,
                    ) * HD ** (-0.5)

                def keep(scores):
                    score_ref[c] = scores
                    high_ref[...] = jnp.maximum(high_ref[...], jnp.max(scores, axis=-1, keepdims=True))

                @pl.when(start + piece <= live)
                def _():
                    keep(scores_of())

                @pl.when(jnp.logical_and(start < live, live < start + piece))
                def _():
                    visible = lax.broadcasted_iota(jnp.int32, (1, piece), 1) < live - start
                    keep(jnp.where(visible, scores_of(), -jnp.inf))

            highest = high_ref[...]
            for c in range(pieces):
                start = c * piece

                @pl.when(start < live)
                def _():
                    weights = jnp.exp(score_ref[c] - highest)
                    sum_ref[...] += jnp.sum(weights, axis=-1, keepdims=True)
                    acc_ref[...] += jnp.dot(
                        weights.astype(jnp.bfloat16), v_ref[start:start + piece, :],
                        preferred_element_type=jnp.float32,
                    )

            totals = sum_ref[...]
            out_ref[src, :rows, h * HD:(h + 1) * HD] = (acc_ref[...] / totals).astype(out_ref.dtype)
            log_col = jnp.broadcast_to(highest + jnp.log(totals), (rows, HD))
            rest = jnp.transpose(log_col)[0:1, :]
            for _ in range(3):
                part = rest.astype(jnp.bfloat16).astype(jnp.float32)
                log_rows.append(part)
                rest = rest - part
        if rows < width:
            log_rows = [jnp.concatenate([r, jnp.zeros((1, width - rows), jnp.float32)], axis=1) for r in log_rows]
        log_rows += [jnp.zeros((1, width), jnp.float32)] * (out_ref.shape[1] - rows - len(log_rows))
        out_ref[src, rows:, :] = jnp.concatenate(log_rows, axis=0).astype(out_ref.dtype)


PIECE = 512
LOG_ROWS = 8


def cache_attention(live, every_query, cached_keys, cached_values):
    sources, span_rows, width = every_query.shape
    kv_heads = cached_keys.shape[1] // HD
    per_head = sources // kv_heads
    rows = cached_keys.shape[0]
    grid_spec = pltpu.PrefetchScalarGridSpec(
        num_scalar_prefetch=1,
        grid=(kv_heads,),
        in_specs=[
            pl.BlockSpec((per_head, span_rows, width), lambda g, live: (g, 0, 0)),
            pl.BlockSpec((rows, HD), lambda g, live: (0, g)),
            pl.BlockSpec((rows, HD), lambda g, live: (0, g)),
        ],
        out_specs=pl.BlockSpec((per_head, span_rows + LOG_ROWS, width), lambda g, live: (g, 0, 0)),
        scratch_shapes=[
            pltpu.VMEM((rows // PIECE, span_rows, PIECE), jnp.float32),
            pltpu.VMEM((span_rows, 1), jnp.float32),
            pltpu.VMEM((span_rows, 1), jnp.float32),
            pltpu.VMEM((span_rows, HD), jnp.float32),
        ],
    )
    return pl.pallas_call(
        cache_kernel,
        grid_spec=grid_spec,
        out_shape=jax.ShapeDtypeStruct((sources, span_rows + LOG_ROWS, width), jnp.bfloat16),
    )(live, every_query, cached_keys, cached_values)


def combine_kernel(parts_ref, own_out_ref, own_log_ref, out_ref):
    sources = parts_ref.shape[0]
    rows = out_ref.shape[0]
    heads_here = out_ref.shape[1] // HD
    log_rows = []
    for b in range(sources):
        packed = parts_ref[b, rows:rows + LOG_ROWS, :].astype(jnp.float32)
        for h in range(heads_here):
            log_rows.append((packed[3 * h + 2:3 * h + 3] + packed[3 * h + 1:3 * h + 2]) + packed[3 * h:3 * h + 1])
    table_rows = 128 * pl.cdiv(len(log_rows), 128)
    which = lax.broadcasted_iota(jnp.int32, (table_rows, rows), 0)
    table = jnp.zeros((table_rows, rows), jnp.float32)
    for j, row in enumerate(log_rows):
        table = jnp.where(which == j, jnp.broadcast_to(row, (table_rows, rows)), table)
    columns = jnp.transpose(table)
    for h in range(heads_here):
        own_log = own_log_ref[:, h:h + 1]
        logs = [columns[:, b * heads_here + h:b * heads_here + h + 1] for b in range(sources)]
        ceiling = own_log
        for lg in logs:
            ceiling = jnp.maximum(ceiling, lg)
        own_factor = jnp.exp(own_log - ceiling)
        weighted = own_factor * own_out_ref[:, h * HD:(h + 1) * HD].astype(jnp.float32)
        total = own_factor
        for b, lg in enumerate(logs):
            factor = jnp.exp(lg - ceiling)
            weighted = weighted + factor * parts_ref[b, :rows, h * HD:(h + 1) * HD].astype(jnp.float32)
            total = total + factor
        out_ref[:, h * HD:(h + 1) * HD] = (weighted / total).astype(out_ref.dtype)


def combine(arrived_parts, own_out, own_log):
    return pl.pallas_call(
        combine_kernel,
        out_shape=jax.ShapeDtypeStruct(own_out.shape, jnp.bfloat16),
    )(arrived_parts, own_out, own_log)


def shards(
    fresh,
    previous,
    span_index,
    cache_counts,
    norm_gain,
    w_query,
    w_keyval,
    w_out,
    cache_keys,
    cache_values,
):
    blocks = lax.axis_size("blk")
    position = lax.axis_index("blk")
    span_rows = fresh.shape[0]
    first_span = span_index[0]
    heads_here = w_query.shape[2] // HD
    odd_member = position % 2 == 1
    live = cache_counts[0, position].reshape(1)
    arrived = passed_along(previous[0], "segment", 1)
    current = jnp.where(lax.axis_index("segment") == 0, fresh, arrived)
    widened = current.astype(jnp.float32)
    normed = (
        widened
        * lax.rsqrt(jnp.mean(widened * widened, axis=-1, keepdims=True) + EPSILON)
        * norm_gain[0]
    ).astype(jnp.bfloat16)
    queries = jnp.dot(normed, w_query[0], preferred_element_type=jnp.float32).reshape(
        span_rows, heads_here, HD
    )
    queries = rotate(queries, first_span).astype(jnp.bfloat16).reshape(span_rows, heads_here * HD)
    projected = jnp.dot(normed, w_keyval[0], preferred_element_type=jnp.float32)
    as_key = rotate(projected[:, None, :], first_span)[:, 0, :].astype(jnp.bfloat16)
    mine = jnp.where(odd_member, projected.astype(jnp.bfloat16), as_key)
    partner = swapped(mine, "blk", 0)
    own_keys = jnp.where(odd_member, partner, mine)
    own_values = jnp.where(odd_member, mine, partner)
    every_query = lax.all_to_all(
        jnp.broadcast_to(queries[None], (blocks,) + queries.shape), "blk", 0, 0, tiled=True
    )
    held = cache_attention(live, every_query, cache_keys[0], cache_values[0])
    arrived_parts = lax.all_to_all(held, "blk", split_axis=0, concat_axis=0, tiled=True)
    query_rows = queries.reshape(span_rows * heads_here, HD)
    row_tokens = jnp.arange(span_rows * heads_here, dtype=jnp.int32) // heads_here
    causal = row_tokens[:, None] >= jnp.arange(span_rows, dtype=jnp.int32)[None, :]
    own_out, own_log = attend_rows(query_rows, own_keys, own_values, causal)
    own_out = own_out.reshape(span_rows, heads_here * HD)
    own_log = own_log.reshape(span_rows, heads_here)
    attended = combine(arrived_parts, own_out, own_log)
    head_terms = jnp.dot(attended, w_out[0], preferred_element_type=jnp.float32).astype(jnp.bfloat16)
    chunk = span_rows // blocks
    gathered_terms = lax.all_to_all(
        head_terms.reshape(blocks, chunk, -1), "blk", 0, 0, tiled=True
    )
    own_rows = lax.dynamic_slice_in_dim(widened, position * chunk, chunk, 0)
    mixed_rows = (own_rows + jnp.sum(gathered_terms.astype(jnp.float32), axis=0)).astype(jnp.bfloat16)
    mixed = lax.all_to_all(
        jnp.broadcast_to(mixed_rows[None], (blocks,) + mixed_rows.shape), "blk", 0, 0, tiled=True
    ).reshape(span_rows, -1)
    return mixed[None]


def solution(mesh):
    placed = (
        P(),
        P("segment", None, None),
        P("segment"),
        P("segment", None),
        P("segment", None),
        P("segment", None, "blk"),
        P("segment", None, "blk"),
        P("segment", "blk", None),
        P("segment", "blk", None),
        P("segment", "blk", None),
    )
    return jax.shard_map(
        shards, mesh=mesh, in_specs=placed, out_specs=P("segment", None, None), check_vma=False
    )
```

```python
import jax
import jax.numpy as jnp
from jax import lax
from jax.sharding import PartitionSpec as P
from jax.experimental import pallas as pl
from jax.experimental.pallas import tpu as pltpu

KVH = 8
HD = 128


ROPE_BASE = 500000.0
EPSILON = 1e-05


def passed_along(block, axis, distance):
    devices = range(lax.axis_size(axis))
    route = [(i - distance, i) for i in devices if i - distance in devices]
    return lax.ppermute(block, axis, route)


def swapped(block, axis, distance):
    count = lax.axis_size(axis)
    route = []
    for low in range(count):
        high = low | 1 << distance
        if high != low and high < count:
            route += [(low, high), (high, low)]
    return lax.ppermute(block, axis, route)


def rotate(projected, first_span):
    length = projected.shape[0]
    half_width = projected.shape[-1] // 2
    positions = (first_span * length + jnp.arange(length, dtype=jnp.int32)).astype(jnp.float32)
    inverse = ROPE_BASE ** (
        -(jnp.arange(half_width, dtype=jnp.float32) * 2.0) / projected.shape[-1]
    )
    angles = positions[:, None] * inverse[None, :]
    cosine = jnp.cos(angles)[:, None, :]
    sine_table = jnp.sin(angles)[:, None, :]
    left_part = projected[..., :half_width]
    right_part = projected[..., half_width:]
    return jnp.concatenate(
        [
            left_part * cosine - right_part * sine_table,
            right_part * cosine + left_part * sine_table,
        ],
        axis=-1,
    )


def attend_rows(query_rows, key_rows, value_rows, allowed):
    scores = lax.dot_general(
        query_rows, key_rows, (((1,), (1,)), ((), ())), preferred_element_type=jnp.float32
    ) * query_rows.shape[-1] ** (-0.5)
    scores = jnp.where(allowed, scores, -jnp.inf)
    highest = jnp.max(scores, axis=-1, keepdims=True)
    weights = jnp.exp(scores - highest)
    totals = jnp.sum(weights, axis=-1, keepdims=True)
    partial_out = (
        jnp.dot(weights.astype(jnp.bfloat16), value_rows, preferred_element_type=jnp.float32)
        / totals
    ).astype(jnp.bfloat16)
    return (partial_out, (highest + jnp.log(totals))[:, 0])


def cache_kernel(live_ref, q_ref, k_ref, v_ref, out_ref):
    live = live_ref[0]
    keys = k_ref[...]
    values = v_ref[...]
    rows = q_ref.shape[1]
    width = out_ref.shape[2]
    visible = lax.broadcasted_iota(jnp.int32, (1, keys.shape[0]), 1) < live
    ones = jnp.ones((keys.shape[0], HD), jnp.bfloat16)
    for src in range(q_ref.shape[0]):
        log_rows = []
        for h in range(q_ref.shape[2] // HD):
            q = q_ref[src, :, h * HD:(h + 1) * HD]
            scores = lax.dot_general(
                q, keys, (((1,), (1,)), ((), ())), preferred_element_type=jnp.float32
            ) * HD ** (-0.5)
            scores = jnp.where(visible, scores, -jnp.inf)
            highest = jnp.max(scores, axis=-1, keepdims=True)
            weights = jnp.exp(scores - highest).astype(jnp.bfloat16)
            totals = jnp.dot(weights, ones, preferred_element_type=jnp.float32)[:, 0:1]
            part = jnp.dot(weights, values, preferred_element_type=jnp.float32)
            out_ref[src, :rows, h * HD:(h + 1) * HD] = (part / totals).astype(out_ref.dtype)
            log_col = jnp.broadcast_to(highest + jnp.log(totals), (rows, HD))
            rest = jnp.transpose(log_col)[0:1, :]
            for _ in range(3):
                piece = rest.astype(jnp.bfloat16).astype(jnp.float32)
                log_rows.append(piece)
                rest = rest - piece
        if rows < width:
            log_rows = [jnp.concatenate([r, jnp.zeros((1, width - rows), jnp.float32)], axis=1) for r in log_rows]
        log_rows += [jnp.zeros((1, width), jnp.float32)] * (out_ref.shape[1] - rows - len(log_rows))
        out_ref[src, rows:, :] = jnp.concatenate(log_rows, axis=0).astype(out_ref.dtype)


LOG_ROWS = 8


def cache_attention(live, every_query, cached_keys, cached_values):
    sources, span_rows, width = every_query.shape
    kv_heads = cached_keys.shape[1] // HD
    per_head = sources // kv_heads
    rows = cached_keys.shape[0]
    grid_spec = pltpu.PrefetchScalarGridSpec(
        num_scalar_prefetch=1,
        grid=(kv_heads,),
        in_specs=[
            pl.BlockSpec((per_head, span_rows, width), lambda g, live: (g, 0, 0)),
            pl.BlockSpec((rows, HD), lambda g, live: (0, g)),
            pl.BlockSpec((rows, HD), lambda g, live: (0, g)),
        ],
        out_specs=pl.BlockSpec((per_head, span_rows + LOG_ROWS, width), lambda g, live: (g, 0, 0)),
    )
    return pl.pallas_call(
        cache_kernel,
        grid_spec=grid_spec,
        out_shape=jax.ShapeDtypeStruct((sources, span_rows + LOG_ROWS, width), jnp.bfloat16),
    )(live, every_query, cached_keys, cached_values)


def combine_kernel(parts_ref, own_out_ref, own_log_ref, out_ref):
    sources = parts_ref.shape[0]
    rows = out_ref.shape[0]
    heads_here = out_ref.shape[1] // HD
    logs = [[] for _ in range(heads_here)]
    for b in range(sources):
        packed = parts_ref[b, rows:rows + LOG_ROWS, :].astype(jnp.float32)
        for h in range(heads_here):
            logs[h].append((packed[3 * h + 2:3 * h + 3] + packed[3 * h + 1:3 * h + 2]) + packed[3 * h:3 * h + 1])
    own_logs = own_log_ref[...]
    table_rows = []
    for h in range(heads_here):
        own_log = own_logs[h:h + 1]
        ceiling = own_log
        for lg in logs[h]:
            ceiling = jnp.maximum(ceiling, lg)
        own_factor = jnp.exp(own_log - ceiling)
        factors = [jnp.exp(lg - ceiling) for lg in logs[h]]
        total = own_factor
        for factor in factors:
            total = total + factor
        table_rows += [own_factor] + factors + [total]
    size = 128 * pl.cdiv(len(table_rows), 128)
    which = lax.broadcasted_iota(jnp.int32, (size, rows), 0)
    table = jnp.zeros((size, rows), jnp.float32)
    for j, row in enumerate(table_rows):
        table = jnp.where(which == j, jnp.broadcast_to(row, (size, rows)), table)
    columns = jnp.transpose(table)
    for h in range(heads_here):
        base = h * (sources + 2)
        weighted = columns[:, base:base + 1] * own_out_ref[:, h * HD:(h + 1) * HD].astype(jnp.float32)
        for b in range(sources):
            weighted = weighted + columns[:, base + 1 + b:base + 2 + b] * parts_ref[
                b, :rows, h * HD:(h + 1) * HD
            ].astype(jnp.float32)
        total = columns[:, base + sources + 1:base + sources + 2]
        out_ref[:, h * HD:(h + 1) * HD] = (weighted / total).astype(out_ref.dtype)


def combine(arrived_parts, own_out, own_log):
    return pl.pallas_call(
        combine_kernel,
        out_shape=jax.ShapeDtypeStruct(own_out.shape, jnp.bfloat16),
    )(arrived_parts, own_out, own_log)


def shards(
    fresh,
    previous,
    span_index,
    cache_counts,
    norm_gain,
    w_query,
    w_keyval,
    w_out,
    cache_keys,
    cache_values,
):
    blocks = lax.axis_size("blk")
    position = lax.axis_index("blk")
    span_rows = fresh.shape[0]
    first_span = span_index[0]
    heads_here = w_query.shape[2] // HD
    odd_member = position % 2 == 1
    live = cache_counts[0, position].reshape(1)
    arrived = passed_along(previous[0], "segment", 1)
    current = jnp.where(lax.axis_index("segment") == 0, fresh, arrived)
    widened = current.astype(jnp.float32)
    normed = (
        widened
        * lax.rsqrt(jnp.mean(widened * widened, axis=-1, keepdims=True) + EPSILON)
        * norm_gain[0]
    ).astype(jnp.bfloat16)
    queries = jnp.dot(normed, w_query[0], preferred_element_type=jnp.float32).reshape(
        span_rows, heads_here, HD
    )
    queries = rotate(queries, first_span).astype(jnp.bfloat16).reshape(span_rows, heads_here * HD)
    projected = jnp.dot(normed, w_keyval[0], preferred_element_type=jnp.float32)
    as_key = rotate(projected[:, None, :], first_span)[:, 0, :].astype(jnp.bfloat16)
    mine = jnp.where(odd_member, projected.astype(jnp.bfloat16), as_key)
    partner = swapped(mine, "blk", 0)
    own_keys = jnp.where(odd_member, partner, mine)
    own_values = jnp.where(odd_member, mine, partner)
    every_query = lax.all_to_all(
        jnp.broadcast_to(queries[None], (blocks,) + queries.shape), "blk", 0, 0, tiled=True
    )
    held = cache_attention(live, every_query, cache_keys[0], cache_values[0])
    arrived_parts = lax.all_to_all(held, "blk", split_axis=0, concat_axis=0, tiled=True)
    query_rows = queries.reshape(span_rows * heads_here, HD)
    row_tokens = jnp.arange(span_rows * heads_here, dtype=jnp.int32) // heads_here
    causal = row_tokens[:, None] >= jnp.arange(span_rows, dtype=jnp.int32)[None, :]
    own_out, own_log = attend_rows(query_rows, own_keys, own_values, causal)
    own_out = own_out.reshape(span_rows, heads_here * HD)
    own_log = own_log.reshape(span_rows, heads_here).T
    attended = combine(arrived_parts, own_out, own_log)
    head_terms = jnp.dot(attended, w_out[0], preferred_element_type=jnp.float32).astype(jnp.bfloat16)
    chunk = span_rows // blocks
    gathered_terms = lax.all_to_all(
        head_terms.reshape(blocks, chunk, -1), "blk", 0, 0, tiled=True
    )
    own_rows = lax.dynamic_slice_in_dim(widened, position * chunk, chunk, 0)
    mixed_rows = (own_rows + jnp.sum(gathered_terms.astype(jnp.float32), axis=0)).astype(jnp.bfloat16)
    mixed = lax.all_to_all(
        jnp.broadcast_to(mixed_rows[None], (blocks,) + mixed_rows.shape), "blk", 0, 0, tiled=True
    ).reshape(span_rows, -1)
    return mixed[None]


def solution(mesh):
    placed = (
        P(),
        P("segment", None, None),
        P("segment"),
        P("segment", None),
        P("segment", None),
        P("segment", None, "blk"),
        P("segment", None, "blk"),
        P("segment", "blk", None),
        P("segment", "blk", None),
        P("segment", "blk", None),
    )
    return jax.shard_map(
        shards, mesh=mesh, in_specs=placed, out_specs=P("segment", None, None), check_vma=False
    )
```

```python
import jax
import jax.numpy as jnp
from jax import lax
from jax.sharding import PartitionSpec as P
from jax.experimental import pallas as pl
from jax.experimental.pallas import tpu as pltpu

KVH = 8
HD = 128


ROPE_BASE = 500000.0
EPSILON = 1e-05


def passed_along(block, axis, distance):
    devices = range(lax.axis_size(axis))
    route = [(i - distance, i) for i in devices if i - distance in devices]
    return lax.ppermute(block, axis, route)


def swapped(block, axis, distance):
    count = lax.axis_size(axis)
    route = []
    for low in range(count):
        high = low | 1 << distance
        if high != low and high < count:
            route += [(low, high), (high, low)]
    return lax.ppermute(block, axis, route)


def rotate(projected, first_span):
    length = projected.shape[0]
    half_width = projected.shape[-1] // 2
    positions = (first_span * length + jnp.arange(length, dtype=jnp.int32)).astype(jnp.float32)
    inverse = ROPE_BASE ** (
        -(jnp.arange(half_width, dtype=jnp.float32) * 2.0) / projected.shape[-1]
    )
    angles = positions[:, None] * inverse[None, :]
    cosine = jnp.cos(angles)[:, None, :]
    sine_table = jnp.sin(angles)[:, None, :]
    left_part = projected[..., :half_width]
    right_part = projected[..., half_width:]
    return jnp.concatenate(
        [
            left_part * cosine - right_part * sine_table,
            right_part * cosine + left_part * sine_table,
        ],
        axis=-1,
    )


def attend_rows(query_rows, key_rows, value_rows, allowed):
    scores = lax.dot_general(
        query_rows, key_rows, (((1,), (1,)), ((), ())), preferred_element_type=jnp.float32
    ) * query_rows.shape[-1] ** (-0.5)
    scores = jnp.where(allowed, scores, -jnp.inf)
    highest = jnp.max(scores, axis=-1, keepdims=True)
    weights = jnp.exp(scores - highest)
    totals = jnp.sum(weights, axis=-1, keepdims=True)
    partial_out = (
        jnp.dot(weights.astype(jnp.bfloat16), value_rows, preferred_element_type=jnp.float32)
        / totals
    ).astype(jnp.bfloat16)
    return (partial_out, (highest + jnp.log(totals))[:, 0])


def cache_kernel(live_ref, q_ref, k_ref, v_ref, out_ref):
    live = live_ref[0]
    keys = k_ref[...]
    values = v_ref[...]
    rows = q_ref.shape[1]
    width = out_ref.shape[2]
    visible = lax.broadcasted_iota(jnp.int32, (1, keys.shape[0]), 1) < live
    for src in range(q_ref.shape[0]):
        log_rows = []
        for h in range(q_ref.shape[2] // HD):
            q = q_ref[src, :, h * HD:(h + 1) * HD]
            scores = lax.dot_general(
                q, keys, (((1,), (1,)), ((), ())), preferred_element_type=jnp.float32
            ) * HD ** (-0.5)
            scores = jnp.where(visible, scores, -jnp.inf)
            highest = jnp.max(scores, axis=-1, keepdims=True)
            weights = jnp.exp(scores - highest)
            totals = jnp.sum(weights, axis=-1, keepdims=True)
            part = jnp.dot(weights.astype(jnp.bfloat16), values, preferred_element_type=jnp.float32)
            out_ref[src, :rows, h * HD:(h + 1) * HD] = (part / totals).astype(out_ref.dtype)
            log_col = jnp.broadcast_to(highest + jnp.log(totals), (rows, HD))
            rest = jnp.transpose(log_col)[0:1, :]
            for _ in range(3):
                piece = rest.astype(jnp.bfloat16).astype(jnp.float32)
                log_rows.append(piece)
                rest = rest - piece
        if rows < width:
            log_rows = [jnp.concatenate([r, jnp.zeros((1, width - rows), jnp.float32)], axis=1) for r in log_rows]
        log_rows += [jnp.zeros((1, width), jnp.float32)] * (out_ref.shape[1] - rows - len(log_rows))
        out_ref[src, rows:, :] = jnp.concatenate(log_rows, axis=0).astype(out_ref.dtype)


LOG_ROWS = 8


def cache_attention(live, every_query, cached_keys, cached_values):
    sources, span_rows, width = every_query.shape
    kv_heads = cached_keys.shape[1] // HD
    per_head = sources // kv_heads
    rows = cached_keys.shape[0]
    grid_spec = pltpu.PrefetchScalarGridSpec(
        num_scalar_prefetch=1,
        grid=(kv_heads,),
        in_specs=[
            pl.BlockSpec((per_head, span_rows, width), lambda g, live: (g, 0, 0)),
            pl.BlockSpec((rows, HD), lambda g, live: (0, g)),
            pl.BlockSpec((rows, HD), lambda g, live: (0, g)),
        ],
        out_specs=pl.BlockSpec((per_head, span_rows + LOG_ROWS, width), lambda g, live: (g, 0, 0)),
    )
    return pl.pallas_call(
        cache_kernel,
        grid_spec=grid_spec,
        out_shape=jax.ShapeDtypeStruct((sources, span_rows + LOG_ROWS, width), jnp.bfloat16),
    )(live, every_query, cached_keys, cached_values)


def combine_kernel(parts_ref, own_out_ref, own_log_ref, out_ref):
    sources = parts_ref.shape[0]
    rows = out_ref.shape[0]
    heads_here = out_ref.shape[1] // HD
    logs = [[] for _ in range(heads_here)]
    for b in range(sources):
        packed = parts_ref[b, rows:rows + LOG_ROWS, :].astype(jnp.float32)
        for h in range(heads_here):
            logs[h].append((packed[3 * h + 2:3 * h + 3] + packed[3 * h + 1:3 * h + 2]) + packed[3 * h:3 * h + 1])
    own_logs = own_log_ref[...]
    table_rows = []
    for h in range(heads_here):
        own_log = own_logs[h:h + 1]
        ceiling = own_log
        for lg in logs[h]:
            ceiling = jnp.maximum(ceiling, lg)
        own_factor = jnp.exp(own_log - ceiling)
        factors = [jnp.exp(lg - ceiling) for lg in logs[h]]
        total = own_factor
        for factor in factors:
            total = total + factor
        table_rows += [own_factor] + factors + [total]
    size = 128 * pl.cdiv(len(table_rows), 128)
    which = lax.broadcasted_iota(jnp.int32, (size, rows), 0)
    table = jnp.zeros((size, rows), jnp.float32)
    for j, row in enumerate(table_rows):
        table = jnp.where(which == j, jnp.broadcast_to(row, (size, rows)), table)
    columns = jnp.transpose(table)
    for h in range(heads_here):
        base = h * (sources + 2)
        weighted = columns[:, base:base + 1] * own_out_ref[:, h * HD:(h + 1) * HD].astype(jnp.float32)
        for b in range(sources):
            weighted = weighted + columns[:, base + 1 + b:base + 2 + b] * parts_ref[
                b, :rows, h * HD:(h + 1) * HD
            ].astype(jnp.float32)
        total = columns[:, base + sources + 1:base + sources + 2]
        out_ref[:, h * HD:(h + 1) * HD] = (weighted / total).astype(out_ref.dtype)


def combine(arrived_parts, own_out, own_log):
    return pl.pallas_call(
        combine_kernel,
        out_shape=jax.ShapeDtypeStruct(own_out.shape, jnp.bfloat16),
    )(arrived_parts, own_out, own_log)


def shards(
    fresh,
    previous,
    span_index,
    cache_counts,
    norm_gain,
    w_query,
    w_keyval,
    w_out,
    cache_keys,
    cache_values,
):
    blocks = lax.axis_size("blk")
    position = lax.axis_index("blk")
    span_rows = fresh.shape[0]
    first_span = span_index[0]
    heads_here = w_query.shape[2] // HD
    odd_member = position % 2 == 1
    live = cache_counts[0, position].reshape(1)
    arrived = passed_along(previous[0], "segment", 1)
    current = jnp.where(lax.axis_index("segment") == 0, fresh, arrived)
    widened = current.astype(jnp.float32)
    normed = (
        widened
        * lax.rsqrt(jnp.mean(widened * widened, axis=-1, keepdims=True) + EPSILON)
        * norm_gain[0]
    ).astype(jnp.bfloat16)
    queries = jnp.dot(normed, w_query[0], preferred_element_type=jnp.float32).reshape(
        span_rows, heads_here, HD
    )
    queries = rotate(queries, first_span).astype(jnp.bfloat16).reshape(span_rows, heads_here * HD)
    projected = jnp.dot(normed, w_keyval[0], preferred_element_type=jnp.float32)
    as_key = rotate(projected[:, None, :], first_span)[:, 0, :].astype(jnp.bfloat16)
    mine = jnp.where(odd_member, projected.astype(jnp.bfloat16), as_key)
    partner = swapped(mine, "blk", 0)
    own_keys = jnp.where(odd_member, partner, mine)
    own_values = jnp.where(odd_member, mine, partner)
    every_query = lax.all_to_all(
        jnp.broadcast_to(queries[None], (blocks,) + queries.shape), "blk", 0, 0, tiled=True
    )
    held = cache_attention(live, every_query, cache_keys[0], cache_values[0])
    arrived_parts = lax.all_to_all(held, "blk", split_axis=0, concat_axis=0, tiled=True)
    query_rows = queries.reshape(span_rows * heads_here, HD)
    row_tokens = jnp.arange(span_rows * heads_here, dtype=jnp.int32) // heads_here
    causal = row_tokens[:, None] >= jnp.arange(span_rows, dtype=jnp.int32)[None, :]
    own_out, own_log = attend_rows(query_rows, own_keys, own_values, causal)
    own_out = own_out.reshape(span_rows, heads_here * HD)
    own_log = own_log.reshape(span_rows, heads_here).T
    attended = combine(arrived_parts, own_out, own_log)
    head_terms = jnp.dot(attended, w_out[0], preferred_element_type=jnp.float32).astype(jnp.bfloat16)
    chunk = span_rows // blocks
    gathered_terms = lax.all_to_all(
        head_terms.reshape(blocks, chunk, -1), "blk", 0, 0, tiled=True
    )
    own_rows = lax.dynamic_slice_in_dim(current, position * chunk, chunk, 0).astype(jnp.float32)
    mixed_rows = (own_rows + jnp.sum(gathered_terms.astype(jnp.float32), axis=0)).astype(jnp.bfloat16)
    mixed = lax.all_to_all(
        jnp.broadcast_to(mixed_rows[None], (blocks,) + mixed_rows.shape), "blk", 0, 0, tiled=True
    ).reshape(span_rows, -1)
    return mixed[None]


def solution(mesh):
    placed = (
        P(),
        P("segment", None, None),
        P("segment"),
        P("segment", None),
        P("segment", None),
        P("segment", None, "blk"),
        P("segment", None, "blk"),
        P("segment", "blk", None),
        P("segment", "blk", None),
        P("segment", "blk", None),
    )
    return jax.shard_map(
        shards, mesh=mesh, in_specs=placed, out_specs=P("segment", None, None), check_vma=False
    )
```

```python
import jax
import jax.numpy as jnp
from jax import lax
from jax.sharding import PartitionSpec as P
from jax.experimental import pallas as pl
from jax.experimental.pallas import tpu as pltpu

KVH = 8
HD = 128


ROPE_BASE = 500000.0
EPSILON = 1e-05


def passed_along(block, axis, distance):
    devices = range(lax.axis_size(axis))
    route = [(i - distance, i) for i in devices if i - distance in devices]
    return lax.ppermute(block, axis, route)


def swapped(block, axis, distance):
    count = lax.axis_size(axis)
    route = []
    for low in range(count):
        high = low | 1 << distance
        if high != low and high < count:
            route += [(low, high), (high, low)]
    return lax.ppermute(block, axis, route)


def rotate(projected, first_span):
    length = projected.shape[0]
    half_width = projected.shape[-1] // 2
    positions = (first_span * length + jnp.arange(length, dtype=jnp.int32)).astype(jnp.float32)
    inverse = ROPE_BASE ** (
        -(jnp.arange(half_width, dtype=jnp.float32) * 2.0) / projected.shape[-1]
    )
    angles = positions[:, None] * inverse[None, :]
    cosine = jnp.cos(angles)[:, None, :]
    sine_table = jnp.sin(angles)[:, None, :]
    left_part = projected[..., :half_width]
    right_part = projected[..., half_width:]
    return jnp.concatenate(
        [
            left_part * cosine - right_part * sine_table,
            right_part * cosine + left_part * sine_table,
        ],
        axis=-1,
    )


def attend_rows(query_rows, key_rows, value_rows, allowed):
    scores = lax.dot_general(
        query_rows, key_rows, (((1,), (1,)), ((), ())), preferred_element_type=jnp.float32
    ) * query_rows.shape[-1] ** (-0.5)
    scores = jnp.where(allowed, scores, -jnp.inf)
    highest = jnp.max(scores, axis=-1, keepdims=True)
    weights = jnp.exp(scores - highest)
    totals = jnp.sum(weights, axis=-1, keepdims=True)
    partial_out = (
        jnp.dot(weights.astype(jnp.bfloat16), value_rows, preferred_element_type=jnp.float32)
        / totals
    ).astype(jnp.bfloat16)
    return (partial_out, (highest + jnp.log(totals))[:, 0])


def cache_kernel(live_ref, q_ref, k_ref, v_ref, out_ref):
    live = live_ref[0]
    keys = k_ref[...]
    values = v_ref[...]
    rows = q_ref.shape[1]
    width = out_ref.shape[2]
    heads_here = q_ref.shape[2] // HD
    sets = [(src, h) for src in range(q_ref.shape[0]) for h in range(heads_here)]
    stacked = jnp.concatenate([q_ref[src, :, h * HD:(h + 1) * HD] for src, h in sets], axis=0)
    visible = lax.broadcasted_iota(jnp.int32, (1, keys.shape[0]), 1) < live
    scores = lax.dot_general(
        stacked, keys, (((1,), (1,)), ((), ())), preferred_element_type=jnp.float32
    ) * HD ** (-0.5)
    scores = jnp.where(visible, scores, -jnp.inf)
    highest = jnp.max(scores, axis=-1, keepdims=True)
    weights = jnp.exp(scores - highest)
    totals = jnp.sum(weights, axis=-1, keepdims=True)
    part = jnp.dot(weights.astype(jnp.bfloat16), values, preferred_element_type=jnp.float32)
    normalized = (part / totals).astype(out_ref.dtype)
    log_totals = highest + jnp.log(totals)
    log_rows = {}
    for i, (src, h) in enumerate(sets):
        out_ref[src, :rows, h * HD:(h + 1) * HD] = normalized[i * rows:(i + 1) * rows]
        log_col = jnp.broadcast_to(log_totals[i * rows:(i + 1) * rows], (rows, HD))
        rest = jnp.transpose(log_col)[0:1, :]
        pieces = []
        for _ in range(3):
            piece = rest.astype(jnp.bfloat16).astype(jnp.float32)
            pieces.append(piece)
            rest = rest - piece
        log_rows.setdefault(src, []).extend(pieces)
    for src, rows_here in log_rows.items():
        if rows < width:
            rows_here = [jnp.concatenate([r, jnp.zeros((1, width - rows), jnp.float32)], axis=1) for r in rows_here]
        rows_here = rows_here + [jnp.zeros((1, width), jnp.float32)] * (out_ref.shape[1] - rows - len(rows_here))
        out_ref[src, rows:, :] = jnp.concatenate(rows_here, axis=0).astype(out_ref.dtype)


LOG_ROWS = 8


def cache_attention(live, every_query, cached_keys, cached_values):
    sources, span_rows, width = every_query.shape
    kv_heads = cached_keys.shape[1] // HD
    per_head = sources // kv_heads
    rows = cached_keys.shape[0]
    grid_spec = pltpu.PrefetchScalarGridSpec(
        num_scalar_prefetch=1,
        grid=(kv_heads,),
        in_specs=[
            pl.BlockSpec((per_head, span_rows, width), lambda g, live: (g, 0, 0)),
            pl.BlockSpec((rows, HD), lambda g, live: (0, g)),
            pl.BlockSpec((rows, HD), lambda g, live: (0, g)),
        ],
        out_specs=pl.BlockSpec((per_head, span_rows + LOG_ROWS, width), lambda g, live: (g, 0, 0)),
    )
    return pl.pallas_call(
        cache_kernel,
        grid_spec=grid_spec,
        out_shape=jax.ShapeDtypeStruct((sources, span_rows + LOG_ROWS, width), jnp.bfloat16),
    )(live, every_query, cached_keys, cached_values)


def combine_kernel(parts_ref, own_out_ref, own_log_ref, out_ref):
    sources = parts_ref.shape[0]
    rows = out_ref.shape[0]
    heads_here = out_ref.shape[1] // HD
    logs = [[] for _ in range(heads_here)]
    for b in range(sources):
        packed = parts_ref[b, rows:rows + LOG_ROWS, :].astype(jnp.float32)
        for h in range(heads_here):
            logs[h].append((packed[3 * h + 2:3 * h + 3] + packed[3 * h + 1:3 * h + 2]) + packed[3 * h:3 * h + 1])
    own_logs = own_log_ref[...]
    table_rows = []
    for h in range(heads_here):
        own_log = own_logs[h:h + 1]
        ceiling = own_log
        for lg in logs[h]:
            ceiling = jnp.maximum(ceiling, lg)
        own_factor = jnp.exp(own_log - ceiling)
        factors = [jnp.exp(lg - ceiling) for lg in logs[h]]
        total = own_factor
        for factor in factors:
            total = total + factor
        table_rows += [own_factor] + factors + [total]
    size = 128 * pl.cdiv(len(table_rows), 128)
    which = lax.broadcasted_iota(jnp.int32, (size, rows), 0)
    table = jnp.zeros((size, rows), jnp.float32)
    for j, row in enumerate(table_rows):
        table = jnp.where(which == j, jnp.broadcast_to(row, (size, rows)), table)
    columns = jnp.transpose(table)
    for h in range(heads_here):
        base = h * (sources + 2)
        weighted = columns[:, base:base + 1] * own_out_ref[:, h * HD:(h + 1) * HD].astype(jnp.float32)
        for b in range(sources):
            weighted = weighted + columns[:, base + 1 + b:base + 2 + b] * parts_ref[
                b, :rows, h * HD:(h + 1) * HD
            ].astype(jnp.float32)
        total = columns[:, base + sources + 1:base + sources + 2]
        out_ref[:, h * HD:(h + 1) * HD] = (weighted / total).astype(out_ref.dtype)


def combine(arrived_parts, own_out, own_log):
    return pl.pallas_call(
        combine_kernel,
        out_shape=jax.ShapeDtypeStruct(own_out.shape, jnp.bfloat16),
    )(arrived_parts, own_out, own_log)


def shards(
    fresh,
    previous,
    span_index,
    cache_counts,
    norm_gain,
    w_query,
    w_keyval,
    w_out,
    cache_keys,
    cache_values,
):
    blocks = lax.axis_size("blk")
    position = lax.axis_index("blk")
    span_rows = fresh.shape[0]
    first_span = span_index[0]
    heads_here = w_query.shape[2] // HD
    odd_member = position % 2 == 1
    live = cache_counts[0, position].reshape(1)
    arrived = passed_along(previous[0], "segment", 1)
    current = jnp.where(lax.axis_index("segment") == 0, fresh, arrived)
    widened = current.astype(jnp.float32)
    normed = (
        widened
        * lax.rsqrt(jnp.mean(widened * widened, axis=-1, keepdims=True) + EPSILON)
        * norm_gain[0]
    ).astype(jnp.bfloat16)
    queries = jnp.dot(normed, w_query[0], preferred_element_type=jnp.float32).reshape(
        span_rows, heads_here, HD
    )
    queries = rotate(queries, first_span).astype(jnp.bfloat16).reshape(span_rows, heads_here * HD)
    projected = jnp.dot(normed, w_keyval[0], preferred_element_type=jnp.float32)
    as_key = rotate(projected[:, None, :], first_span)[:, 0, :].astype(jnp.bfloat16)
    mine = jnp.where(odd_member, projected.astype(jnp.bfloat16), as_key)
    partner = swapped(mine, "blk", 0)
    own_keys = jnp.where(odd_member, partner, mine)
    own_values = jnp.where(odd_member, mine, partner)
    every_query = lax.all_to_all(
        jnp.broadcast_to(queries[None], (blocks,) + queries.shape), "blk", 0, 0, tiled=True
    )
    held = cache_attention(live, every_query, cache_keys[0], cache_values[0])
    arrived_parts = lax.all_to_all(held, "blk", split_axis=0, concat_axis=0, tiled=True)
    query_rows = queries.reshape(span_rows * heads_here, HD)
    row_tokens = jnp.arange(span_rows * heads_here, dtype=jnp.int32) // heads_here
    causal = row_tokens[:, None] >= jnp.arange(span_rows, dtype=jnp.int32)[None, :]
    own_out, own_log = attend_rows(query_rows, own_keys, own_values, causal)
    own_out = own_out.reshape(span_rows, heads_here * HD)
    own_log = own_log.reshape(span_rows, heads_here).T
    attended = combine(arrived_parts, own_out, own_log)
    head_terms = jnp.dot(attended, w_out[0], preferred_element_type=jnp.float32).astype(jnp.bfloat16)
    chunk = span_rows // blocks
    gathered_terms = lax.all_to_all(
        head_terms.reshape(blocks, chunk, -1), "blk", 0, 0, tiled=True
    )
    own_rows = lax.dynamic_slice_in_dim(current, position * chunk, chunk, 0).astype(jnp.float32)
    mixed_rows = (own_rows + jnp.sum(gathered_terms.astype(jnp.float32), axis=0)).astype(jnp.bfloat16)
    mixed = lax.all_to_all(
        jnp.broadcast_to(mixed_rows[None], (blocks,) + mixed_rows.shape), "blk", 0, 0, tiled=True
    ).reshape(span_rows, -1)
    return mixed[None]


def solution(mesh):
    placed = (
        P(),
        P("segment", None, None),
        P("segment"),
        P("segment", None),
        P("segment", None),
        P("segment", None, "blk"),
        P("segment", None, "blk"),
        P("segment", "blk", None),
        P("segment", "blk", None),
        P("segment", "blk", None),
    )
    return jax.shard_map(
        shards, mesh=mesh, in_specs=placed, out_specs=P("segment", None, None), check_vma=False
    )
```

```python
import jax
import jax.numpy as jnp
from jax import lax
from jax.sharding import PartitionSpec as P
from jax.experimental import pallas as pl
from jax.experimental.pallas import tpu as pltpu

KVH = 8
HD = 128


ROPE_BASE = 500000.0
EPSILON = 1e-05


def passed_along(block, axis, distance):
    devices = range(lax.axis_size(axis))
    route = [(i - distance, i) for i in devices if i - distance in devices]
    return lax.ppermute(block, axis, route)


def swapped(block, axis, distance):
    count = lax.axis_size(axis)
    route = []
    for low in range(count):
        high = low | 1 << distance
        if high != low and high < count:
            route += [(low, high), (high, low)]
    return lax.ppermute(block, axis, route)


def rotate(projected, first_span):
    length = projected.shape[0]
    half_width = projected.shape[-1] // 2
    positions = (first_span * length + jnp.arange(length, dtype=jnp.int32)).astype(jnp.float32)
    inverse = ROPE_BASE ** (
        -(jnp.arange(half_width, dtype=jnp.float32) * 2.0) / projected.shape[-1]
    )
    angles = positions[:, None] * inverse[None, :]
    cosine = jnp.cos(angles)[:, None, :]
    sine_table = jnp.sin(angles)[:, None, :]
    left_part = projected[..., :half_width]
    right_part = projected[..., half_width:]
    return jnp.concatenate(
        [
            left_part * cosine - right_part * sine_table,
            right_part * cosine + left_part * sine_table,
        ],
        axis=-1,
    )


def attend_rows(query_rows, key_rows, value_rows, allowed):
    scores = lax.dot_general(
        query_rows, key_rows, (((1,), (1,)), ((), ())), preferred_element_type=jnp.float32
    ) * query_rows.shape[-1] ** (-0.5)
    scores = jnp.where(allowed, scores, -jnp.inf)
    highest = jnp.max(scores, axis=-1, keepdims=True)
    weights = jnp.exp(scores - highest)
    totals = jnp.sum(weights, axis=-1, keepdims=True)
    partial_out = (
        jnp.dot(weights.astype(jnp.bfloat16), value_rows, preferred_element_type=jnp.float32)
        / totals
    ).astype(jnp.bfloat16)
    return (partial_out, (highest + jnp.log(totals))[:, 0])


def cache_kernel(live_ref, q_ref, k_ref, v_ref, out_ref):
    live = live_ref[0]
    keys = k_ref[...]
    values = v_ref[...]
    rows = q_ref.shape[1]
    width = out_ref.shape[2]
    visible = lax.broadcasted_iota(jnp.int32, (1, keys.shape[0]), 1) < live
    for src in range(q_ref.shape[0]):
        log_rows = []
        for h in range(q_ref.shape[2] // HD):
            q = q_ref[src, :, h * HD:(h + 1) * HD]
            scores = lax.dot_general(
                q, keys, (((1,), (1,)), ((), ())), preferred_element_type=jnp.float32
            ) * HD ** (-0.5)
            scores = jnp.where(visible, scores, -jnp.inf)
            highest = jnp.max(scores, axis=-1, keepdims=True)
            weights = jnp.exp(scores - highest)
            totals = jnp.sum(weights, axis=-1, keepdims=True)
            part = jnp.dot(weights.astype(jnp.bfloat16), values, preferred_element_type=jnp.float32)
            out_ref[src, :rows, h * HD:(h + 1) * HD] = (part / totals).astype(out_ref.dtype)
            log_col = jnp.broadcast_to(highest + jnp.log(totals), (rows, HD))
            rest = jnp.transpose(log_col)[0:1, :]
            for _ in range(3):
                piece = rest.astype(jnp.bfloat16).astype(jnp.float32)
                log_rows.append(piece)
                rest = rest - piece
        if rows < width:
            log_rows = [jnp.concatenate([r, jnp.zeros((1, width - rows), jnp.float32)], axis=1) for r in log_rows]
        log_rows += [jnp.zeros((1, width), jnp.float32)] * (out_ref.shape[1] - rows - len(log_rows))
        out_ref[src, rows:, :] = jnp.concatenate(log_rows, axis=0).astype(out_ref.dtype)


LOG_ROWS = 8


def cache_attention(live, every_query, cached_keys, cached_values):
    sources, span_rows, width = every_query.shape
    kv_heads = cached_keys.shape[1] // HD
    per_head = sources // kv_heads
    rows = cached_keys.shape[0]
    grid_spec = pltpu.PrefetchScalarGridSpec(
        num_scalar_prefetch=1,
        grid=(kv_heads,),
        in_specs=[
            pl.BlockSpec((per_head, span_rows, width), lambda g, live: (g, 0, 0)),
            pl.BlockSpec((rows, HD), lambda g, live: (0, g)),
            pl.BlockSpec((rows, HD), lambda g, live: (0, g)),
        ],
        out_specs=pl.BlockSpec((per_head, span_rows + LOG_ROWS, width), lambda g, live: (g, 0, 0)),
    )
    return pl.pallas_call(
        cache_kernel,
        grid_spec=grid_spec,
        out_shape=jax.ShapeDtypeStruct((sources, span_rows + LOG_ROWS, width), jnp.bfloat16),
    )(live, every_query, cached_keys, cached_values)


def combine_kernel(parts_ref, own_out_ref, own_log_ref, weight_ref, out_ref, attended_ref):
    @pl.when(pl.program_id(0) == 0)
    def _():
        combine_into(parts_ref, own_out_ref, own_log_ref, attended_ref)

    out_ref[...] = jnp.dot(
        attended_ref[...], weight_ref[...], preferred_element_type=jnp.float32
    ).astype(out_ref.dtype)


def combine_into(parts_ref, own_out_ref, own_log_ref, out_ref):
    sources = parts_ref.shape[0]
    rows = out_ref.shape[0]
    heads_here = out_ref.shape[1] // HD
    logs = [[] for _ in range(heads_here)]
    for b in range(sources):
        packed = parts_ref[b, rows:rows + LOG_ROWS, :].astype(jnp.float32)
        for h in range(heads_here):
            logs[h].append((packed[3 * h + 2:3 * h + 3] + packed[3 * h + 1:3 * h + 2]) + packed[3 * h:3 * h + 1])
    own_logs = own_log_ref[...]
    table_rows = []
    for h in range(heads_here):
        own_log = own_logs[h:h + 1]
        ceiling = own_log
        for lg in logs[h]:
            ceiling = jnp.maximum(ceiling, lg)
        own_factor = jnp.exp(own_log - ceiling)
        factors = [jnp.exp(lg - ceiling) for lg in logs[h]]
        total = own_factor
        for factor in factors:
            total = total + factor
        table_rows += [own_factor] + factors + [total]
    size = 128 * pl.cdiv(len(table_rows), 128)
    which = lax.broadcasted_iota(jnp.int32, (size, rows), 0)
    table = jnp.zeros((size, rows), jnp.float32)
    for j, row in enumerate(table_rows):
        table = jnp.where(which == j, jnp.broadcast_to(row, (size, rows)), table)
    columns = jnp.transpose(table)
    for h in range(heads_here):
        base = h * (sources + 2)
        weighted = columns[:, base:base + 1] * own_out_ref[:, h * HD:(h + 1) * HD].astype(jnp.float32)
        for b in range(sources):
            weighted = weighted + columns[:, base + 1 + b:base + 2 + b] * parts_ref[
                b, :rows, h * HD:(h + 1) * HD
            ].astype(jnp.float32)
        total = columns[:, base + sources + 1:base + sources + 2]
        out_ref[:, h * HD:(h + 1) * HD] = (weighted / total).astype(out_ref.dtype)


COLUMN_BLOCK = 1024


def combine(arrived_parts, own_out, own_log, out_weight):
    sources, packed_rows, width = arrived_parts.shape
    rows = own_out.shape[0]
    columns = out_weight.shape[1]
    return pl.pallas_call(
        combine_kernel,
        grid=(columns // COLUMN_BLOCK,),
        in_specs=[
            pl.BlockSpec((sources, packed_rows, width), lambda j: (0, 0, 0)),
            pl.BlockSpec(own_out.shape, lambda j: (0, 0)),
            pl.BlockSpec(own_log.shape, lambda j: (0, 0)),
            pl.BlockSpec((out_weight.shape[0], COLUMN_BLOCK), lambda j: (0, j)),
        ],
        out_specs=pl.BlockSpec((rows, COLUMN_BLOCK), lambda j: (0, j)),
        out_shape=jax.ShapeDtypeStruct((rows, columns), jnp.bfloat16),
        scratch_shapes=[pltpu.VMEM(own_out.shape, jnp.bfloat16)],
        compiler_params=pltpu.CompilerParams(dimension_semantics=("arbitrary",)),
    )(arrived_parts, own_out, own_log, out_weight)


def residual_kernel(position_ref, terms_ref, current_ref, out_ref):
    total = terms_ref[0].astype(jnp.float32)
    for n in range(1, terms_ref.shape[0]):
        total = total + terms_ref[n].astype(jnp.float32)
    mixed = (current_ref[...].astype(jnp.float32) + total).astype(out_ref.dtype)
    for n in range(out_ref.shape[0]):
        out_ref[n] = mixed


def residual(position, gathered_terms, current):
    sources, chunk, width = gathered_terms.shape
    grid_spec = pltpu.PrefetchScalarGridSpec(
        num_scalar_prefetch=1,
        grid=(1,),
        in_specs=[
            pl.BlockSpec((sources, chunk, width), lambda i, pos: (0, 0, 0)),
            pl.BlockSpec((chunk, width), lambda i, pos: (pos[0], 0)),
        ],
        out_specs=pl.BlockSpec((sources, chunk, width), lambda i, pos: (0, 0, 0)),
    )
    return pl.pallas_call(
        residual_kernel,
        grid_spec=grid_spec,
        out_shape=jax.ShapeDtypeStruct((sources, chunk, width), jnp.bfloat16),
    )(position, gathered_terms, current)


def shards(
    fresh,
    previous,
    span_index,
    cache_counts,
    norm_gain,
    w_query,
    w_keyval,
    w_out,
    cache_keys,
    cache_values,
):
    blocks = lax.axis_size("blk")
    position = lax.axis_index("blk")
    span_rows = fresh.shape[0]
    first_span = span_index[0]
    heads_here = w_query.shape[2] // HD
    odd_member = position % 2 == 1
    live = cache_counts[0, position].reshape(1)
    arrived = passed_along(previous[0], "segment", 1)
    current = jnp.where(lax.axis_index("segment") == 0, fresh, arrived)
    widened = current.astype(jnp.float32)
    normed = (
        widened
        * lax.rsqrt(jnp.mean(widened * widened, axis=-1, keepdims=True) + EPSILON)
        * norm_gain[0]
    ).astype(jnp.bfloat16)
    queries = jnp.dot(normed, w_query[0], preferred_element_type=jnp.float32).reshape(
        span_rows, heads_here, HD
    )
    queries = rotate(queries, first_span).astype(jnp.bfloat16).reshape(span_rows, heads_here * HD)
    projected = jnp.dot(normed, w_keyval[0], preferred_element_type=jnp.float32)
    as_key = rotate(projected[:, None, :], first_span)[:, 0, :].astype(jnp.bfloat16)
    mine = jnp.where(odd_member, projected.astype(jnp.bfloat16), as_key)
    partner = swapped(mine, "blk", 0)
    own_keys = jnp.where(odd_member, partner, mine)
    own_values = jnp.where(odd_member, mine, partner)
    every_query = lax.all_to_all(
        jnp.broadcast_to(queries[None], (blocks,) + queries.shape), "blk", 0, 0, tiled=True
    )
    held = cache_attention(live, every_query, cache_keys[0], cache_values[0])
    arrived_parts = lax.all_to_all(held, "blk", split_axis=0, concat_axis=0, tiled=True)
    query_rows = queries.reshape(span_rows * heads_here, HD)
    row_tokens = jnp.arange(span_rows * heads_here, dtype=jnp.int32) // heads_here
    causal = row_tokens[:, None] >= jnp.arange(span_rows, dtype=jnp.int32)[None, :]
    own_out, own_log = attend_rows(query_rows, own_keys, own_values, causal)
    own_out = own_out.reshape(span_rows, heads_here * HD)
    own_log = own_log.reshape(span_rows, heads_here).T
    head_terms = combine(arrived_parts, own_out, own_log, w_out[0])
    chunk = span_rows // blocks
    gathered_terms = lax.all_to_all(
        head_terms.reshape(blocks, chunk, -1), "blk", 0, 0, tiled=True
    )
    spread = residual(position.reshape(1), gathered_terms, current)
    mixed = lax.all_to_all(spread, "blk", 0, 0, tiled=True).reshape(span_rows, -1)
    return mixed[None]


def solution(mesh):
    placed = (
        P(),
        P("segment", None, None),
        P("segment"),
        P("segment", None),
        P("segment", None),
        P("segment", None, "blk"),
        P("segment", None, "blk"),
        P("segment", "blk", None),
        P("segment", "blk", None),
        P("segment", "blk", None),
    )
    return jax.shard_map(
        shards, mesh=mesh, in_specs=placed, out_specs=P("segment", None, None), check_vma=False
    )
```

```python
import jax
import jax.numpy as jnp
from jax import lax
from jax.sharding import PartitionSpec as P
from jax.experimental import pallas as pl
from jax.experimental.pallas import tpu as pltpu

KVH = 8
HD = 128


ROPE_BASE = 500000.0
EPSILON = 1e-05


def passed_along(block, axis, distance):
    devices = range(lax.axis_size(axis))
    route = [(i - distance, i) for i in devices if i - distance in devices]
    return lax.ppermute(block, axis, route)


def swapped(block, axis, distance):
    count = lax.axis_size(axis)
    route = []
    for low in range(count):
        high = low | 1 << distance
        if high != low and high < count:
            route += [(low, high), (high, low)]
    return lax.ppermute(block, axis, route)


def rotate(projected, first_span):
    length = projected.shape[0]
    half_width = projected.shape[-1] // 2
    positions = (first_span * length + jnp.arange(length, dtype=jnp.int32)).astype(jnp.float32)
    inverse = ROPE_BASE ** (
        -(jnp.arange(half_width, dtype=jnp.float32) * 2.0) / projected.shape[-1]
    )
    angles = positions[:, None] * inverse[None, :]
    cosine = jnp.cos(angles)[:, None, :]
    sine_table = jnp.sin(angles)[:, None, :]
    left_part = projected[..., :half_width]
    right_part = projected[..., half_width:]
    return jnp.concatenate(
        [
            left_part * cosine - right_part * sine_table,
            right_part * cosine + left_part * sine_table,
        ],
        axis=-1,
    )


def attend_rows(query_rows, key_rows, value_rows, allowed):
    scores = lax.dot_general(
        query_rows, key_rows, (((1,), (1,)), ((), ())), preferred_element_type=jnp.float32
    ) * query_rows.shape[-1] ** (-0.5)
    scores = jnp.where(allowed, scores, -jnp.inf)
    highest = jnp.max(scores, axis=-1, keepdims=True)
    weights = jnp.exp(scores - highest)
    totals = jnp.sum(weights, axis=-1, keepdims=True)
    partial_out = (
        jnp.dot(weights.astype(jnp.bfloat16), value_rows, preferred_element_type=jnp.float32)
        / totals
    ).astype(jnp.bfloat16)
    return (partial_out, (highest + jnp.log(totals))[:, 0])


def cache_kernel(live_ref, q_ref, k_ref, v_ref, out_ref):
    live = live_ref[0]
    keys = k_ref[...]
    values = v_ref[...]
    rows = q_ref.shape[1]
    width = out_ref.shape[2]
    visible = lax.broadcasted_iota(jnp.int32, (1, keys.shape[0]), 1) < live
    for src in range(q_ref.shape[0]):
        log_rows = []
        for h in range(q_ref.shape[2] // HD):
            q = q_ref[src, :, h * HD:(h + 1) * HD]
            scores = lax.dot_general(
                q, keys, (((1,), (1,)), ((), ())), preferred_element_type=jnp.float32
            ) * HD ** (-0.5)
            scores = jnp.where(visible, scores, -jnp.inf)
            highest = jnp.max(scores, axis=-1, keepdims=True)
            weights = jnp.exp(scores - highest)
            totals = jnp.sum(weights, axis=-1, keepdims=True)
            part = jnp.dot(weights.astype(jnp.bfloat16), values, preferred_element_type=jnp.float32)
            out_ref[src, :rows, h * HD:(h + 1) * HD] = (part / totals).astype(out_ref.dtype)
            log_col = jnp.broadcast_to(highest + jnp.log(totals), (rows, HD))
            rest = jnp.transpose(log_col)[0:1, :]
            for _ in range(3):
                piece = rest.astype(jnp.bfloat16).astype(jnp.float32)
                log_rows.append(piece)
                rest = rest - piece
        if rows < width:
            log_rows = [jnp.concatenate([r, jnp.zeros((1, width - rows), jnp.float32)], axis=1) for r in log_rows]
        log_rows += [jnp.zeros((1, width), jnp.float32)] * (out_ref.shape[1] - rows - len(log_rows))
        out_ref[src, rows:, :] = jnp.concatenate(log_rows, axis=0).astype(out_ref.dtype)


LOG_ROWS = 8


def cache_attention(live, every_query, cached_keys, cached_values):
    sources, span_rows, width = every_query.shape
    kv_heads = cached_keys.shape[1] // HD
    per_head = sources // kv_heads
    rows = cached_keys.shape[0]
    grid_spec = pltpu.PrefetchScalarGridSpec(
        num_scalar_prefetch=1,
        grid=(kv_heads,),
        in_specs=[
            pl.BlockSpec((per_head, span_rows, width), lambda g, live: (g, 0, 0)),
            pl.BlockSpec((rows, HD), lambda g, live: (0, g)),
            pl.BlockSpec((rows, HD), lambda g, live: (0, g)),
        ],
        out_specs=pl.BlockSpec((per_head, span_rows + LOG_ROWS, width), lambda g, live: (g, 0, 0)),
    )
    return pl.pallas_call(
        cache_kernel,
        grid_spec=grid_spec,
        out_shape=jax.ShapeDtypeStruct((sources, span_rows + LOG_ROWS, width), jnp.bfloat16),
    )(live, every_query, cached_keys, cached_values)


def combine_kernel(*refs):
    parts_refs = refs[:-5]
    own_out_ref, own_log_ref, weight_ref, out_ref, attended_ref = refs[-5:]

    @pl.when(pl.program_id(0) == 0)
    def _():
        rows = own_out_ref.shape[0] // len(parts_refs)
        for i, parts_ref in enumerate(parts_refs):
            combine_into(
                parts_ref,
                own_out_ref.at[pl.ds(i * rows, rows), :],
                own_log_ref.at[:, pl.ds(i * rows, rows)],
                attended_ref.at[pl.ds(i * rows, rows), :],
            )

    out_ref[...] = jnp.dot(
        attended_ref[...], weight_ref[...], preferred_element_type=jnp.float32
    ).astype(out_ref.dtype)


def combine_into(parts_ref, own_out_ref, own_log_ref, out_ref):
    sources = parts_ref.shape[0]
    rows = out_ref.shape[0]
    heads_here = out_ref.shape[1] // HD
    logs = [[] for _ in range(heads_here)]
    for b in range(sources):
        packed = parts_ref[b, rows:rows + LOG_ROWS, :rows].astype(jnp.float32)
        for h in range(heads_here):
            logs[h].append((packed[3 * h + 2:3 * h + 3] + packed[3 * h + 1:3 * h + 2]) + packed[3 * h:3 * h + 1])
    own_logs = own_log_ref[...]
    table_rows = []
    for h in range(heads_here):
        own_log = own_logs[h:h + 1]
        ceiling = own_log
        for lg in logs[h]:
            ceiling = jnp.maximum(ceiling, lg)
        own_factor = jnp.exp(own_log - ceiling)
        factors = [jnp.exp(lg - ceiling) for lg in logs[h]]
        total = own_factor
        for factor in factors:
            total = total + factor
        table_rows += [own_factor] + factors + [total]
    size = 128 * pl.cdiv(len(table_rows), 128)
    which = lax.broadcasted_iota(jnp.int32, (size, rows), 0)
    table = jnp.zeros((size, rows), jnp.float32)
    for j, row in enumerate(table_rows):
        table = jnp.where(which == j, jnp.broadcast_to(row, (size, rows)), table)
    columns = jnp.transpose(table)
    for h in range(heads_here):
        base = h * (sources + 2)
        weighted = columns[:, base:base + 1] * own_out_ref[:, h * HD:(h + 1) * HD].astype(jnp.float32)
        for b in range(sources):
            weighted = weighted + columns[:, base + 1 + b:base + 2 + b] * parts_ref[
                b, :rows, h * HD:(h + 1) * HD
            ].astype(jnp.float32)
        total = columns[:, base + sources + 1:base + sources + 2]
        out_ref[:, h * HD:(h + 1) * HD] = (weighted / total).astype(out_ref.dtype)


COLUMN_BLOCK = 1024


def combine(arrived_halves, own_out, own_log, out_weight):
    sources, packed_rows, width = arrived_halves[0].shape
    rows = own_out.shape[0]
    columns = out_weight.shape[1]
    return pl.pallas_call(
        combine_kernel,
        grid=(columns // COLUMN_BLOCK,),
        in_specs=[pl.BlockSpec((sources, packed_rows, width), lambda j: (0, 0, 0)) for _ in arrived_halves]
        + [
            pl.BlockSpec(own_out.shape, lambda j: (0, 0)),
            pl.BlockSpec(own_log.shape, lambda j: (0, 0)),
            pl.BlockSpec((out_weight.shape[0], COLUMN_BLOCK), lambda j: (0, j)),
        ],
        out_specs=pl.BlockSpec((rows, COLUMN_BLOCK), lambda j: (0, j)),
        out_shape=jax.ShapeDtypeStruct((rows, columns), jnp.bfloat16),
        scratch_shapes=[pltpu.VMEM(own_out.shape, jnp.bfloat16)],
        compiler_params=pltpu.CompilerParams(dimension_semantics=("arbitrary",)),
    )(*arrived_halves, own_out, own_log, out_weight)


def residual_kernel(position_ref, terms_ref, current_ref, out_ref):
    total = terms_ref[0].astype(jnp.float32)
    for n in range(1, terms_ref.shape[0]):
        total = total + terms_ref[n].astype(jnp.float32)
    mixed = (current_ref[...].astype(jnp.float32) + total).astype(out_ref.dtype)
    for n in range(out_ref.shape[0]):
        out_ref[n] = mixed


def residual(position, gathered_terms, current):
    sources, chunk, width = gathered_terms.shape
    grid_spec = pltpu.PrefetchScalarGridSpec(
        num_scalar_prefetch=1,
        grid=(1,),
        in_specs=[
            pl.BlockSpec((sources, chunk, width), lambda i, pos: (0, 0, 0)),
            pl.BlockSpec((chunk, width), lambda i, pos: (pos[0], 0)),
        ],
        out_specs=pl.BlockSpec((sources, chunk, width), lambda i, pos: (0, 0, 0)),
    )
    return pl.pallas_call(
        residual_kernel,
        grid_spec=grid_spec,
        out_shape=jax.ShapeDtypeStruct((sources, chunk, width), jnp.bfloat16),
    )(position, gathered_terms, current)


def shards(
    fresh,
    previous,
    span_index,
    cache_counts,
    norm_gain,
    w_query,
    w_keyval,
    w_out,
    cache_keys,
    cache_values,
):
    blocks = lax.axis_size("blk")
    position = lax.axis_index("blk")
    span_rows = fresh.shape[0]
    first_span = span_index[0]
    heads_here = w_query.shape[2] // HD
    odd_member = position % 2 == 1
    live = cache_counts[0, position].reshape(1)
    arrived = passed_along(previous[0], "segment", 1)
    current = jnp.where(lax.axis_index("segment") == 0, fresh, arrived)
    widened = current.astype(jnp.float32)
    normed = (
        widened
        * lax.rsqrt(jnp.mean(widened * widened, axis=-1, keepdims=True) + EPSILON)
        * norm_gain[0]
    ).astype(jnp.bfloat16)
    queries = jnp.dot(normed, w_query[0], preferred_element_type=jnp.float32).reshape(
        span_rows, heads_here, HD
    )
    queries = rotate(queries, first_span).astype(jnp.bfloat16).reshape(span_rows, heads_here * HD)
    projected = jnp.dot(normed, w_keyval[0], preferred_element_type=jnp.float32)
    as_key = rotate(projected[:, None, :], first_span)[:, 0, :].astype(jnp.bfloat16)
    mine = jnp.where(odd_member, projected.astype(jnp.bfloat16), as_key)
    partner = swapped(mine, "blk", 0)
    own_keys = jnp.where(odd_member, partner, mine)
    own_values = jnp.where(odd_member, mine, partner)
    partner, queries = lax.optimization_barrier((partner, queries))
    halves = 2
    half_rows = span_rows // halves
    arrived_halves = []
    for i in range(halves):
        half = queries[i * half_rows:(i + 1) * half_rows]
        every_query = lax.all_to_all(
            jnp.broadcast_to(half[None], (blocks,) + half.shape), "blk", 0, 0, tiled=True
        )
        held = cache_attention(live, every_query, cache_keys[0], cache_values[0])
        arrived_halves.append(lax.all_to_all(held, "blk", split_axis=0, concat_axis=0, tiled=True))
    query_rows = queries.reshape(span_rows * heads_here, HD)
    row_tokens = jnp.arange(span_rows * heads_here, dtype=jnp.int32) // heads_here
    causal = row_tokens[:, None] >= jnp.arange(span_rows, dtype=jnp.int32)[None, :]
    own_out, own_log = attend_rows(query_rows, own_keys, own_values, causal)
    own_out = own_out.reshape(span_rows, heads_here * HD)
    own_log = own_log.reshape(span_rows, heads_here).T
    head_terms = combine(arrived_halves, own_out, own_log, w_out[0])
    chunk = span_rows // blocks
    gathered_terms = lax.all_to_all(
        head_terms.reshape(blocks, chunk, -1), "blk", 0, 0, tiled=True
    )
    spread = residual(position.reshape(1), gathered_terms, current)
    mixed = lax.all_to_all(spread, "blk", 0, 0, tiled=True).reshape(span_rows, -1)
    return mixed[None]


def solution(mesh):
    placed = (
        P(),
        P("segment", None, None),
        P("segment"),
        P("segment", None),
        P("segment", None),
        P("segment", None, "blk"),
        P("segment", None, "blk"),
        P("segment", "blk", None),
        P("segment", "blk", None),
        P("segment", "blk", None),
    )
    return jax.shard_map(
        shards, mesh=mesh, in_specs=placed, out_specs=P("segment", None, None), check_vma=False
    )
```

```python
import jax
import jax.numpy as jnp
from jax import lax
from jax.sharding import PartitionSpec as P
from jax.experimental import pallas as pl
from jax.experimental.pallas import tpu as pltpu

KVH = 8
HD = 128


ROPE_BASE = 500000.0
EPSILON = 1e-05


def passed_along(block, axis, distance):
    devices = range(lax.axis_size(axis))
    route = [(i - distance, i) for i in devices if i - distance in devices]
    return lax.ppermute(block, axis, route)


def swapped(block, axis, distance):
    count = lax.axis_size(axis)
    route = []
    for low in range(count):
        high = low | 1 << distance
        if high != low and high < count:
            route += [(low, high), (high, low)]
    return lax.ppermute(block, axis, route)


def rotate(projected, first_span):
    length = projected.shape[0]
    half_width = projected.shape[-1] // 2
    positions = (first_span * length + jnp.arange(length, dtype=jnp.int32)).astype(jnp.float32)
    inverse = ROPE_BASE ** (
        -(jnp.arange(half_width, dtype=jnp.float32) * 2.0) / projected.shape[-1]
    )
    angles = positions[:, None] * inverse[None, :]
    cosine = jnp.cos(angles)[:, None, :]
    sine_table = jnp.sin(angles)[:, None, :]
    left_part = projected[..., :half_width]
    right_part = projected[..., half_width:]
    return jnp.concatenate(
        [
            left_part * cosine - right_part * sine_table,
            right_part * cosine + left_part * sine_table,
        ],
        axis=-1,
    )


def attend_rows(query_rows, key_rows, value_rows, allowed):
    scores = lax.dot_general(
        query_rows, key_rows, (((1,), (1,)), ((), ())), preferred_element_type=jnp.float32
    ) * query_rows.shape[-1] ** (-0.5)
    scores = jnp.where(allowed, scores, -jnp.inf)
    highest = jnp.max(scores, axis=-1, keepdims=True)
    weights = jnp.exp(scores - highest)
    totals = jnp.sum(weights, axis=-1, keepdims=True)
    partial_out = (
        jnp.dot(weights.astype(jnp.bfloat16), value_rows, preferred_element_type=jnp.float32)
        / totals
    ).astype(jnp.bfloat16)
    return (partial_out, (highest + jnp.log(totals))[:, 0])


def cache_kernel(live_ref, q_ref, k_ref, v_ref, out_ref):
    live = live_ref[0]
    keys = k_ref[...]
    values = v_ref[...]
    sources, rows = q_ref.shape[0], q_ref.shape[1]
    width = out_ref.shape[2]
    group = max(1, min(sources, 256 // rows))
    visible = lax.broadcasted_iota(jnp.int32, (1, keys.shape[0]), 1) < live
    log_rows = {src: [] for src in range(sources)}
    for first in range(0, sources, group):
        members = list(range(first, min(first + group, sources)))
        for h in range(q_ref.shape[2] // HD):
            q = jnp.concatenate([q_ref[src, :, h * HD:(h + 1) * HD] for src in members], axis=0)
            scores = lax.dot_general(
                q, keys, (((1,), (1,)), ((), ())), preferred_element_type=jnp.float32
            ) * HD ** (-0.5)
            scores = jnp.where(visible, scores, -jnp.inf)
            highest = jnp.max(scores, axis=-1, keepdims=True)
            weights = jnp.exp(scores - highest)
            totals = jnp.sum(weights, axis=-1, keepdims=True)
            part = jnp.dot(weights.astype(jnp.bfloat16), values, preferred_element_type=jnp.float32)
            normalized = (part / totals).astype(out_ref.dtype)
            log_totals = highest + jnp.log(totals)
            for i, src in enumerate(members):
                out_ref[src, :rows, h * HD:(h + 1) * HD] = normalized[i * rows:(i + 1) * rows]
                log_col = jnp.broadcast_to(log_totals[i * rows:(i + 1) * rows], (rows, HD))
                rest = jnp.transpose(log_col)[0:1, :]
                for _ in range(3):
                    piece = rest.astype(jnp.bfloat16).astype(jnp.float32)
                    log_rows[src].append(piece)
                    rest = rest - piece
    for src in range(sources):
        rows_here = log_rows[src]
        if rows < width:
            rows_here = [jnp.concatenate([r, jnp.zeros((1, width - rows), jnp.float32)], axis=1) for r in rows_here]
        rows_here = rows_here + [jnp.zeros((1, width), jnp.float32)] * (out_ref.shape[1] - rows - len(rows_here))
        out_ref[src, rows:, :] = jnp.concatenate(rows_here, axis=0).astype(out_ref.dtype)


LOG_ROWS = 8


def cache_attention(live, every_query, cached_keys, cached_values):
    sources, span_rows, width = every_query.shape
    kv_heads = cached_keys.shape[1] // HD
    per_head = sources // kv_heads
    rows = cached_keys.shape[0]
    grid_spec = pltpu.PrefetchScalarGridSpec(
        num_scalar_prefetch=1,
        grid=(kv_heads,),
        in_specs=[
            pl.BlockSpec((per_head, span_rows, width), lambda g, live: (g, 0, 0)),
            pl.BlockSpec((rows, HD), lambda g, live: (0, g)),
            pl.BlockSpec((rows, HD), lambda g, live: (0, g)),
        ],
        out_specs=pl.BlockSpec((per_head, span_rows + LOG_ROWS, width), lambda g, live: (g, 0, 0)),
    )
    return pl.pallas_call(
        cache_kernel,
        grid_spec=grid_spec,
        out_shape=jax.ShapeDtypeStruct((sources, span_rows + LOG_ROWS, width), jnp.bfloat16),
    )(live, every_query, cached_keys, cached_values)


def combine_kernel(*refs):
    parts_refs = refs[:-5]
    own_out_ref, own_log_ref, weight_ref, out_ref, attended_ref = refs[-5:]

    @pl.when(pl.program_id(0) == 0)
    def _():
        rows = own_out_ref.shape[0] // len(parts_refs)
        for i, parts_ref in enumerate(parts_refs):
            combine_into(
                parts_ref,
                own_out_ref.at[pl.ds(i * rows, rows), :],
                own_log_ref.at[:, pl.ds(i * rows, rows)],
                attended_ref.at[pl.ds(i * rows, rows), :],
            )

    out_ref[...] = jnp.dot(
        attended_ref[...], weight_ref[...], preferred_element_type=jnp.float32
    ).astype(out_ref.dtype)


def combine_into(parts_ref, own_out_ref, own_log_ref, out_ref):
    sources = parts_ref.shape[0]
    rows = out_ref.shape[0]
    heads_here = out_ref.shape[1] // HD
    logs = [[] for _ in range(heads_here)]
    for b in range(sources):
        packed = parts_ref[b, rows:rows + LOG_ROWS, :rows].astype(jnp.float32)
        for h in range(heads_here):
            logs[h].append((packed[3 * h + 2:3 * h + 3] + packed[3 * h + 1:3 * h + 2]) + packed[3 * h:3 * h + 1])
    own_logs = own_log_ref[...]
    table_rows = []
    for h in range(heads_here):
        own_log = own_logs[h:h + 1]
        ceiling = own_log
        for lg in logs[h]:
            ceiling = jnp.maximum(ceiling, lg)
        own_factor = jnp.exp(own_log - ceiling)
        factors = [jnp.exp(lg - ceiling) for lg in logs[h]]
        total = own_factor
        for factor in factors:
            total = total + factor
        table_rows += [own_factor] + factors + [total]
    size = 128 * pl.cdiv(len(table_rows), 128)
    which = lax.broadcasted_iota(jnp.int32, (size, rows), 0)
    table = jnp.zeros((size, rows), jnp.float32)
    for j, row in enumerate(table_rows):
        table = jnp.where(which == j, jnp.broadcast_to(row, (size, rows)), table)
    columns = jnp.transpose(table)
    for h in range(heads_here):
        base = h * (sources + 2)
        weighted = columns[:, base:base + 1] * own_out_ref[:, h * HD:(h + 1) * HD].astype(jnp.float32)
        for b in range(sources):
            weighted = weighted + columns[:, base + 1 + b:base + 2 + b] * parts_ref[
                b, :rows, h * HD:(h + 1) * HD
            ].astype(jnp.float32)
        total = columns[:, base + sources + 1:base + sources + 2]
        out_ref[:, h * HD:(h + 1) * HD] = (weighted / total).astype(out_ref.dtype)


COLUMN_BLOCK = 1024


def combine(arrived_halves, own_out, own_log, out_weight):
    sources, packed_rows, width = arrived_halves[0].shape
    rows = own_out.shape[0]
    columns = out_weight.shape[1]
    return pl.pallas_call(
        combine_kernel,
        grid=(columns // COLUMN_BLOCK,),
        in_specs=[pl.BlockSpec((sources, packed_rows, width), lambda j: (0, 0, 0)) for _ in arrived_halves]
        + [
            pl.BlockSpec(own_out.shape, lambda j: (0, 0)),
            pl.BlockSpec(own_log.shape, lambda j: (0, 0)),
            pl.BlockSpec((out_weight.shape[0], COLUMN_BLOCK), lambda j: (0, j)),
        ],
        out_specs=pl.BlockSpec((rows, COLUMN_BLOCK), lambda j: (0, j)),
        out_shape=jax.ShapeDtypeStruct((rows, columns), jnp.bfloat16),
        scratch_shapes=[pltpu.VMEM(own_out.shape, jnp.bfloat16)],
        compiler_params=pltpu.CompilerParams(dimension_semantics=("arbitrary",)),
    )(*arrived_halves, own_out, own_log, out_weight)


def residual_kernel(position_ref, terms_ref, current_ref, out_ref):
    total = terms_ref[0].astype(jnp.float32)
    for n in range(1, terms_ref.shape[0]):
        total = total + terms_ref[n].astype(jnp.float32)
    mixed = (current_ref[...].astype(jnp.float32) + total).astype(out_ref.dtype)
    for n in range(out_ref.shape[0]):
        out_ref[n] = mixed


def residual(position, gathered_terms, current):
    sources, chunk, width = gathered_terms.shape
    grid_spec = pltpu.PrefetchScalarGridSpec(
        num_scalar_prefetch=1,
        grid=(1,),
        in_specs=[
            pl.BlockSpec((sources, chunk, width), lambda i, pos: (0, 0, 0)),
            pl.BlockSpec((chunk, width), lambda i, pos: (pos[0], 0)),
        ],
        out_specs=pl.BlockSpec((sources, chunk, width), lambda i, pos: (0, 0, 0)),
    )
    return pl.pallas_call(
        residual_kernel,
        grid_spec=grid_spec,
        out_shape=jax.ShapeDtypeStruct((sources, chunk, width), jnp.bfloat16),
    )(position, gathered_terms, current)


def shards(
    fresh,
    previous,
    span_index,
    cache_counts,
    norm_gain,
    w_query,
    w_keyval,
    w_out,
    cache_keys,
    cache_values,
):
    blocks = lax.axis_size("blk")
    position = lax.axis_index("blk")
    span_rows = fresh.shape[0]
    first_span = span_index[0]
    heads_here = w_query.shape[2] // HD
    odd_member = position % 2 == 1
    live = cache_counts[0, position].reshape(1)
    arrived = passed_along(previous[0], "segment", 1)
    current = jnp.where(lax.axis_index("segment") == 0, fresh, arrived)
    widened = current.astype(jnp.float32)
    normed = (
        widened
        * lax.rsqrt(jnp.mean(widened * widened, axis=-1, keepdims=True) + EPSILON)
        * norm_gain[0]
    ).astype(jnp.bfloat16)
    queries = jnp.dot(normed, w_query[0], preferred_element_type=jnp.float32).reshape(
        span_rows, heads_here, HD
    )
    queries = rotate(queries, first_span).astype(jnp.bfloat16).reshape(span_rows, heads_here * HD)
    projected = jnp.dot(normed, w_keyval[0], preferred_element_type=jnp.float32)
    as_key = rotate(projected[:, None, :], first_span)[:, 0, :].astype(jnp.bfloat16)
    mine = jnp.where(odd_member, projected.astype(jnp.bfloat16), as_key)
    partner = swapped(mine, "blk", 0)
    own_keys = jnp.where(odd_member, partner, mine)
    own_values = jnp.where(odd_member, mine, partner)
    partner, queries = lax.optimization_barrier((partner, queries))
    halves = 2
    half_rows = span_rows // halves
    arrived_halves = []
    for i in range(halves):
        half = queries[i * half_rows:(i + 1) * half_rows]
        every_query = lax.all_to_all(
            jnp.broadcast_to(half[None], (blocks,) + half.shape), "blk", 0, 0, tiled=True
        )
        held = cache_attention(live, every_query, cache_keys[0], cache_values[0])
        arrived_halves.append(lax.all_to_all(held, "blk", split_axis=0, concat_axis=0, tiled=True))
    query_rows = queries.reshape(span_rows * heads_here, HD)
    row_tokens = jnp.arange(span_rows * heads_here, dtype=jnp.int32) // heads_here
    causal = row_tokens[:, None] >= jnp.arange(span_rows, dtype=jnp.int32)[None, :]
    own_out, own_log = attend_rows(query_rows, own_keys, own_values, causal)
    own_out = own_out.reshape(span_rows, heads_here * HD)
    own_log = own_log.reshape(span_rows, heads_here).T
    head_terms = combine(arrived_halves, own_out, own_log, w_out[0])
    chunk = span_rows // blocks
    gathered_terms = lax.all_to_all(
        head_terms.reshape(blocks, chunk, -1), "blk", 0, 0, tiled=True
    )
    spread = residual(position.reshape(1), gathered_terms, current)
    mixed = lax.all_to_all(spread, "blk", 0, 0, tiled=True).reshape(span_rows, -1)
    return mixed[None]


def solution(mesh):
    placed = (
        P(),
        P("segment", None, None),
        P("segment"),
        P("segment", None),
        P("segment", None),
        P("segment", None, "blk"),
        P("segment", None, "blk"),
        P("segment", "blk", None),
        P("segment", "blk", None),
        P("segment", "blk", None),
    )
    return jax.shard_map(
        shards, mesh=mesh, in_specs=placed, out_specs=P("segment", None, None), check_vma=False
    )
```

```python
import jax
import jax.numpy as jnp
from jax import lax
from jax.sharding import PartitionSpec as P
from jax.experimental import pallas as pl
from jax.experimental.pallas import tpu as pltpu

KVH = 8
HD = 128


ROPE_BASE = 500000.0
EPSILON = 1e-05


def passed_along(block, axis, distance):
    devices = range(lax.axis_size(axis))
    route = [(i - distance, i) for i in devices if i - distance in devices]
    return lax.ppermute(block, axis, route)


def swapped(block, axis, distance):
    count = lax.axis_size(axis)
    route = []
    for low in range(count):
        high = low | 1 << distance
        if high != low and high < count:
            route += [(low, high), (high, low)]
    return lax.ppermute(block, axis, route)


def rotate(projected, first_span):
    length = projected.shape[0]
    half_width = projected.shape[-1] // 2
    positions = (first_span * length + jnp.arange(length, dtype=jnp.int32)).astype(jnp.float32)
    inverse = ROPE_BASE ** (
        -(jnp.arange(half_width, dtype=jnp.float32) * 2.0) / projected.shape[-1]
    )
    angles = positions[:, None] * inverse[None, :]
    cosine = jnp.cos(angles)[:, None, :]
    sine_table = jnp.sin(angles)[:, None, :]
    left_part = projected[..., :half_width]
    right_part = projected[..., half_width:]
    return jnp.concatenate(
        [
            left_part * cosine - right_part * sine_table,
            right_part * cosine + left_part * sine_table,
        ],
        axis=-1,
    )


def attend_rows(query_rows, key_rows, value_rows, allowed):
    scores = lax.dot_general(
        query_rows, key_rows, (((1,), (1,)), ((), ())), preferred_element_type=jnp.float32
    ) * query_rows.shape[-1] ** (-0.5)
    scores = jnp.where(allowed, scores, -jnp.inf)
    highest = jnp.max(scores, axis=-1, keepdims=True)
    weights = jnp.exp(scores - highest)
    totals = jnp.sum(weights, axis=-1, keepdims=True)
    partial_out = (
        jnp.dot(weights.astype(jnp.bfloat16), value_rows, preferred_element_type=jnp.float32)
        / totals
    ).astype(jnp.bfloat16)
    return (partial_out, (highest + jnp.log(totals))[:, 0])


def cache_kernel(live_ref, q_ref, k_ref, v_ref, out_ref):
    live = live_ref[0]
    keys = k_ref[...]
    values = v_ref[...]
    sources, rows = q_ref.shape[0], q_ref.shape[1]
    width = out_ref.shape[2]
    group = max(1, min(sources, 256 // rows))
    visible = lax.broadcasted_iota(jnp.int32, (1, keys.shape[0]), 1) < live
    log_rows = {src: [] for src in range(sources)}
    for first in range(0, sources, group):
        members = list(range(first, min(first + group, sources)))
        for h in range(q_ref.shape[2] // HD):
            q = jnp.concatenate([q_ref[src, :, h * HD:(h + 1) * HD] for src in members], axis=0)
            scores = lax.dot_general(
                q, keys, (((1,), (1,)), ((), ())), preferred_element_type=jnp.float32
            ) * HD ** (-0.5)
            scores = jnp.where(visible, scores, -jnp.inf)
            highest = jnp.max(scores, axis=-1, keepdims=True)
            weights = jnp.exp(scores - highest)
            totals = jnp.sum(weights, axis=-1, keepdims=True)
            part = jnp.dot(weights.astype(jnp.bfloat16), values, preferred_element_type=jnp.float32)
            normalized = (part / totals).astype(out_ref.dtype)
            log_totals = highest + jnp.log(totals)
            for i, src in enumerate(members):
                out_ref[src, :rows, h * HD:(h + 1) * HD] = normalized[i * rows:(i + 1) * rows]
                log_col = jnp.broadcast_to(log_totals[i * rows:(i + 1) * rows], (rows, HD))
                rest = jnp.transpose(log_col)[0:1, :]
                for _ in range(3):
                    piece = rest.astype(jnp.bfloat16).astype(jnp.float32)
                    log_rows[src].append(piece)
                    rest = rest - piece
    for src in range(sources):
        rows_here = log_rows[src]
        if rows < width:
            rows_here = [jnp.concatenate([r, jnp.zeros((1, width - rows), jnp.float32)], axis=1) for r in rows_here]
        rows_here = rows_here + [jnp.zeros((1, width), jnp.float32)] * (out_ref.shape[1] - rows - len(rows_here))
        out_ref[src, rows:, :] = jnp.concatenate(rows_here, axis=0).astype(out_ref.dtype)


LOG_ROWS = 8


def cache_attention(live, every_query, cached_keys, cached_values):
    sources, span_rows, width = every_query.shape
    kv_heads = cached_keys.shape[1] // HD
    per_head = sources // kv_heads
    rows = cached_keys.shape[0]
    grid_spec = pltpu.PrefetchScalarGridSpec(
        num_scalar_prefetch=1,
        grid=(kv_heads,),
        in_specs=[
            pl.BlockSpec((per_head, span_rows, width), lambda g, live: (g, 0, 0)),
            pl.BlockSpec((rows, HD), lambda g, live: (0, g)),
            pl.BlockSpec((rows, HD), lambda g, live: (0, g)),
        ],
        out_specs=pl.BlockSpec((per_head, span_rows + LOG_ROWS, width), lambda g, live: (g, 0, 0)),
    )
    return pl.pallas_call(
        cache_kernel,
        grid_spec=grid_spec,
        out_shape=jax.ShapeDtypeStruct((sources, span_rows + LOG_ROWS, width), jnp.bfloat16),
    )(live, every_query, cached_keys, cached_values)


def combine_kernel(*refs):
    parts_refs = refs[:-5]
    own_out_ref, own_log_ref, weight_ref, out_ref, attended_ref = refs[-5:]

    @pl.when(pl.program_id(0) == 0)
    def _():
        rows = own_out_ref.shape[0] // len(parts_refs)
        for i, parts_ref in enumerate(parts_refs):
            combine_into(
                parts_ref,
                own_out_ref.at[pl.ds(i * rows, rows), :],
                own_log_ref.at[:, pl.ds(i * rows, rows)],
                attended_ref.at[pl.ds(i * rows, rows), :],
            )

    out_ref[...] = jnp.dot(
        attended_ref[...], weight_ref[...], preferred_element_type=jnp.float32
    ).astype(out_ref.dtype)


def combine_into(parts_ref, own_out_ref, own_log_ref, out_ref):
    sources = parts_ref.shape[0]
    rows = out_ref.shape[0]
    heads_here = out_ref.shape[1] // HD
    logs = [[] for _ in range(heads_here)]
    for b in range(sources):
        packed = parts_ref[b, rows:rows + LOG_ROWS, :rows].astype(jnp.float32)
        for h in range(heads_here):
            logs[h].append((packed[3 * h + 2:3 * h + 3] + packed[3 * h + 1:3 * h + 2]) + packed[3 * h:3 * h + 1])
    own_logs = own_log_ref[...]
    table_rows = []
    for h in range(heads_here):
        own_log = own_logs[h:h + 1]
        ceiling = own_log
        for lg in logs[h]:
            ceiling = jnp.maximum(ceiling, lg)
        own_factor = jnp.exp(own_log - ceiling)
        factors = [jnp.exp(lg - ceiling) for lg in logs[h]]
        total = own_factor
        for factor in factors:
            total = total + factor
        table_rows += [own_factor] + factors + [total]
    size = 128 * pl.cdiv(len(table_rows), 128)
    which = lax.broadcasted_iota(jnp.int32, (size, rows), 0)
    table = jnp.zeros((size, rows), jnp.float32)
    for j, row in enumerate(table_rows):
        table = jnp.where(which == j, jnp.broadcast_to(row, (size, rows)), table)
    columns = jnp.transpose(table)
    for h in range(heads_here):
        base = h * (sources + 2)
        weighted = columns[:, base:base + 1] * own_out_ref[:, h * HD:(h + 1) * HD].astype(jnp.float32)
        for b in range(sources):
            weighted = weighted + columns[:, base + 1 + b:base + 2 + b] * parts_ref[
                b, :rows, h * HD:(h + 1) * HD
            ].astype(jnp.float32)
        total = columns[:, base + sources + 1:base + sources + 2]
        out_ref[:, h * HD:(h + 1) * HD] = (weighted / total).astype(out_ref.dtype)


COLUMN_BLOCK = 1024


def combine(arrived_halves, own_out, own_log, out_weight):
    sources, packed_rows, width = arrived_halves[0].shape
    rows = own_out.shape[0]
    columns = out_weight.shape[1]
    return pl.pallas_call(
        combine_kernel,
        grid=(columns // COLUMN_BLOCK,),
        in_specs=[pl.BlockSpec((sources, packed_rows, width), lambda j: (0, 0, 0)) for _ in arrived_halves]
        + [
            pl.BlockSpec(own_out.shape, lambda j: (0, 0)),
            pl.BlockSpec(own_log.shape, lambda j: (0, 0)),
            pl.BlockSpec((out_weight.shape[0], COLUMN_BLOCK), lambda j: (0, j)),
        ],
        out_specs=pl.BlockSpec((rows, COLUMN_BLOCK), lambda j: (0, j)),
        out_shape=jax.ShapeDtypeStruct((rows, columns), jnp.bfloat16),
        scratch_shapes=[pltpu.VMEM(own_out.shape, jnp.bfloat16)],
        compiler_params=pltpu.CompilerParams(dimension_semantics=("arbitrary",)),
    )(*arrived_halves, own_out, own_log, out_weight)


def residual_kernel(position_ref, terms_ref, current_ref, out_ref):
    total = terms_ref[0].astype(jnp.float32)
    for n in range(1, terms_ref.shape[0]):
        total = total + terms_ref[n].astype(jnp.float32)
    mixed = (current_ref[...].astype(jnp.float32) + total).astype(out_ref.dtype)
    for n in range(out_ref.shape[0]):
        out_ref[n] = mixed


def residual(position, gathered_terms, current):
    sources, chunk, width = gathered_terms.shape
    grid_spec = pltpu.PrefetchScalarGridSpec(
        num_scalar_prefetch=1,
        grid=(1,),
        in_specs=[
            pl.BlockSpec((sources, chunk, width), lambda i, pos: (0, 0, 0)),
            pl.BlockSpec((chunk, width), lambda i, pos: (pos[0], 0)),
        ],
        out_specs=pl.BlockSpec((sources, chunk, width), lambda i, pos: (0, 0, 0)),
    )
    return pl.pallas_call(
        residual_kernel,
        grid_spec=grid_spec,
        out_shape=jax.ShapeDtypeStruct((sources, chunk, width), jnp.bfloat16),
    )(position, gathered_terms, current)


def shards(
    fresh,
    previous,
    span_index,
    cache_counts,
    norm_gain,
    w_query,
    w_keyval,
    w_out,
    cache_keys,
    cache_values,
):
    blocks = lax.axis_size("blk")
    position = lax.axis_index("blk")
    span_rows = fresh.shape[0]
    first_span = span_index[0]
    heads_here = w_query.shape[2] // HD
    odd_member = position % 2 == 1
    live = cache_counts[0, position].reshape(1)
    first_segment = lax.axis_index("segment") == 0
    halves = 2
    half_rows = span_rows // halves
    currents, query_parts, key_parts, value_parts, arrived_halves = [], [], [], [], []
    outgoing = previous[0, :half_rows]
    for i in range(halves):
        rows_of = slice(i * half_rows, (i + 1) * half_rows)
        received = passed_along(outgoing, "segment", 1)
        if i + 1 < halves:
            outgoing, received = lax.optimization_barrier(
                (previous[0, (i + 1) * half_rows:(i + 2) * half_rows], received)
            )
        if i > 0:
            received, every_query = lax.optimization_barrier((received, every_query))
            held = cache_attention(live, every_query, cache_keys[0], cache_values[0])
            arrived_halves.append(lax.all_to_all(held, "blk", split_axis=0, concat_axis=0, tiled=True))
        current = jnp.where(first_segment, fresh[rows_of], received)
        currents.append(current)
        widened = current.astype(jnp.float32)
        normed = (
            widened
            * lax.rsqrt(jnp.mean(widened * widened, axis=-1, keepdims=True) + EPSILON)
            * norm_gain[0]
        ).astype(jnp.bfloat16)
        part_span = first_span * halves + i
        queries = jnp.dot(normed, w_query[0], preferred_element_type=jnp.float32).reshape(
            half_rows, heads_here, HD
        )
        queries = rotate(queries, part_span).astype(jnp.bfloat16).reshape(half_rows, heads_here * HD)
        projected = jnp.dot(normed, w_keyval[0], preferred_element_type=jnp.float32)
        as_key = rotate(projected[:, None, :], part_span)[:, 0, :].astype(jnp.bfloat16)
        mine = jnp.where(odd_member, projected.astype(jnp.bfloat16), as_key)
        partner = swapped(mine, "blk", 0)
        key_parts.append(jnp.where(odd_member, partner, mine))
        value_parts.append(jnp.where(odd_member, mine, partner))
        query_parts.append(queries)
        every_query = lax.all_to_all(
            jnp.broadcast_to(queries[None], (blocks,) + queries.shape), "blk", 0, 0, tiled=True
        )
    held = cache_attention(live, every_query, cache_keys[0], cache_values[0])
    arrived_halves.append(lax.all_to_all(held, "blk", split_axis=0, concat_axis=0, tiled=True))
    current = jnp.concatenate(currents, axis=0)
    queries = jnp.concatenate(query_parts, axis=0)
    own_keys = jnp.concatenate(key_parts, axis=0)
    own_values = jnp.concatenate(value_parts, axis=0)
    query_rows = queries.reshape(span_rows * heads_here, HD)
    row_tokens = jnp.arange(span_rows * heads_here, dtype=jnp.int32) // heads_here
    causal = row_tokens[:, None] >= jnp.arange(span_rows, dtype=jnp.int32)[None, :]
    own_out, own_log = attend_rows(query_rows, own_keys, own_values, causal)
    own_out = own_out.reshape(span_rows, heads_here * HD)
    own_log = own_log.reshape(span_rows, heads_here).T
    head_terms = combine(arrived_halves, own_out, own_log, w_out[0])
    chunk = span_rows // blocks
    gathered_terms = lax.all_to_all(
        head_terms.reshape(blocks, chunk, -1), "blk", 0, 0, tiled=True
    )
    spread = residual(position.reshape(1), gathered_terms, current)
    mixed = lax.all_to_all(spread, "blk", 0, 0, tiled=True).reshape(span_rows, -1)
    return mixed[None]


def solution(mesh):
    placed = (
        P(),
        P("segment", None, None),
        P("segment"),
        P("segment", None),
        P("segment", None),
        P("segment", None, "blk"),
        P("segment", None, "blk"),
        P("segment", "blk", None),
        P("segment", "blk", None),
        P("segment", "blk", None),
    )
    return jax.shard_map(
        shards, mesh=mesh, in_specs=placed, out_specs=P("segment", None, None), check_vma=False
    )
```

```python
import jax
import jax.numpy as jnp
from jax import lax
from jax.sharding import PartitionSpec as P
from jax.experimental import pallas as pl
from jax.experimental.pallas import tpu as pltpu

KVH = 8
HD = 128


ROPE_BASE = 500000.0
EPSILON = 1e-05


def passed_along(block, axis, distance):
    devices = range(lax.axis_size(axis))
    route = [(i - distance, i) for i in devices if i - distance in devices]
    return lax.ppermute(block, axis, route)


def swapped(block, axis, distance):
    count = lax.axis_size(axis)
    route = []
    for low in range(count):
        high = low | 1 << distance
        if high != low and high < count:
            route += [(low, high), (high, low)]
    return lax.ppermute(block, axis, route)


def rotate(projected, first_span):
    length = projected.shape[0]
    half_width = projected.shape[-1] // 2
    positions = (first_span * length + jnp.arange(length, dtype=jnp.int32)).astype(jnp.float32)
    inverse = ROPE_BASE ** (
        -(jnp.arange(half_width, dtype=jnp.float32) * 2.0) / projected.shape[-1]
    )
    angles = positions[:, None] * inverse[None, :]
    cosine = jnp.cos(angles)[:, None, :]
    sine_table = jnp.sin(angles)[:, None, :]
    left_part = projected[..., :half_width]
    right_part = projected[..., half_width:]
    return jnp.concatenate(
        [
            left_part * cosine - right_part * sine_table,
            right_part * cosine + left_part * sine_table,
        ],
        axis=-1,
    )


def attend_rows(query_rows, key_rows, value_rows, allowed):
    scores = lax.dot_general(
        query_rows, key_rows, (((1,), (1,)), ((), ())), preferred_element_type=jnp.float32
    ) * query_rows.shape[-1] ** (-0.5)
    scores = jnp.where(allowed, scores, -jnp.inf)
    highest = jnp.max(scores, axis=-1, keepdims=True)
    weights = jnp.exp(scores - highest)
    totals = jnp.sum(weights, axis=-1, keepdims=True)
    partial_out = (
        jnp.dot(weights.astype(jnp.bfloat16), value_rows, preferred_element_type=jnp.float32)
        / totals
    ).astype(jnp.bfloat16)
    return (partial_out, (highest + jnp.log(totals))[:, 0])


def cache_kernel(live_ref, q_ref, k_ref, v_ref, out_ref):
    live = live_ref[0]
    keys = k_ref[...]
    values = v_ref[...]
    sources, rows = q_ref.shape[0], q_ref.shape[1]
    width = out_ref.shape[2]
    group = max(1, min(sources, 256 // rows))
    visible = lax.broadcasted_iota(jnp.int32, (1, keys.shape[0]), 1) < live
    log_rows = {src: [] for src in range(sources)}
    for first in range(0, sources, group):
        members = list(range(first, min(first + group, sources)))
        for h in range(q_ref.shape[2] // HD):
            q = jnp.concatenate([q_ref[src, :, h * HD:(h + 1) * HD] for src in members], axis=0)
            scores = lax.dot_general(
                q, keys, (((1,), (1,)), ((), ())), preferred_element_type=jnp.float32
            ) * HD ** (-0.5)
            scores = jnp.where(visible, scores, -jnp.inf)
            highest = jnp.max(scores, axis=-1, keepdims=True)
            weights = jnp.exp(scores - highest)
            totals = jnp.sum(weights, axis=-1, keepdims=True)
            part = jnp.dot(weights.astype(jnp.bfloat16), values, preferred_element_type=jnp.float32)
            normalized = (part / totals).astype(out_ref.dtype)
            log_totals = highest + jnp.log(totals)
            for i, src in enumerate(members):
                out_ref[src, :rows, h * HD:(h + 1) * HD] = normalized[i * rows:(i + 1) * rows]
                log_col = jnp.broadcast_to(log_totals[i * rows:(i + 1) * rows], (rows, HD))
                rest = jnp.transpose(log_col)[0:1, :]
                for _ in range(3):
                    piece = rest.astype(jnp.bfloat16).astype(jnp.float32)
                    log_rows[src].append(piece)
                    rest = rest - piece
    for src in range(sources):
        rows_here = log_rows[src]
        if rows < width:
            rows_here = [jnp.concatenate([r, jnp.zeros((1, width - rows), jnp.float32)], axis=1) for r in rows_here]
        rows_here = rows_here + [jnp.zeros((1, width), jnp.float32)] * (out_ref.shape[1] - rows - len(rows_here))
        out_ref[src, rows:, :] = jnp.concatenate(rows_here, axis=0).astype(out_ref.dtype)


LOG_ROWS = 8


def cache_attention(live, every_query, cached_keys, cached_values):
    sources, span_rows, width = every_query.shape
    kv_heads = cached_keys.shape[1] // HD
    per_head = sources // kv_heads
    rows = cached_keys.shape[0]
    grid_spec = pltpu.PrefetchScalarGridSpec(
        num_scalar_prefetch=1,
        grid=(kv_heads,),
        in_specs=[
            pl.BlockSpec((per_head, span_rows, width), lambda g, live: (g, 0, 0)),
            pl.BlockSpec((rows, HD), lambda g, live: (0, g)),
            pl.BlockSpec((rows, HD), lambda g, live: (0, g)),
        ],
        out_specs=pl.BlockSpec((per_head, span_rows + LOG_ROWS, width), lambda g, live: (g, 0, 0)),
    )
    return pl.pallas_call(
        cache_kernel,
        grid_spec=grid_spec,
        out_shape=jax.ShapeDtypeStruct((sources, span_rows + LOG_ROWS, width), jnp.bfloat16),
    )(live, every_query, cached_keys, cached_values)


def combine_kernel(*refs):
    parts_refs = refs[:-5]
    own_out_ref, own_log_ref, weight_ref, out_ref, attended_ref = refs[-5:]

    @pl.when(pl.program_id(0) == 0)
    def _():
        rows = own_out_ref.shape[0] // len(parts_refs)
        for i, parts_ref in enumerate(parts_refs):
            combine_into(
                parts_ref,
                own_out_ref.at[pl.ds(i * rows, rows), :],
                own_log_ref.at[:, pl.ds(i * rows, rows)],
                attended_ref.at[pl.ds(i * rows, rows), :],
            )

    out_ref[...] = jnp.dot(
        attended_ref[...], weight_ref[...], preferred_element_type=jnp.float32
    ).astype(out_ref.dtype)


def combine_into(parts_ref, own_out_ref, own_log_ref, out_ref):
    sources = parts_ref.shape[0]
    rows = out_ref.shape[0]
    heads_here = out_ref.shape[1] // HD
    logs = [[] for _ in range(heads_here)]
    for b in range(sources):
        packed = parts_ref[b, rows:rows + LOG_ROWS, :rows].astype(jnp.float32)
        for h in range(heads_here):
            logs[h].append((packed[3 * h + 2:3 * h + 3] + packed[3 * h + 1:3 * h + 2]) + packed[3 * h:3 * h + 1])
    own_logs = own_log_ref[...]
    table_rows = []
    for h in range(heads_here):
        own_log = own_logs[h:h + 1]
        ceiling = own_log
        for lg in logs[h]:
            ceiling = jnp.maximum(ceiling, lg)
        own_factor = jnp.exp(own_log - ceiling)
        factors = [jnp.exp(lg - ceiling) for lg in logs[h]]
        total = own_factor
        for factor in factors:
            total = total + factor
        table_rows += [own_factor] + factors + [total]
    size = 128 * pl.cdiv(len(table_rows), 128)
    which = lax.broadcasted_iota(jnp.int32, (size, rows), 0)
    table = jnp.zeros((size, rows), jnp.float32)
    for j, row in enumerate(table_rows):
        table = jnp.where(which == j, jnp.broadcast_to(row, (size, rows)), table)
    columns = jnp.transpose(table)
    for h in range(heads_here):
        base = h * (sources + 2)
        weighted = columns[:, base:base + 1] * own_out_ref[:, h * HD:(h + 1) * HD].astype(jnp.float32)
        for b in range(sources):
            weighted = weighted + columns[:, base + 1 + b:base + 2 + b] * parts_ref[
                b, :rows, h * HD:(h + 1) * HD
            ].astype(jnp.float32)
        total = columns[:, base + sources + 1:base + sources + 2]
        out_ref[:, h * HD:(h + 1) * HD] = (weighted / total).astype(out_ref.dtype)


COLUMN_BLOCK = 1024


def combine(arrived_halves, own_out, own_log, out_weight):
    sources, packed_rows, width = arrived_halves[0].shape
    rows = own_out.shape[0]
    columns = out_weight.shape[1]
    return pl.pallas_call(
        combine_kernel,
        grid=(columns // COLUMN_BLOCK,),
        in_specs=[pl.BlockSpec((sources, packed_rows, width), lambda j: (0, 0, 0)) for _ in arrived_halves]
        + [
            pl.BlockSpec(own_out.shape, lambda j: (0, 0)),
            pl.BlockSpec(own_log.shape, lambda j: (0, 0)),
            pl.BlockSpec((out_weight.shape[0], COLUMN_BLOCK), lambda j: (0, j)),
        ],
        out_specs=pl.BlockSpec((rows, COLUMN_BLOCK), lambda j: (0, j)),
        out_shape=jax.ShapeDtypeStruct((rows, columns), jnp.bfloat16),
        scratch_shapes=[pltpu.VMEM(own_out.shape, jnp.bfloat16)],
        compiler_params=pltpu.CompilerParams(dimension_semantics=("arbitrary",)),
    )(*arrived_halves, own_out, own_log, out_weight)


def residual_kernel(position_ref, terms_ref, current_ref, out_ref):
    total = terms_ref[0].astype(jnp.float32)
    for n in range(1, terms_ref.shape[0]):
        total = total + terms_ref[n].astype(jnp.float32)
    mixed = (current_ref[...].astype(jnp.float32) + total).astype(out_ref.dtype)
    for n in range(out_ref.shape[0]):
        out_ref[n] = mixed


def residual(position, gathered_terms, current):
    sources, chunk, width = gathered_terms.shape
    grid_spec = pltpu.PrefetchScalarGridSpec(
        num_scalar_prefetch=1,
        grid=(1,),
        in_specs=[
            pl.BlockSpec((sources, chunk, width), lambda i, pos: (0, 0, 0)),
            pl.BlockSpec((chunk, width), lambda i, pos: (pos[0], 0)),
        ],
        out_specs=pl.BlockSpec((sources, chunk, width), lambda i, pos: (0, 0, 0)),
    )
    return pl.pallas_call(
        residual_kernel,
        grid_spec=grid_spec,
        out_shape=jax.ShapeDtypeStruct((sources, chunk, width), jnp.bfloat16),
    )(position, gathered_terms, current)


def shards(
    fresh,
    previous,
    span_index,
    cache_counts,
    norm_gain,
    w_query,
    w_keyval,
    w_out,
    cache_keys,
    cache_values,
):
    blocks = lax.axis_size("blk")
    position = lax.axis_index("blk")
    span_rows = fresh.shape[0]
    first_span = span_index[0]
    heads_here = w_query.shape[2] // HD
    odd_member = position % 2 == 1
    live = cache_counts[0, position].reshape(1)
    arrived = passed_along(previous[0], "segment", 1)
    current = jnp.where(lax.axis_index("segment") == 0, fresh, arrived)
    widened = current.astype(jnp.float32)
    normed = (
        widened
        * lax.rsqrt(jnp.mean(widened * widened, axis=-1, keepdims=True) + EPSILON)
        * norm_gain[0]
    ).astype(jnp.bfloat16)
    queries = jnp.dot(normed, w_query[0], preferred_element_type=jnp.float32).reshape(
        span_rows, heads_here, HD
    )
    queries = rotate(queries, first_span).astype(jnp.bfloat16).reshape(span_rows, heads_here * HD)
    projected = jnp.dot(normed, w_keyval[0], preferred_element_type=jnp.float32)
    as_key = rotate(projected[:, None, :], first_span)[:, 0, :].astype(jnp.bfloat16)
    mine = jnp.where(odd_member, projected.astype(jnp.bfloat16), as_key)
    partner = swapped(mine, "blk", 0)
    own_keys = jnp.where(odd_member, partner, mine)
    own_values = jnp.where(odd_member, mine, partner)
    partner, queries = lax.optimization_barrier((partner, queries))
    halves = 2
    half_rows = span_rows // halves
    arrived_halves = []
    for i in range(halves):
        half = queries[i * half_rows:(i + 1) * half_rows]
        every_query = lax.all_to_all(
            jnp.broadcast_to(half[None], (blocks,) + half.shape), "blk", 0, 0, tiled=True
        )
        held = cache_attention(live, every_query, cache_keys[0], cache_values[0])
        arrived_halves.append(lax.all_to_all(held, "blk", split_axis=0, concat_axis=0, tiled=True))
    query_rows = queries.reshape(span_rows * heads_here, HD)
    row_tokens = jnp.arange(span_rows * heads_here, dtype=jnp.int32) // heads_here
    causal = row_tokens[:, None] >= jnp.arange(span_rows, dtype=jnp.int32)[None, :]
    own_out, own_log = attend_rows(query_rows, own_keys, own_values, causal)
    own_out = own_out.reshape(span_rows, heads_here * HD)
    own_log = own_log.reshape(span_rows, heads_here).T
    head_terms = jnp.concatenate(
        [
            combine(
                [part],
                own_out[i * half_rows:(i + 1) * half_rows],
                own_log[:, i * half_rows:(i + 1) * half_rows],
                w_out[0],
            )
            for i, part in enumerate(arrived_halves)
        ],
        axis=0,
    )
    chunk = span_rows // blocks
    gathered_terms = lax.all_to_all(
        head_terms.reshape(blocks, chunk, -1), "blk", 0, 0, tiled=True
    )
    spread = residual(position.reshape(1), gathered_terms, current)
    mixed = lax.all_to_all(spread, "blk", 0, 0, tiled=True).reshape(span_rows, -1)
    return mixed[None]


def solution(mesh):
    placed = (
        P(),
        P("segment", None, None),
        P("segment"),
        P("segment", None),
        P("segment", None),
        P("segment", None, "blk"),
        P("segment", None, "blk"),
        P("segment", "blk", None),
        P("segment", "blk", None),
        P("segment", "blk", None),
    )
    return jax.shard_map(
        shards, mesh=mesh, in_specs=placed, out_specs=P("segment", None, None), check_vma=False
    )
```

```python
import jax
import jax.numpy as jnp
from jax import lax
from jax.sharding import PartitionSpec as P
from jax.experimental import pallas as pl
from jax.experimental.pallas import tpu as pltpu

KVH = 8
HD = 128


ROPE_BASE = 500000.0
EPSILON = 1e-05


def passed_along(block, axis, distance):
    devices = range(lax.axis_size(axis))
    route = [(i - distance, i) for i in devices if i - distance in devices]
    return lax.ppermute(block, axis, route)


def swapped(block, axis, distance):
    count = lax.axis_size(axis)
    route = []
    for low in range(count):
        high = low | 1 << distance
        if high != low and high < count:
            route += [(low, high), (high, low)]
    return lax.ppermute(block, axis, route)


def rotate(projected, first_span):
    length = projected.shape[0]
    half_width = projected.shape[-1] // 2
    positions = (first_span * length + jnp.arange(length, dtype=jnp.int32)).astype(jnp.float32)
    inverse = ROPE_BASE ** (
        -(jnp.arange(half_width, dtype=jnp.float32) * 2.0) / projected.shape[-1]
    )
    angles = positions[:, None] * inverse[None, :]
    cosine = jnp.cos(angles)[:, None, :]
    sine_table = jnp.sin(angles)[:, None, :]
    left_part = projected[..., :half_width]
    right_part = projected[..., half_width:]
    return jnp.concatenate(
        [
            left_part * cosine - right_part * sine_table,
            right_part * cosine + left_part * sine_table,
        ],
        axis=-1,
    )


def attend_rows(query_rows, key_rows, value_rows, allowed):
    scores = lax.dot_general(
        query_rows, key_rows, (((1,), (1,)), ((), ())), preferred_element_type=jnp.float32
    ) * query_rows.shape[-1] ** (-0.5)
    scores = jnp.where(allowed, scores, -jnp.inf)
    highest = jnp.max(scores, axis=-1, keepdims=True)
    weights = jnp.exp(scores - highest)
    totals = jnp.sum(weights, axis=-1, keepdims=True)
    partial_out = (
        jnp.dot(weights.astype(jnp.bfloat16), value_rows, preferred_element_type=jnp.float32)
        / totals
    ).astype(jnp.bfloat16)
    return (partial_out, (highest + jnp.log(totals))[:, 0])


def cache_kernel(live_ref, q_ref, k_ref, v_ref, out_ref):
    live = live_ref[0]
    keys = k_ref[...]
    values = v_ref[...]
    sources, rows = q_ref.shape[0], q_ref.shape[1]
    width = out_ref.shape[2]
    group = max(1, min(sources, 256 // rows))
    visible = lax.broadcasted_iota(jnp.int32, (1, keys.shape[0]), 1) < live
    log_rows = {src: [] for src in range(sources)}
    for first in range(0, sources, group):
        members = list(range(first, min(first + group, sources)))
        for h in range(q_ref.shape[2] // HD):
            q = jnp.concatenate([q_ref[src, :, h * HD:(h + 1) * HD] for src in members], axis=0)
            scores = lax.dot_general(
                q, keys, (((1,), (1,)), ((), ())), preferred_element_type=jnp.float32
            ) * HD ** (-0.5)
            scores = jnp.where(visible, scores, -jnp.inf)
            highest = jnp.max(scores, axis=-1, keepdims=True)
            weights = jnp.exp(scores - highest)
            totals = jnp.sum(weights, axis=-1, keepdims=True)
            part = jnp.dot(weights.astype(jnp.bfloat16), values, preferred_element_type=jnp.float32)
            normalized = (part / totals).astype(out_ref.dtype)
            log_totals = highest + jnp.log(totals)
            for i, src in enumerate(members):
                out_ref[src, :rows, h * HD:(h + 1) * HD] = normalized[i * rows:(i + 1) * rows]
                log_col = jnp.broadcast_to(log_totals[i * rows:(i + 1) * rows], (rows, HD))
                rest = jnp.transpose(log_col)[0:1, :]
                for _ in range(3):
                    piece = rest.astype(jnp.bfloat16).astype(jnp.float32)
                    log_rows[src].append(piece)
                    rest = rest - piece
    for src in range(sources):
        rows_here = log_rows[src]
        if rows < width:
            rows_here = [jnp.concatenate([r, jnp.zeros((1, width - rows), jnp.float32)], axis=1) for r in rows_here]
        rows_here = rows_here + [jnp.zeros((1, width), jnp.float32)] * (out_ref.shape[1] - rows - len(rows_here))
        out_ref[src, rows:, :] = jnp.concatenate(rows_here, axis=0).astype(out_ref.dtype)


LOG_ROWS = 8


def cache_attention(live, every_query, cached_keys, cached_values):
    sources, span_rows, width = every_query.shape
    kv_heads = cached_keys.shape[1] // HD
    per_head = sources // kv_heads
    rows = cached_keys.shape[0]
    grid_spec = pltpu.PrefetchScalarGridSpec(
        num_scalar_prefetch=1,
        grid=(kv_heads,),
        in_specs=[
            pl.BlockSpec((per_head, span_rows, width), lambda g, live: (g, 0, 0)),
            pl.BlockSpec((rows, HD), lambda g, live: (0, g)),
            pl.BlockSpec((rows, HD), lambda g, live: (0, g)),
        ],
        out_specs=pl.BlockSpec((per_head, span_rows + LOG_ROWS, width), lambda g, live: (g, 0, 0)),
    )
    return pl.pallas_call(
        cache_kernel,
        grid_spec=grid_spec,
        out_shape=jax.ShapeDtypeStruct((sources, span_rows + LOG_ROWS, width), jnp.bfloat16),
    )(live, every_query, cached_keys, cached_values)


def combine_kernel(*refs):
    parts_refs = refs[:-5]
    own_out_ref, own_log_ref, weight_ref, out_ref, attended_ref = refs[-5:]

    @pl.when(pl.program_id(0) == 0)
    def _():
        rows = own_out_ref.shape[0] // len(parts_refs)
        for i, parts_ref in enumerate(parts_refs):
            combine_into(
                parts_ref,
                own_out_ref.at[pl.ds(i * rows, rows), :],
                own_log_ref.at[:, pl.ds(i * rows, rows)],
                attended_ref.at[pl.ds(i * rows, rows), :],
            )

    out_ref[...] = jnp.dot(
        attended_ref[...], weight_ref[...], preferred_element_type=jnp.float32
    ).astype(out_ref.dtype)


def combine_into(parts_ref, own_out_ref, own_log_ref, out_ref):
    sources = parts_ref.shape[0]
    rows = out_ref.shape[0]
    heads_here = out_ref.shape[1] // HD
    logs = [[] for _ in range(heads_here)]
    for b in range(sources):
        packed = parts_ref[b, rows:rows + LOG_ROWS, :rows].astype(jnp.float32)
        for h in range(heads_here):
            logs[h].append((packed[3 * h + 2:3 * h + 3] + packed[3 * h + 1:3 * h + 2]) + packed[3 * h:3 * h + 1])
    own_logs = own_log_ref[...]
    table_rows = []
    for h in range(heads_here):
        own_log = own_logs[h:h + 1]
        ceiling = own_log
        for lg in logs[h]:
            ceiling = jnp.maximum(ceiling, lg)
        own_factor = jnp.exp(own_log - ceiling)
        factors = [jnp.exp(lg - ceiling) for lg in logs[h]]
        total = own_factor
        for factor in factors:
            total = total + factor
        table_rows += [own_factor] + factors + [total]
    size = 128 * pl.cdiv(len(table_rows), 128)
    which = lax.broadcasted_iota(jnp.int32, (size, rows), 0)
    table = jnp.zeros((size, rows), jnp.float32)
    for j, row in enumerate(table_rows):
        table = jnp.where(which == j, jnp.broadcast_to(row, (size, rows)), table)
    columns = jnp.transpose(table)
    for h in range(heads_here):
        base = h * (sources + 2)
        weighted = columns[:, base:base + 1] * own_out_ref[:, h * HD:(h + 1) * HD].astype(jnp.float32)
        for b in range(sources):
            weighted = weighted + columns[:, base + 1 + b:base + 2 + b] * parts_ref[
                b, :rows, h * HD:(h + 1) * HD
            ].astype(jnp.float32)
        total = columns[:, base + sources + 1:base + sources + 2]
        out_ref[:, h * HD:(h + 1) * HD] = (weighted / total).astype(out_ref.dtype)


COLUMN_BLOCK = 1024


def combine(arrived_halves, own_out, own_log, out_weight):
    sources, packed_rows, width = arrived_halves[0].shape
    rows = own_out.shape[0]
    columns = out_weight.shape[1]
    return pl.pallas_call(
        combine_kernel,
        grid=(columns // COLUMN_BLOCK,),
        in_specs=[pl.BlockSpec((sources, packed_rows, width), lambda j: (0, 0, 0)) for _ in arrived_halves]
        + [
            pl.BlockSpec(own_out.shape, lambda j: (0, 0)),
            pl.BlockSpec(own_log.shape, lambda j: (0, 0)),
            pl.BlockSpec((out_weight.shape[0], COLUMN_BLOCK), lambda j: (0, j)),
        ],
        out_specs=pl.BlockSpec((rows, COLUMN_BLOCK), lambda j: (0, j)),
        out_shape=jax.ShapeDtypeStruct((rows, columns), jnp.bfloat16),
        scratch_shapes=[pltpu.VMEM(own_out.shape, jnp.bfloat16)],
        compiler_params=pltpu.CompilerParams(dimension_semantics=("arbitrary",)),
    )(*arrived_halves, own_out, own_log, out_weight)


def residual_kernel(position_ref, terms_ref, current_ref, out_ref):
    total = terms_ref[0].astype(jnp.float32)
    for n in range(1, terms_ref.shape[0]):
        total = total + terms_ref[n].astype(jnp.float32)
    mixed = (current_ref[...].astype(jnp.float32) + total).astype(out_ref.dtype)
    for n in range(out_ref.shape[0]):
        out_ref[n] = mixed


def residual(position, gathered_terms, current):
    sources, chunk, width = gathered_terms.shape
    grid_spec = pltpu.PrefetchScalarGridSpec(
        num_scalar_prefetch=1,
        grid=(1,),
        in_specs=[
            pl.BlockSpec((sources, chunk, width), lambda i, pos: (0, 0, 0)),
            pl.BlockSpec((chunk, width), lambda i, pos: (pos[0], 0)),
        ],
        out_specs=pl.BlockSpec((sources, chunk, width), lambda i, pos: (0, 0, 0)),
    )
    return pl.pallas_call(
        residual_kernel,
        grid_spec=grid_spec,
        out_shape=jax.ShapeDtypeStruct((sources, chunk, width), jnp.bfloat16),
    )(position, gathered_terms, current)


def shards(
    fresh,
    previous,
    span_index,
    cache_counts,
    norm_gain,
    w_query,
    w_keyval,
    w_out,
    cache_keys,
    cache_values,
):
    blocks = lax.axis_size("blk")
    position = lax.axis_index("blk")
    span_rows = fresh.shape[0]
    first_span = span_index[0]
    heads_here = w_query.shape[2] // HD
    odd_member = position % 2 == 1
    live = cache_counts[0, position].reshape(1)
    arrived = passed_along(previous[0], "segment", 1)
    current = jnp.where(lax.axis_index("segment") == 0, fresh, arrived)
    widened = current.astype(jnp.float32)
    normed = (
        widened
        * lax.rsqrt(jnp.mean(widened * widened, axis=-1, keepdims=True) + EPSILON)
        * norm_gain[0]
    ).astype(jnp.bfloat16)
    queries = jnp.dot(normed, w_query[0], preferred_element_type=jnp.float32).reshape(
        span_rows, heads_here, HD
    )
    queries = rotate(queries, first_span).astype(jnp.bfloat16).reshape(span_rows, heads_here * HD)
    projected = jnp.dot(normed, w_keyval[0], preferred_element_type=jnp.float32)
    as_key = rotate(projected[:, None, :], first_span)[:, 0, :].astype(jnp.bfloat16)
    mine = jnp.where(odd_member, projected.astype(jnp.bfloat16), as_key)
    partner = swapped(mine, "blk", 0)
    own_keys = jnp.where(odd_member, partner, mine)
    own_values = jnp.where(odd_member, mine, partner)
    halves = 2
    half_rows = span_rows // halves
    arrived_halves = []
    for i in range(halves):
        half = queries[i * half_rows:(i + 1) * half_rows]
        every_query = lax.all_to_all(
            jnp.broadcast_to(half[None], (blocks,) + half.shape), "blk", 0, 0, tiled=True
        )
        held = cache_attention(live, every_query, cache_keys[0], cache_values[0])
        arrived_halves.append(lax.all_to_all(held, "blk", split_axis=0, concat_axis=0, tiled=True))
    query_rows = queries.reshape(span_rows * heads_here, HD)
    row_tokens = jnp.arange(span_rows * heads_here, dtype=jnp.int32) // heads_here
    causal = row_tokens[:, None] >= jnp.arange(span_rows, dtype=jnp.int32)[None, :]
    own_out, own_log = attend_rows(query_rows, own_keys, own_values, causal)
    own_out = own_out.reshape(span_rows, heads_here * HD)
    own_log = own_log.reshape(span_rows, heads_here).T
    head_terms = combine(arrived_halves, own_out, own_log, w_out[0])
    chunk = span_rows // blocks
    gathered_terms = lax.all_to_all(
        head_terms.reshape(blocks, chunk, -1), "blk", 0, 0, tiled=True
    )
    spread = residual(position.reshape(1), gathered_terms, current)
    mixed = lax.all_to_all(spread, "blk", 0, 0, tiled=True).reshape(span_rows, -1)
    return mixed[None]


def solution(mesh):
    placed = (
        P(),
        P("segment", None, None),
        P("segment"),
        P("segment", None),
        P("segment", None),
        P("segment", None, "blk"),
        P("segment", None, "blk"),
        P("segment", "blk", None),
        P("segment", "blk", None),
        P("segment", "blk", None),
    )
    return jax.shard_map(
        shards, mesh=mesh, in_specs=placed, out_specs=P("segment", None, None), check_vma=False
    )
```

```python
import jax
import jax.numpy as jnp
from jax import lax
from jax.sharding import PartitionSpec as P
from jax.experimental import pallas as pl
from jax.experimental.pallas import tpu as pltpu

KVH = 8
HD = 128


ROPE_BASE = 500000.0
EPSILON = 1e-05


def passed_along(block, axis, distance):
    devices = range(lax.axis_size(axis))
    route = [(i - distance, i) for i in devices if i - distance in devices]
    return lax.ppermute(block, axis, route)


def swapped(block, axis, distance):
    count = lax.axis_size(axis)
    route = []
    for low in range(count):
        high = low | 1 << distance
        if high != low and high < count:
            route += [(low, high), (high, low)]
    return lax.ppermute(block, axis, route)


def rotate(projected, first_span):
    length = projected.shape[0]
    half_width = projected.shape[-1] // 2
    positions = (first_span * length + jnp.arange(length, dtype=jnp.int32)).astype(jnp.float32)
    inverse = ROPE_BASE ** (
        -(jnp.arange(half_width, dtype=jnp.float32) * 2.0) / projected.shape[-1]
    )
    angles = positions[:, None] * inverse[None, :]
    cosine = jnp.cos(angles)[:, None, :]
    sine_table = jnp.sin(angles)[:, None, :]
    left_part = projected[..., :half_width]
    right_part = projected[..., half_width:]
    return jnp.concatenate(
        [
            left_part * cosine - right_part * sine_table,
            right_part * cosine + left_part * sine_table,
        ],
        axis=-1,
    )


def attend_rows(query_rows, key_rows, value_rows, allowed):
    scores = lax.dot_general(
        query_rows, key_rows, (((1,), (1,)), ((), ())), preferred_element_type=jnp.float32
    ) * query_rows.shape[-1] ** (-0.5)
    scores = jnp.where(allowed, scores, -jnp.inf)
    highest = jnp.max(scores, axis=-1, keepdims=True)
    weights = jnp.exp(scores - highest)
    totals = jnp.sum(weights, axis=-1, keepdims=True)
    partial_out = (
        jnp.dot(weights.astype(jnp.bfloat16), value_rows, preferred_element_type=jnp.float32)
        / totals
    ).astype(jnp.bfloat16)
    return (partial_out, (highest + jnp.log(totals))[:, 0])


def cache_kernel(live_ref, q_ref, k_ref, v_ref, out_ref):
    live = live_ref[0]
    keys = k_ref[...]
    values = v_ref[...]
    sources, rows = q_ref.shape[0], q_ref.shape[1]
    width = out_ref.shape[2]
    group = max(1, min(sources, 256 // rows))
    visible = lax.broadcasted_iota(jnp.int32, (1, keys.shape[0]), 1) < live
    log_rows = {src: [] for src in range(sources)}
    for first in range(0, sources, group):
        members = list(range(first, min(first + group, sources)))
        for h in range(q_ref.shape[2] // HD):
            q = jnp.concatenate([q_ref[src, :, h * HD:(h + 1) * HD] for src in members], axis=0)
            scores = lax.dot_general(
                q, keys, (((1,), (1,)), ((), ())), preferred_element_type=jnp.float32
            ) * HD ** (-0.5)
            scores = jnp.where(visible, scores, -jnp.inf)
            highest = jnp.max(scores, axis=-1, keepdims=True)
            weights = jnp.exp(scores - highest)
            totals = jnp.sum(weights, axis=-1, keepdims=True)
            part = jnp.dot(weights.astype(jnp.bfloat16), values, preferred_element_type=jnp.float32)
            normalized = (part / totals).astype(out_ref.dtype)
            log_totals = highest + jnp.log(totals)
            for i, src in enumerate(members):
                out_ref[src, :rows, h * HD:(h + 1) * HD] = normalized[i * rows:(i + 1) * rows]
                log_col = jnp.broadcast_to(log_totals[i * rows:(i + 1) * rows], (rows, HD))
                rest = jnp.transpose(log_col)[0:1, :]
                for _ in range(3):
                    piece = rest.astype(jnp.bfloat16).astype(jnp.float32)
                    log_rows[src].append(piece)
                    rest = rest - piece
    for src in range(sources):
        rows_here = log_rows[src]
        if rows < width:
            rows_here = [jnp.concatenate([r, jnp.zeros((1, width - rows), jnp.float32)], axis=1) for r in rows_here]
        rows_here = rows_here + [jnp.zeros((1, width), jnp.float32)] * (out_ref.shape[1] - rows - len(rows_here))
        out_ref[src, rows:, :] = jnp.concatenate(rows_here, axis=0).astype(out_ref.dtype)


LOG_ROWS = 8


def cache_attention(live, every_query, cached_keys, cached_values):
    sources, span_rows, width = every_query.shape
    kv_heads = cached_keys.shape[1] // HD
    per_head = sources // kv_heads
    rows = cached_keys.shape[0]
    grid_spec = pltpu.PrefetchScalarGridSpec(
        num_scalar_prefetch=1,
        grid=(kv_heads,),
        in_specs=[
            pl.BlockSpec((per_head, span_rows, width), lambda g, live: (g, 0, 0)),
            pl.BlockSpec((rows, HD), lambda g, live: (0, g)),
            pl.BlockSpec((rows, HD), lambda g, live: (0, g)),
        ],
        out_specs=pl.BlockSpec((per_head, span_rows + LOG_ROWS, width), lambda g, live: (g, 0, 0)),
    )
    return pl.pallas_call(
        cache_kernel,
        grid_spec=grid_spec,
        out_shape=jax.ShapeDtypeStruct((sources, span_rows + LOG_ROWS, width), jnp.bfloat16),
    )(live, every_query, cached_keys, cached_values)


def combine_kernel(*refs):
    parts_refs = refs[:-5]
    own_out_ref, own_log_ref, weight_ref, out_ref, attended_ref = refs[-5:]

    @pl.when(pl.program_id(0) == 0)
    def _():
        rows = own_out_ref.shape[0] // len(parts_refs)
        for i, parts_ref in enumerate(parts_refs):
            combine_into(
                parts_ref,
                own_out_ref.at[pl.ds(i * rows, rows), :],
                own_log_ref.at[:, pl.ds(i * rows, rows)],
                attended_ref.at[pl.ds(i * rows, rows), :],
            )

    out_ref[...] = jnp.dot(
        attended_ref[...], weight_ref[...], preferred_element_type=jnp.float32
    ).astype(out_ref.dtype)


def combine_into(parts_ref, own_out_ref, own_log_ref, out_ref):
    sources = parts_ref.shape[0]
    rows = out_ref.shape[0]
    heads_here = out_ref.shape[1] // HD
    logs = [[] for _ in range(heads_here)]
    for b in range(sources):
        packed = parts_ref[b, rows:rows + LOG_ROWS, :rows].astype(jnp.float32)
        for h in range(heads_here):
            logs[h].append((packed[3 * h + 2:3 * h + 3] + packed[3 * h + 1:3 * h + 2]) + packed[3 * h:3 * h + 1])
    own_logs = own_log_ref[...]
    table_rows = []
    for h in range(heads_here):
        own_log = own_logs[h:h + 1]
        ceiling = own_log
        for lg in logs[h]:
            ceiling = jnp.maximum(ceiling, lg)
        own_factor = jnp.exp(own_log - ceiling)
        factors = [jnp.exp(lg - ceiling) for lg in logs[h]]
        total = own_factor
        for factor in factors:
            total = total + factor
        table_rows += [own_factor] + factors + [total]
    size = 128 * pl.cdiv(len(table_rows), 128)
    which = lax.broadcasted_iota(jnp.int32, (size, rows), 0)
    table = jnp.zeros((size, rows), jnp.float32)
    for j, row in enumerate(table_rows):
        table = jnp.where(which == j, jnp.broadcast_to(row, (size, rows)), table)
    columns = jnp.transpose(table)
    for h in range(heads_here):
        base = h * (sources + 2)
        weighted = columns[:, base:base + 1] * own_out_ref[:, h * HD:(h + 1) * HD].astype(jnp.float32)
        for b in range(sources):
            weighted = weighted + columns[:, base + 1 + b:base + 2 + b] * parts_ref[
                b, :rows, h * HD:(h + 1) * HD
            ].astype(jnp.float32)
        total = columns[:, base + sources + 1:base + sources + 2]
        out_ref[:, h * HD:(h + 1) * HD] = (weighted / total).astype(out_ref.dtype)


COLUMN_BLOCK = 1024


def combine(arrived_halves, own_out, own_log, out_weight):
    sources, packed_rows, width = arrived_halves[0].shape
    rows = own_out.shape[0]
    columns = out_weight.shape[1]
    return pl.pallas_call(
        combine_kernel,
        grid=(columns // COLUMN_BLOCK,),
        in_specs=[pl.BlockSpec((sources, packed_rows, width), lambda j: (0, 0, 0)) for _ in arrived_halves]
        + [
            pl.BlockSpec(own_out.shape, lambda j: (0, 0)),
            pl.BlockSpec(own_log.shape, lambda j: (0, 0)),
            pl.BlockSpec((out_weight.shape[0], COLUMN_BLOCK), lambda j: (0, j)),
        ],
        out_specs=pl.BlockSpec((rows, COLUMN_BLOCK), lambda j: (0, j)),
        out_shape=jax.ShapeDtypeStruct((rows, columns), jnp.bfloat16),
        scratch_shapes=[pltpu.VMEM(own_out.shape, jnp.bfloat16)],
        compiler_params=pltpu.CompilerParams(dimension_semantics=("arbitrary",)),
    )(*arrived_halves, own_out, own_log, out_weight)


def residual_kernel(position_ref, terms_ref, current_ref, out_ref):
    total = terms_ref[0].astype(jnp.float32)
    for n in range(1, terms_ref.shape[0]):
        total = total + terms_ref[n].astype(jnp.float32)
    mixed = (current_ref[...].astype(jnp.float32) + total).astype(out_ref.dtype)
    for n in range(out_ref.shape[0]):
        out_ref[n] = mixed


def residual(position, gathered_terms, current):
    sources, chunk, width = gathered_terms.shape
    grid_spec = pltpu.PrefetchScalarGridSpec(
        num_scalar_prefetch=1,
        grid=(1,),
        in_specs=[
            pl.BlockSpec((sources, chunk, width), lambda i, pos: (0, 0, 0)),
            pl.BlockSpec((chunk, width), lambda i, pos: (pos[0], 0)),
        ],
        out_specs=pl.BlockSpec((sources, chunk, width), lambda i, pos: (0, 0, 0)),
    )
    return pl.pallas_call(
        residual_kernel,
        grid_spec=grid_spec,
        out_shape=jax.ShapeDtypeStruct((sources, chunk, width), jnp.bfloat16),
    )(position, gathered_terms, current)


def shards(
    fresh,
    previous,
    span_index,
    cache_counts,
    norm_gain,
    w_query,
    w_keyval,
    w_out,
    cache_keys,
    cache_values,
):
    blocks = lax.axis_size("blk")
    position = lax.axis_index("blk")
    span_rows = fresh.shape[0]
    first_span = span_index[0]
    heads_here = w_query.shape[2] // HD
    odd_member = position % 2 == 1
    live = cache_counts[0, position].reshape(1)
    arrived = passed_along(previous[0], "segment", 1)
    partner_weight = swapped(w_keyval[0], "blk", 0)
    key_weight = jnp.where(odd_member, partner_weight, w_keyval[0])
    value_weight = jnp.where(odd_member, w_keyval[0], partner_weight)
    current = jnp.where(lax.axis_index("segment") == 0, fresh, arrived)
    widened = current.astype(jnp.float32)
    normed = (
        widened
        * lax.rsqrt(jnp.mean(widened * widened, axis=-1, keepdims=True) + EPSILON)
        * norm_gain[0]
    ).astype(jnp.bfloat16)
    key_weight, value_weight, normed = lax.optimization_barrier((key_weight, value_weight, normed))
    queries = jnp.dot(normed, w_query[0], preferred_element_type=jnp.float32).reshape(
        span_rows, heads_here, HD
    )
    queries = rotate(queries, first_span).astype(jnp.bfloat16).reshape(span_rows, heads_here * HD)
    key_projected = jnp.dot(normed, key_weight, preferred_element_type=jnp.float32)
    own_keys = rotate(key_projected[:, None, :], first_span)[:, 0, :].astype(jnp.bfloat16)
    own_values = jnp.dot(normed, value_weight, preferred_element_type=jnp.float32).astype(jnp.bfloat16)
    halves = 2
    half_rows = span_rows // halves
    arrived_halves = []
    for i in range(halves):
        half = queries[i * half_rows:(i + 1) * half_rows]
        every_query = lax.all_to_all(
            jnp.broadcast_to(half[None], (blocks,) + half.shape), "blk", 0, 0, tiled=True
        )
        held = cache_attention(live, every_query, cache_keys[0], cache_values[0])
        arrived_halves.append(lax.all_to_all(held, "blk", split_axis=0, concat_axis=0, tiled=True))
    query_rows = queries.reshape(span_rows * heads_here, HD)
    row_tokens = jnp.arange(span_rows * heads_here, dtype=jnp.int32) // heads_here
    causal = row_tokens[:, None] >= jnp.arange(span_rows, dtype=jnp.int32)[None, :]
    own_out, own_log = attend_rows(query_rows, own_keys, own_values, causal)
    own_out = own_out.reshape(span_rows, heads_here * HD)
    own_log = own_log.reshape(span_rows, heads_here).T
    head_terms = combine(arrived_halves, own_out, own_log, w_out[0])
    chunk = span_rows // blocks
    gathered_terms = lax.all_to_all(
        head_terms.reshape(blocks, chunk, -1), "blk", 0, 0, tiled=True
    )
    spread = residual(position.reshape(1), gathered_terms, current)
    mixed = lax.all_to_all(spread, "blk", 0, 0, tiled=True).reshape(span_rows, -1)
    return mixed[None]


def solution(mesh):
    placed = (
        P(),
        P("segment", None, None),
        P("segment"),
        P("segment", None),
        P("segment", None),
        P("segment", None, "blk"),
        P("segment", None, "blk"),
        P("segment", "blk", None),
        P("segment", "blk", None),
        P("segment", "blk", None),
    )
    return jax.shard_map(
        shards, mesh=mesh, in_specs=placed, out_specs=P("segment", None, None), check_vma=False
    )
```

```python
import jax
import jax.numpy as jnp
from jax import lax
from jax.sharding import PartitionSpec as P
from jax.experimental import pallas as pl
from jax.experimental.pallas import tpu as pltpu

KVH = 8
HD = 128


ROPE_BASE = 500000.0
EPSILON = 1e-05


def passed_along(block, axis, distance):
    devices = range(lax.axis_size(axis))
    route = [(i - distance, i) for i in devices if i - distance in devices]
    return lax.ppermute(block, axis, route)


def swapped(block, axis, distance):
    count = lax.axis_size(axis)
    route = []
    for low in range(count):
        high = low | 1 << distance
        if high != low and high < count:
            route += [(low, high), (high, low)]
    return lax.ppermute(block, axis, route)


def rotate(projected, first_span):
    length = projected.shape[0]
    half_width = projected.shape[-1] // 2
    positions = (first_span * length + jnp.arange(length, dtype=jnp.int32)).astype(jnp.float32)
    inverse = ROPE_BASE ** (
        -(jnp.arange(half_width, dtype=jnp.float32) * 2.0) / projected.shape[-1]
    )
    angles = positions[:, None] * inverse[None, :]
    cosine = jnp.cos(angles)[:, None, :]
    sine_table = jnp.sin(angles)[:, None, :]
    left_part = projected[..., :half_width]
    right_part = projected[..., half_width:]
    return jnp.concatenate(
        [
            left_part * cosine - right_part * sine_table,
            right_part * cosine + left_part * sine_table,
        ],
        axis=-1,
    )


def attend_rows(query_rows, key_rows, value_rows, allowed):
    scores = lax.dot_general(
        query_rows, key_rows, (((1,), (1,)), ((), ())), preferred_element_type=jnp.float32
    ) * query_rows.shape[-1] ** (-0.5)
    scores = jnp.where(allowed, scores, -jnp.inf)
    highest = jnp.max(scores, axis=-1, keepdims=True)
    weights = jnp.exp(scores - highest)
    totals = jnp.sum(weights, axis=-1, keepdims=True)
    partial_out = (
        jnp.dot(weights.astype(jnp.bfloat16), value_rows, preferred_element_type=jnp.float32)
        / totals
    ).astype(jnp.bfloat16)
    return (partial_out, (highest + jnp.log(totals))[:, 0])


def cache_kernel(live_ref, q_ref, k_ref, v_ref, out_ref):
    live = live_ref[0]
    keys = k_ref[...]
    values = v_ref[...]
    sources, rows = q_ref.shape[0], q_ref.shape[1]
    width = out_ref.shape[2]
    group = max(1, min(sources, 256 // rows))
    visible = lax.broadcasted_iota(jnp.int32, (1, keys.shape[0]), 1) < live
    log_rows = {src: [] for src in range(sources)}
    for first in range(0, sources, group):
        members = list(range(first, min(first + group, sources)))
        for h in range(q_ref.shape[2] // HD):
            q = jnp.concatenate([q_ref[src, :, h * HD:(h + 1) * HD] for src in members], axis=0)
            scores = lax.dot_general(
                q, keys, (((1,), (1,)), ((), ())), preferred_element_type=jnp.float32
            ) * HD ** (-0.5)
            scores = jnp.where(visible, scores, -jnp.inf)
            highest = jnp.max(scores, axis=-1, keepdims=True)
            weights = jnp.exp(scores - highest)
            totals = jnp.sum(weights, axis=-1, keepdims=True)
            part = jnp.dot(weights.astype(jnp.bfloat16), values, preferred_element_type=jnp.float32)
            normalized = (part / totals).astype(out_ref.dtype)
            log_totals = highest + jnp.log(totals)
            for i, src in enumerate(members):
                out_ref[src, :rows, h * HD:(h + 1) * HD] = normalized[i * rows:(i + 1) * rows]
                log_col = jnp.broadcast_to(log_totals[i * rows:(i + 1) * rows], (rows, HD))
                rest = jnp.transpose(log_col)[0:1, :]
                for _ in range(3):
                    piece = rest.astype(jnp.bfloat16).astype(jnp.float32)
                    log_rows[src].append(piece)
                    rest = rest - piece
    for src in range(sources):
        rows_here = log_rows[src]
        if rows < width:
            rows_here = [jnp.concatenate([r, jnp.zeros((1, width - rows), jnp.float32)], axis=1) for r in rows_here]
        rows_here = rows_here + [jnp.zeros((1, width), jnp.float32)] * (out_ref.shape[1] - rows - len(rows_here))
        out_ref[src, rows:, :] = jnp.concatenate(rows_here, axis=0).astype(out_ref.dtype)


LOG_ROWS = 8


def cache_attention(live, every_query, cached_keys, cached_values):
    sources, span_rows, width = every_query.shape
    kv_heads = cached_keys.shape[1] // HD
    per_head = sources // kv_heads
    rows = cached_keys.shape[0]
    grid_spec = pltpu.PrefetchScalarGridSpec(
        num_scalar_prefetch=1,
        grid=(kv_heads,),
        in_specs=[
            pl.BlockSpec((per_head, span_rows, width), lambda g, live: (g, 0, 0)),
            pl.BlockSpec((rows, HD), lambda g, live: (0, g)),
            pl.BlockSpec((rows, HD), lambda g, live: (0, g)),
        ],
        out_specs=pl.BlockSpec((per_head, span_rows + LOG_ROWS, width), lambda g, live: (g, 0, 0)),
    )
    return pl.pallas_call(
        cache_kernel,
        grid_spec=grid_spec,
        out_shape=jax.ShapeDtypeStruct((sources, span_rows + LOG_ROWS, width), jnp.bfloat16),
    )(live, every_query, cached_keys, cached_values)


def combine_kernel(*refs):
    parts_refs = refs[:-5]
    own_out_ref, own_log_ref, weight_ref, out_ref, attended_ref = refs[-5:]

    @pl.when(pl.program_id(0) == 0)
    def _():
        rows = own_out_ref.shape[0] // len(parts_refs)
        for i, parts_ref in enumerate(parts_refs):
            combine_into(
                parts_ref,
                own_out_ref.at[pl.ds(i * rows, rows), :],
                own_log_ref.at[:, pl.ds(i * rows, rows)],
                attended_ref.at[pl.ds(i * rows, rows), :],
            )

    out_ref[...] = jnp.dot(
        attended_ref[...], weight_ref[...], preferred_element_type=jnp.float32
    ).astype(out_ref.dtype)


def combine_into(parts_ref, own_out_ref, own_log_ref, out_ref):
    sources = parts_ref.shape[0]
    rows = out_ref.shape[0]
    heads_here = out_ref.shape[1] // HD
    logs = [[] for _ in range(heads_here)]
    for b in range(sources):
        packed = parts_ref[b, rows:rows + LOG_ROWS, :rows].astype(jnp.float32)
        for h in range(heads_here):
            logs[h].append((packed[3 * h + 2:3 * h + 3] + packed[3 * h + 1:3 * h + 2]) + packed[3 * h:3 * h + 1])
    own_logs = own_log_ref[...]
    table_rows = []
    for h in range(heads_here):
        own_log = own_logs[h:h + 1]
        ceiling = own_log
        for lg in logs[h]:
            ceiling = jnp.maximum(ceiling, lg)
        own_factor = jnp.exp(own_log - ceiling)
        factors = [jnp.exp(lg - ceiling) for lg in logs[h]]
        total = own_factor
        for factor in factors:
            total = total + factor
        table_rows += [own_factor] + factors + [total]
    size = 128 * pl.cdiv(len(table_rows), 128)
    which = lax.broadcasted_iota(jnp.int32, (size, rows), 0)
    table = jnp.zeros((size, rows), jnp.float32)
    for j, row in enumerate(table_rows):
        table = jnp.where(which == j, jnp.broadcast_to(row, (size, rows)), table)
    columns = jnp.transpose(table)
    for h in range(heads_here):
        base = h * (sources + 2)
        weighted = columns[:, base:base + 1] * own_out_ref[:, h * HD:(h + 1) * HD].astype(jnp.float32)
        for b in range(sources):
            weighted = weighted + columns[:, base + 1 + b:base + 2 + b] * parts_ref[
                b, :rows, h * HD:(h + 1) * HD
            ].astype(jnp.float32)
        total = columns[:, base + sources + 1:base + sources + 2]
        out_ref[:, h * HD:(h + 1) * HD] = (weighted / total).astype(out_ref.dtype)


COLUMN_BLOCK = 1024


def combine(arrived_halves, own_out, own_log, out_weight):
    sources, packed_rows, width = arrived_halves[0].shape
    rows = own_out.shape[0]
    columns = out_weight.shape[1]
    return pl.pallas_call(
        combine_kernel,
        grid=(columns // COLUMN_BLOCK,),
        in_specs=[pl.BlockSpec((sources, packed_rows, width), lambda j: (0, 0, 0)) for _ in arrived_halves]
        + [
            pl.BlockSpec(own_out.shape, lambda j: (0, 0)),
            pl.BlockSpec(own_log.shape, lambda j: (0, 0)),
            pl.BlockSpec((out_weight.shape[0], COLUMN_BLOCK), lambda j: (0, j)),
        ],
        out_specs=pl.BlockSpec((rows, COLUMN_BLOCK), lambda j: (0, j)),
        out_shape=jax.ShapeDtypeStruct((rows, columns), jnp.bfloat16),
        scratch_shapes=[pltpu.VMEM(own_out.shape, jnp.bfloat16)],
        compiler_params=pltpu.CompilerParams(dimension_semantics=("arbitrary",)),
    )(*arrived_halves, own_out, own_log, out_weight)


def residual_kernel(position_ref, terms_ref, current_ref, out_ref, mixed_ref):
    @pl.when(pl.program_id(0) == 0)
    def _():
        total = terms_ref[0].astype(jnp.float32)
        for n in range(1, terms_ref.shape[0]):
            total = total + terms_ref[n].astype(jnp.float32)
        mixed_ref[...] = (current_ref[...].astype(jnp.float32) + total).astype(mixed_ref.dtype)

    out_ref[0] = mixed_ref[...]


def residual(position, gathered_terms, current):
    sources, chunk, width = gathered_terms.shape
    grid_spec = pltpu.PrefetchScalarGridSpec(
        num_scalar_prefetch=1,
        grid=(sources,),
        in_specs=[
            pl.BlockSpec((sources, chunk, width), lambda i, pos: (0, 0, 0)),
            pl.BlockSpec((chunk, width), lambda i, pos: (pos[0], 0)),
        ],
        out_specs=pl.BlockSpec((1, chunk, width), lambda i, pos: (i, 0, 0)),
        scratch_shapes=[pltpu.VMEM((chunk, width), jnp.bfloat16)],
    )
    return pl.pallas_call(
        residual_kernel,
        grid_spec=grid_spec,
        out_shape=jax.ShapeDtypeStruct((sources, chunk, width), jnp.bfloat16),
        compiler_params=pltpu.CompilerParams(dimension_semantics=("arbitrary",)),
    )(position, gathered_terms, current)

def shards(
    fresh,
    previous,
    span_index,
    cache_counts,
    norm_gain,
    w_query,
    w_keyval,
    w_out,
    cache_keys,
    cache_values,
):
    blocks = lax.axis_size("blk")
    position = lax.axis_index("blk")
    span_rows = fresh.shape[0]
    first_span = span_index[0]
    heads_here = w_query.shape[2] // HD
    odd_member = position % 2 == 1
    live = cache_counts[0, position].reshape(1)
    arrived = passed_along(previous[0], "segment", 1)
    current = jnp.where(lax.axis_index("segment") == 0, fresh, arrived)
    widened = current.astype(jnp.float32)
    normed = (
        widened
        * lax.rsqrt(jnp.mean(widened * widened, axis=-1, keepdims=True) + EPSILON)
        * norm_gain[0]
    ).astype(jnp.bfloat16)
    queries = jnp.dot(normed, w_query[0], preferred_element_type=jnp.float32).reshape(
        span_rows, heads_here, HD
    )
    queries = rotate(queries, first_span).astype(jnp.bfloat16).reshape(span_rows, heads_here * HD)
    projected = jnp.dot(normed, w_keyval[0], preferred_element_type=jnp.float32)
    as_key = rotate(projected[:, None, :], first_span)[:, 0, :].astype(jnp.bfloat16)
    mine = jnp.where(odd_member, projected.astype(jnp.bfloat16), as_key)
    partner = swapped(mine, "blk", 0)
    own_keys = jnp.where(odd_member, partner, mine)
    own_values = jnp.where(odd_member, mine, partner)
    partner, queries = lax.optimization_barrier((partner, queries))
    halves = 2
    half_rows = span_rows // halves
    arrived_halves = []
    for i in range(halves):
        half = queries[i * half_rows:(i + 1) * half_rows]
        every_query = lax.all_to_all(
            jnp.broadcast_to(half[None], (blocks,) + half.shape), "blk", 0, 0, tiled=True
        )
        held = cache_attention(live, every_query, cache_keys[0], cache_values[0])
        arrived_halves.append(lax.all_to_all(held, "blk", split_axis=0, concat_axis=0, tiled=True))
    query_rows = queries.reshape(span_rows * heads_here, HD)
    row_tokens = jnp.arange(span_rows * heads_here, dtype=jnp.int32) // heads_here
    causal = row_tokens[:, None] >= jnp.arange(span_rows, dtype=jnp.int32)[None, :]
    own_out, own_log = attend_rows(query_rows, own_keys, own_values, causal)
    own_out = own_out.reshape(span_rows, heads_here * HD)
    own_log = own_log.reshape(span_rows, heads_here).T
    head_terms = combine(arrived_halves, own_out, own_log, w_out[0])
    chunk = span_rows // blocks
    gathered_terms = lax.all_to_all(
        head_terms.reshape(blocks, chunk, -1), "blk", 0, 0, tiled=True
    )
    spread = residual(position.reshape(1), gathered_terms, current)
    mixed = lax.all_to_all(spread, "blk", 0, 0, tiled=True).reshape(span_rows, -1)
    return mixed[None]


def solution(mesh):
    placed = (
        P(),
        P("segment", None, None),
        P("segment"),
        P("segment", None),
        P("segment", None),
        P("segment", None, "blk"),
        P("segment", None, "blk"),
        P("segment", "blk", None),
        P("segment", "blk", None),
        P("segment", "blk", None),
    )
    return jax.shard_map(
        shards, mesh=mesh, in_specs=placed, out_specs=P("segment", None, None), check_vma=False
    )
```

```python
import jax
import jax.numpy as jnp
from jax import lax
from jax.sharding import PartitionSpec as P
from jax.experimental import pallas as pl
from jax.experimental.pallas import tpu as pltpu

KVH = 8
HD = 128


ROPE_BASE = 500000.0
EPSILON = 1e-05


def passed_along(block, axis, distance):
    devices = range(lax.axis_size(axis))
    route = [(i - distance, i) for i in devices if i - distance in devices]
    return lax.ppermute(block, axis, route)


def swapped(block, axis, distance):
    count = lax.axis_size(axis)
    route = []
    for low in range(count):
        high = low | 1 << distance
        if high != low and high < count:
            route += [(low, high), (high, low)]
    return lax.ppermute(block, axis, route)


def rotate(projected, first_span):
    length = projected.shape[0]
    half_width = projected.shape[-1] // 2
    positions = (first_span * length + jnp.arange(length, dtype=jnp.int32)).astype(jnp.float32)
    inverse = ROPE_BASE ** (
        -(jnp.arange(half_width, dtype=jnp.float32) * 2.0) / projected.shape[-1]
    )
    angles = positions[:, None] * inverse[None, :]
    cosine = jnp.cos(angles)[:, None, :]
    sine_table = jnp.sin(angles)[:, None, :]
    left_part = projected[..., :half_width]
    right_part = projected[..., half_width:]
    return jnp.concatenate(
        [
            left_part * cosine - right_part * sine_table,
            right_part * cosine + left_part * sine_table,
        ],
        axis=-1,
    )


def attend_rows(query_rows, key_rows, value_rows, allowed):
    scores = lax.dot_general(
        query_rows, key_rows, (((1,), (1,)), ((), ())), preferred_element_type=jnp.float32
    ) * query_rows.shape[-1] ** (-0.5)
    scores = jnp.where(allowed, scores, -jnp.inf)
    highest = jnp.max(scores, axis=-1, keepdims=True)
    weights = jnp.exp(scores - highest)
    totals = jnp.sum(weights, axis=-1, keepdims=True)
    partial_out = (
        jnp.dot(weights.astype(jnp.bfloat16), value_rows, preferred_element_type=jnp.float32)
        / totals
    ).astype(jnp.bfloat16)
    return (partial_out, (highest + jnp.log(totals))[:, 0])


def cache_kernel(live_ref, q_ref, k_ref, v_ref, out_ref):
    live = live_ref[0]
    keys = k_ref[...]
    values = v_ref[...]
    sources, rows = q_ref.shape[0], q_ref.shape[1]
    width = out_ref.shape[2]
    group = max(1, min(sources, 256 // rows))
    visible = lax.broadcasted_iota(jnp.int32, (1, keys.shape[0]), 1) < live
    bias = jnp.where(visible, 0.0, -jnp.inf).astype(jnp.float32)
    log_rows = {src: [] for src in range(sources)}
    for first in range(0, sources, group):
        members = list(range(first, min(first + group, sources)))
        for h in range(q_ref.shape[2] // HD):
            q = jnp.concatenate([q_ref[src, :, h * HD:(h + 1) * HD] for src in members], axis=0)
            scores = lax.dot_general(
                q, keys, (((1,), (1,)), ((), ())), preferred_element_type=jnp.float32
            ) * HD ** (-0.5) + bias
            highest = jnp.max(scores, axis=-1, keepdims=True)
            weights = jnp.exp(scores - highest)
            totals = jnp.sum(weights, axis=-1, keepdims=True)
            part = jnp.dot(weights.astype(jnp.bfloat16), values, preferred_element_type=jnp.float32)
            normalized = (part / totals).astype(out_ref.dtype)
            log_totals = highest + jnp.log(totals)
            for i, src in enumerate(members):
                out_ref[src, :rows, h * HD:(h + 1) * HD] = normalized[i * rows:(i + 1) * rows]
                log_col = jnp.broadcast_to(log_totals[i * rows:(i + 1) * rows], (rows, HD))
                rest = jnp.transpose(log_col)[0:1, :]
                for _ in range(3):
                    piece = rest.astype(jnp.bfloat16).astype(jnp.float32)
                    log_rows[src].append(piece)
                    rest = rest - piece
    for src in range(sources):
        rows_here = log_rows[src]
        if rows < width:
            rows_here = [jnp.concatenate([r, jnp.zeros((1, width - rows), jnp.float32)], axis=1) for r in rows_here]
        rows_here = rows_here + [jnp.zeros((1, width), jnp.float32)] * (out_ref.shape[1] - rows - len(rows_here))
        out_ref[src, rows:, :] = jnp.concatenate(rows_here, axis=0).astype(out_ref.dtype)


LOG_ROWS = 8


def cache_attention(live, every_query, cached_keys, cached_values):
    sources, span_rows, width = every_query.shape
    kv_heads = cached_keys.shape[1] // HD
    per_head = sources // kv_heads
    rows = cached_keys.shape[0]
    grid_spec = pltpu.PrefetchScalarGridSpec(
        num_scalar_prefetch=1,
        grid=(kv_heads,),
        in_specs=[
            pl.BlockSpec((per_head, span_rows, width), lambda g, live: (g, 0, 0)),
            pl.BlockSpec((rows, HD), lambda g, live: (0, g)),
            pl.BlockSpec((rows, HD), lambda g, live: (0, g)),
        ],
        out_specs=pl.BlockSpec((per_head, span_rows + LOG_ROWS, width), lambda g, live: (g, 0, 0)),
    )
    return pl.pallas_call(
        cache_kernel,
        grid_spec=grid_spec,
        out_shape=jax.ShapeDtypeStruct((sources, span_rows + LOG_ROWS, width), jnp.bfloat16),
    )(live, every_query, cached_keys, cached_values)


def combine_kernel(*refs):
    parts_refs = refs[:-5]
    own_out_ref, own_log_ref, weight_ref, out_ref, attended_ref = refs[-5:]

    @pl.when(pl.program_id(0) == 0)
    def _():
        rows = own_out_ref.shape[0] // len(parts_refs)
        for i, parts_ref in enumerate(parts_refs):
            combine_into(
                parts_ref,
                own_out_ref.at[pl.ds(i * rows, rows), :],
                own_log_ref.at[:, pl.ds(i * rows, rows)],
                attended_ref.at[pl.ds(i * rows, rows), :],
            )

    out_ref[...] = jnp.dot(
        attended_ref[...], weight_ref[...], preferred_element_type=jnp.float32
    ).astype(out_ref.dtype)


def combine_into(parts_ref, own_out_ref, own_log_ref, out_ref):
    sources = parts_ref.shape[0]
    rows = out_ref.shape[0]
    heads_here = out_ref.shape[1] // HD
    logs = [[] for _ in range(heads_here)]
    for b in range(sources):
        packed = parts_ref[b, rows:rows + LOG_ROWS, :rows].astype(jnp.float32)
        for h in range(heads_here):
            logs[h].append((packed[3 * h + 2:3 * h + 3] + packed[3 * h + 1:3 * h + 2]) + packed[3 * h:3 * h + 1])
    own_logs = own_log_ref[...]
    table_rows = []
    for h in range(heads_here):
        own_log = own_logs[h:h + 1]
        ceiling = own_log
        for lg in logs[h]:
            ceiling = jnp.maximum(ceiling, lg)
        own_factor = jnp.exp(own_log - ceiling)
        factors = [jnp.exp(lg - ceiling) for lg in logs[h]]
        total = own_factor
        for factor in factors:
            total = total + factor
        table_rows += [own_factor] + factors + [total]
    size = 128 * pl.cdiv(len(table_rows), 128)
    which = lax.broadcasted_iota(jnp.int32, (size, rows), 0)
    table = jnp.zeros((size, rows), jnp.float32)
    for j, row in enumerate(table_rows):
        table = jnp.where(which == j, jnp.broadcast_to(row, (size, rows)), table)
    columns = jnp.transpose(table)
    for h in range(heads_here):
        base = h * (sources + 2)
        weighted = columns[:, base:base + 1] * own_out_ref[:, h * HD:(h + 1) * HD].astype(jnp.float32)
        for b in range(sources):
            weighted = weighted + columns[:, base + 1 + b:base + 2 + b] * parts_ref[
                b, :rows, h * HD:(h + 1) * HD
            ].astype(jnp.float32)
        total = columns[:, base + sources + 1:base + sources + 2]
        out_ref[:, h * HD:(h + 1) * HD] = (weighted / total).astype(out_ref.dtype)


COLUMN_BLOCK = 1024


def combine(arrived_halves, own_out, own_log, out_weight):
    sources, packed_rows, width = arrived_halves[0].shape
    rows = own_out.shape[0]
    columns = out_weight.shape[1]
    return pl.pallas_call(
        combine_kernel,
        grid=(columns // COLUMN_BLOCK,),
        in_specs=[pl.BlockSpec((sources, packed_rows, width), lambda j: (0, 0, 0)) for _ in arrived_halves]
        + [
            pl.BlockSpec(own_out.shape, lambda j: (0, 0)),
            pl.BlockSpec(own_log.shape, lambda j: (0, 0)),
            pl.BlockSpec((out_weight.shape[0], COLUMN_BLOCK), lambda j: (0, j)),
        ],
        out_specs=pl.BlockSpec((rows, COLUMN_BLOCK), lambda j: (0, j)),
        out_shape=jax.ShapeDtypeStruct((rows, columns), jnp.bfloat16),
        scratch_shapes=[pltpu.VMEM(own_out.shape, jnp.bfloat16)],
        compiler_params=pltpu.CompilerParams(dimension_semantics=("arbitrary",)),
    )(*arrived_halves, own_out, own_log, out_weight)


def residual_kernel(position_ref, terms_ref, current_ref, out_ref):
    total = terms_ref[0].astype(jnp.float32)
    for n in range(1, terms_ref.shape[0]):
        total = total + terms_ref[n].astype(jnp.float32)
    mixed = (current_ref[...].astype(jnp.float32) + total).astype(out_ref.dtype)
    for n in range(out_ref.shape[0]):
        out_ref[n] = mixed


def residual(position, gathered_terms, current):
    sources, chunk, width = gathered_terms.shape
    grid_spec = pltpu.PrefetchScalarGridSpec(
        num_scalar_prefetch=1,
        grid=(1,),
        in_specs=[
            pl.BlockSpec((sources, chunk, width), lambda i, pos: (0, 0, 0)),
            pl.BlockSpec((chunk, width), lambda i, pos: (pos[0], 0)),
        ],
        out_specs=pl.BlockSpec((sources, chunk, width), lambda i, pos: (0, 0, 0)),
    )
    return pl.pallas_call(
        residual_kernel,
        grid_spec=grid_spec,
        out_shape=jax.ShapeDtypeStruct((sources, chunk, width), jnp.bfloat16),
    )(position, gathered_terms, current)


def shards(
    fresh,
    previous,
    span_index,
    cache_counts,
    norm_gain,
    w_query,
    w_keyval,
    w_out,
    cache_keys,
    cache_values,
):
    blocks = lax.axis_size("blk")
    position = lax.axis_index("blk")
    span_rows = fresh.shape[0]
    first_span = span_index[0]
    heads_here = w_query.shape[2] // HD
    odd_member = position % 2 == 1
    live = cache_counts[0, position].reshape(1)
    arrived = passed_along(previous[0], "segment", 1)
    current = jnp.where(lax.axis_index("segment") == 0, fresh, arrived)
    widened = current.astype(jnp.float32)
    normed = (
        widened
        * lax.rsqrt(jnp.mean(widened * widened, axis=-1, keepdims=True) + EPSILON)
        * norm_gain[0]
    ).astype(jnp.bfloat16)
    queries = jnp.dot(normed, w_query[0], preferred_element_type=jnp.float32).reshape(
        span_rows, heads_here, HD
    )
    queries = rotate(queries, first_span).astype(jnp.bfloat16).reshape(span_rows, heads_here * HD)
    projected = jnp.dot(normed, w_keyval[0], preferred_element_type=jnp.float32)
    as_key = rotate(projected[:, None, :], first_span)[:, 0, :].astype(jnp.bfloat16)
    mine = jnp.where(odd_member, projected.astype(jnp.bfloat16), as_key)
    partner = swapped(mine, "blk", 0)
    own_keys = jnp.where(odd_member, partner, mine)
    own_values = jnp.where(odd_member, mine, partner)
    partner, queries = lax.optimization_barrier((partner, queries))
    halves = 2
    half_rows = span_rows // halves
    arrived_halves = []
    for i in range(halves):
        half = queries[i * half_rows:(i + 1) * half_rows]
        every_query = lax.all_to_all(
            jnp.broadcast_to(half[None], (blocks,) + half.shape), "blk", 0, 0, tiled=True
        )
        held = cache_attention(live, every_query, cache_keys[0], cache_values[0])
        arrived_halves.append(lax.all_to_all(held, "blk", split_axis=0, concat_axis=0, tiled=True))
    query_rows = queries.reshape(span_rows * heads_here, HD)
    row_tokens = jnp.arange(span_rows * heads_here, dtype=jnp.int32) // heads_here
    causal = row_tokens[:, None] >= jnp.arange(span_rows, dtype=jnp.int32)[None, :]
    own_out, own_log = attend_rows(query_rows, own_keys, own_values, causal)
    own_out = own_out.reshape(span_rows, heads_here * HD)
    own_log = own_log.reshape(span_rows, heads_here).T
    head_terms = combine(arrived_halves, own_out, own_log, w_out[0])
    chunk = span_rows // blocks
    gathered_terms = lax.all_to_all(
        head_terms.reshape(blocks, chunk, -1), "blk", 0, 0, tiled=True
    )
    spread = residual(position.reshape(1), gathered_terms, current)
    mixed = lax.all_to_all(spread, "blk", 0, 0, tiled=True).reshape(span_rows, -1)
    return mixed[None]


def solution(mesh):
    placed = (
        P(),
        P("segment", None, None),
        P("segment"),
        P("segment", None),
        P("segment", None),
        P("segment", None, "blk"),
        P("segment", None, "blk"),
        P("segment", "blk", None),
        P("segment", "blk", None),
        P("segment", "blk", None),
    )
    return jax.shard_map(
        shards, mesh=mesh, in_specs=placed, out_specs=P("segment", None, None), check_vma=False
    )
```

```python
import jax
import jax.numpy as jnp
from jax import lax
from jax.sharding import PartitionSpec as P
from jax.experimental import pallas as pl
from jax.experimental.pallas import tpu as pltpu

KVH = 8
HD = 128


ROPE_BASE = 500000.0
EPSILON = 1e-05


def passed_along(block, axis, distance):
    devices = range(lax.axis_size(axis))
    route = [(i - distance, i) for i in devices if i - distance in devices]
    return lax.ppermute(block, axis, route)


def swapped(block, axis, distance):
    count = lax.axis_size(axis)
    route = []
    for low in range(count):
        high = low | 1 << distance
        if high != low and high < count:
            route += [(low, high), (high, low)]
    return lax.ppermute(block, axis, route)


def rotate(projected, first_span):
    length = projected.shape[0]
    half_width = projected.shape[-1] // 2
    positions = (first_span * length + jnp.arange(length, dtype=jnp.int32)).astype(jnp.float32)
    inverse = ROPE_BASE ** (
        -(jnp.arange(half_width, dtype=jnp.float32) * 2.0) / projected.shape[-1]
    )
    angles = positions[:, None] * inverse[None, :]
    cosine = jnp.cos(angles)[:, None, :]
    sine_table = jnp.sin(angles)[:, None, :]
    left_part = projected[..., :half_width]
    right_part = projected[..., half_width:]
    return jnp.concatenate(
        [
            left_part * cosine - right_part * sine_table,
            right_part * cosine + left_part * sine_table,
        ],
        axis=-1,
    )


def attend_rows(query_rows, key_rows, value_rows, allowed):
    scores = lax.dot_general(
        query_rows, key_rows, (((1,), (1,)), ((), ())), preferred_element_type=jnp.float32
    ) * query_rows.shape[-1] ** (-0.5)
    scores = jnp.where(allowed, scores, -jnp.inf)
    highest = jnp.max(scores, axis=-1, keepdims=True)
    weights = jnp.exp(scores - highest)
    totals = jnp.sum(weights, axis=-1, keepdims=True)
    partial_out = (
        jnp.dot(weights.astype(jnp.bfloat16), value_rows, preferred_element_type=jnp.float32)
        / totals
    ).astype(jnp.bfloat16)
    return (partial_out, (highest + jnp.log(totals))[:, 0])


def cache_kernel(live_ref, q_ref, k_ref, v_ref, out_ref):
    live = live_ref[0]
    keys = k_ref[...]
    values = v_ref[...]
    sources, rows = q_ref.shape[0], q_ref.shape[1]
    width = out_ref.shape[2]
    group = max(1, min(sources, 256 // rows))
    visible = lax.broadcasted_iota(jnp.int32, (1, keys.shape[0]), 1) < live
    bias = jnp.where(visible, 0.0, -jnp.inf).astype(jnp.float32)
    log_rows = {src: [] for src in range(sources)}
    for first in range(0, sources, group):
        members = list(range(first, min(first + group, sources)))
        for h in range(q_ref.shape[2] // HD):
            q = jnp.concatenate([q_ref[src, :, h * HD:(h + 1) * HD] for src in members], axis=0)
            scores = lax.dot_general(
                q, keys, (((1,), (1,)), ((), ())), preferred_element_type=jnp.float32
            ) * HD ** (-0.5) + bias
            highest = jnp.max(scores, axis=-1, keepdims=True)
            weights = jnp.exp(scores - highest)
            totals = jnp.sum(weights, axis=-1, keepdims=True)
            part = jnp.dot(weights.astype(jnp.bfloat16), values, preferred_element_type=jnp.float32)
            normalized = (part / totals).astype(out_ref.dtype)
            log_totals = highest + jnp.log(totals)
            for i, src in enumerate(members):
                out_ref[src, :rows, h * HD:(h + 1) * HD] = normalized[i * rows:(i + 1) * rows]
                log_col = jnp.broadcast_to(log_totals[i * rows:(i + 1) * rows], (rows, HD))
                rest = jnp.transpose(log_col)[0:1, :]
                for _ in range(3):
                    piece = rest.astype(jnp.bfloat16).astype(jnp.float32)
                    log_rows[src].append(piece)
                    rest = rest - piece
    for src in range(sources):
        rows_here = log_rows[src]
        if rows < width:
            rows_here = [jnp.concatenate([r, jnp.zeros((1, width - rows), jnp.float32)], axis=1) for r in rows_here]
        rows_here = rows_here + [jnp.zeros((1, width), jnp.float32)] * (out_ref.shape[1] - rows - len(rows_here))
        out_ref[src, rows:, :] = jnp.concatenate(rows_here, axis=0).astype(out_ref.dtype)


LOG_ROWS = 8


def cache_attention(live, every_query, cached_keys, cached_values):
    sources, span_rows, width = every_query.shape
    kv_heads = cached_keys.shape[1] // HD
    per_head = sources // kv_heads
    rows = cached_keys.shape[0]
    grid_spec = pltpu.PrefetchScalarGridSpec(
        num_scalar_prefetch=1,
        grid=(kv_heads,),
        in_specs=[
            pl.BlockSpec((per_head, span_rows, width), lambda g, live: (g, 0, 0)),
            pl.BlockSpec((rows, HD), lambda g, live: (0, g)),
            pl.BlockSpec((rows, HD), lambda g, live: (0, g)),
        ],
        out_specs=pl.BlockSpec((per_head, span_rows + LOG_ROWS, width), lambda g, live: (g, 0, 0)),
    )
    return pl.pallas_call(
        cache_kernel,
        grid_spec=grid_spec,
        out_shape=jax.ShapeDtypeStruct((sources, span_rows + LOG_ROWS, width), jnp.bfloat16),
    )(live, every_query, cached_keys, cached_values)


def combine_kernel(*refs):
    parts_refs = refs[:-5]
    own_out_ref, own_log_ref, weight_ref, out_ref, attended_ref = refs[-5:]

    @pl.when(pl.program_id(0) == 0)
    def _():
        rows = own_out_ref.shape[0] // len(parts_refs)
        for i, parts_ref in enumerate(parts_refs):
            combine_into(
                parts_ref,
                own_out_ref.at[pl.ds(i * rows, rows), :],
                own_log_ref.at[:, pl.ds(i * rows, rows)],
                attended_ref.at[pl.ds(i * rows, rows), :],
            )

    out_ref[...] = jnp.dot(
        attended_ref[...], weight_ref[...], preferred_element_type=jnp.float32
    ).astype(out_ref.dtype)


def combine_into(parts_ref, own_out_ref, own_log_ref, out_ref):
    sources = parts_ref.shape[0]
    rows = out_ref.shape[0]
    heads_here = out_ref.shape[1] // HD
    logs = [[] for _ in range(heads_here)]
    for b in range(sources):
        packed = parts_ref[b, rows:rows + LOG_ROWS, :rows].astype(jnp.float32)
        for h in range(heads_here):
            logs[h].append((packed[3 * h + 2:3 * h + 3] + packed[3 * h + 1:3 * h + 2]) + packed[3 * h:3 * h + 1])
    own_logs = own_log_ref[...]
    table_rows = []
    for h in range(heads_here):
        own_log = own_logs[h:h + 1]
        ceiling = own_log
        for lg in logs[h]:
            ceiling = jnp.maximum(ceiling, lg)
        own_factor = jnp.exp(own_log - ceiling)
        factors = [jnp.exp(lg - ceiling) for lg in logs[h]]
        total = own_factor
        for factor in factors:
            total = total + factor
        table_rows += [own_factor] + factors + [total]
    size = 128 * pl.cdiv(len(table_rows), 128)
    which = lax.broadcasted_iota(jnp.int32, (size, rows), 0)
    table = jnp.zeros((size, rows), jnp.float32)
    for j, row in enumerate(table_rows):
        table = jnp.where(which == j, jnp.broadcast_to(row, (size, rows)), table)
    columns = jnp.transpose(table)
    for h in range(heads_here):
        base = h * (sources + 2)
        weighted = columns[:, base:base + 1] * own_out_ref[:, h * HD:(h + 1) * HD].astype(jnp.float32)
        for b in range(sources):
            weighted = weighted + columns[:, base + 1 + b:base + 2 + b] * parts_ref[
                b, :rows, h * HD:(h + 1) * HD
            ].astype(jnp.float32)
        total = columns[:, base + sources + 1:base + sources + 2]
        out_ref[:, h * HD:(h + 1) * HD] = (weighted / total).astype(out_ref.dtype)


COLUMN_BLOCK = 2048


def combine(arrived_halves, own_out, own_log, out_weight):
    sources, packed_rows, width = arrived_halves[0].shape
    rows = own_out.shape[0]
    columns = out_weight.shape[1]
    return pl.pallas_call(
        combine_kernel,
        grid=(columns // COLUMN_BLOCK,),
        in_specs=[pl.BlockSpec((sources, packed_rows, width), lambda j: (0, 0, 0)) for _ in arrived_halves]
        + [
            pl.BlockSpec(own_out.shape, lambda j: (0, 0)),
            pl.BlockSpec(own_log.shape, lambda j: (0, 0)),
            pl.BlockSpec((out_weight.shape[0], COLUMN_BLOCK), lambda j: (0, j)),
        ],
        out_specs=pl.BlockSpec((rows, COLUMN_BLOCK), lambda j: (0, j)),
        out_shape=jax.ShapeDtypeStruct((rows, columns), jnp.bfloat16),
        scratch_shapes=[pltpu.VMEM(own_out.shape, jnp.bfloat16)],
        compiler_params=pltpu.CompilerParams(dimension_semantics=("arbitrary",)),
    )(*arrived_halves, own_out, own_log, out_weight)


def residual_kernel(position_ref, terms_ref, current_ref, out_ref):
    total = terms_ref[0].astype(jnp.float32)
    for n in range(1, terms_ref.shape[0]):
        total = total + terms_ref[n].astype(jnp.float32)
    mixed = (current_ref[...].astype(jnp.float32) + total).astype(out_ref.dtype)
    for n in range(out_ref.shape[0]):
        out_ref[n] = mixed


def residual(position, gathered_terms, current):
    sources, chunk, width = gathered_terms.shape
    grid_spec = pltpu.PrefetchScalarGridSpec(
        num_scalar_prefetch=1,
        grid=(1,),
        in_specs=[
            pl.BlockSpec((sources, chunk, width), lambda i, pos: (0, 0, 0)),
            pl.BlockSpec((chunk, width), lambda i, pos: (pos[0], 0)),
        ],
        out_specs=pl.BlockSpec((sources, chunk, width), lambda i, pos: (0, 0, 0)),
    )
    return pl.pallas_call(
        residual_kernel,
        grid_spec=grid_spec,
        out_shape=jax.ShapeDtypeStruct((sources, chunk, width), jnp.bfloat16),
    )(position, gathered_terms, current)


def shards(
    fresh,
    previous,
    span_index,
    cache_counts,
    norm_gain,
    w_query,
    w_keyval,
    w_out,
    cache_keys,
    cache_values,
):
    blocks = lax.axis_size("blk")
    position = lax.axis_index("blk")
    span_rows = fresh.shape[0]
    first_span = span_index[0]
    heads_here = w_query.shape[2] // HD
    odd_member = position % 2 == 1
    live = cache_counts[0, position].reshape(1)
    arrived = passed_along(previous[0], "segment", 1)
    current = jnp.where(lax.axis_index("segment") == 0, fresh, arrived)
    widened = current.astype(jnp.float32)
    normed = (
        widened
        * lax.rsqrt(jnp.mean(widened * widened, axis=-1, keepdims=True) + EPSILON)
        * norm_gain[0]
    ).astype(jnp.bfloat16)
    queries = jnp.dot(normed, w_query[0], preferred_element_type=jnp.float32).reshape(
        span_rows, heads_here, HD
    )
    queries = rotate(queries, first_span).astype(jnp.bfloat16).reshape(span_rows, heads_here * HD)
    projected = jnp.dot(normed, w_keyval[0], preferred_element_type=jnp.float32)
    as_key = rotate(projected[:, None, :], first_span)[:, 0, :].astype(jnp.bfloat16)
    mine = jnp.where(odd_member, projected.astype(jnp.bfloat16), as_key)
    partner = swapped(mine, "blk", 0)
    own_keys = jnp.where(odd_member, partner, mine)
    own_values = jnp.where(odd_member, mine, partner)
    partner, queries = lax.optimization_barrier((partner, queries))
    halves = 2
    half_rows = span_rows // halves
    arrived_halves = []
    for i in range(halves):
        half = queries[i * half_rows:(i + 1) * half_rows]
        every_query = lax.all_to_all(
            jnp.broadcast_to(half[None], (blocks,) + half.shape), "blk", 0, 0, tiled=True
        )
        held = cache_attention(live, every_query, cache_keys[0], cache_values[0])
        arrived_halves.append(lax.all_to_all(held, "blk", split_axis=0, concat_axis=0, tiled=True))
    query_rows = queries.reshape(span_rows * heads_here, HD)
    row_tokens = jnp.arange(span_rows * heads_here, dtype=jnp.int32) // heads_here
    causal = row_tokens[:, None] >= jnp.arange(span_rows, dtype=jnp.int32)[None, :]
    own_out, own_log = attend_rows(query_rows, own_keys, own_values, causal)
    own_out = own_out.reshape(span_rows, heads_here * HD)
    own_log = own_log.reshape(span_rows, heads_here).T
    head_terms = combine(arrived_halves, own_out, own_log, w_out[0])
    chunk = span_rows // blocks
    gathered_terms = lax.all_to_all(
        head_terms.reshape(blocks, chunk, -1), "blk", 0, 0, tiled=True
    )
    spread = residual(position.reshape(1), gathered_terms, current)
    mixed = lax.all_to_all(spread, "blk", 0, 0, tiled=True).reshape(span_rows, -1)
    return mixed[None]


def solution(mesh):
    placed = (
        P(),
        P("segment", None, None),
        P("segment"),
        P("segment", None),
        P("segment", None),
        P("segment", None, "blk"),
        P("segment", None, "blk"),
        P("segment", "blk", None),
        P("segment", "blk", None),
        P("segment", "blk", None),
    )
    return jax.shard_map(
        shards, mesh=mesh, in_specs=placed, out_specs=P("segment", None, None), check_vma=False
    )
```

```python
import jax
import jax.numpy as jnp
from jax import lax
from jax.sharding import PartitionSpec as P
from jax.experimental import pallas as pl
from jax.experimental.pallas import tpu as pltpu

KVH = 8
HD = 128


ROPE_BASE = 500000.0
EPSILON = 1e-05


def passed_along(block, axis, distance):
    devices = range(lax.axis_size(axis))
    route = [(i - distance, i) for i in devices if i - distance in devices]
    return lax.ppermute(block, axis, route)


def swapped(block, axis, distance):
    count = lax.axis_size(axis)
    route = []
    for low in range(count):
        high = low | 1 << distance
        if high != low and high < count:
            route += [(low, high), (high, low)]
    return lax.ppermute(block, axis, route)


def rotate(projected, first_span):
    length = projected.shape[0]
    half_width = projected.shape[-1] // 2
    positions = (first_span * length + jnp.arange(length, dtype=jnp.int32)).astype(jnp.float32)
    inverse = ROPE_BASE ** (
        -(jnp.arange(half_width, dtype=jnp.float32) * 2.0) / projected.shape[-1]
    )
    angles = positions[:, None] * inverse[None, :]
    cosine = jnp.cos(angles)[:, None, :]
    sine_table = jnp.sin(angles)[:, None, :]
    left_part = projected[..., :half_width]
    right_part = projected[..., half_width:]
    return jnp.concatenate(
        [
            left_part * cosine - right_part * sine_table,
            right_part * cosine + left_part * sine_table,
        ],
        axis=-1,
    )


def attend_rows(query_rows, key_rows, value_rows, allowed):
    scores = lax.dot_general(
        query_rows, key_rows, (((1,), (1,)), ((), ())), preferred_element_type=jnp.float32
    ) * query_rows.shape[-1] ** (-0.5)
    scores = jnp.where(allowed, scores, -jnp.inf)
    highest = jnp.max(scores, axis=-1, keepdims=True)
    weights = jnp.exp(scores - highest)
    totals = jnp.sum(weights, axis=-1, keepdims=True)
    partial_out = (
        jnp.dot(weights.astype(jnp.bfloat16), value_rows, preferred_element_type=jnp.float32)
        / totals
    ).astype(jnp.bfloat16)
    return (partial_out, (highest + jnp.log(totals))[:, 0])


def cache_kernel(live_ref, q_ref, k_ref, v_ref, out_ref):
    live = live_ref[0]
    keys = k_ref[...]
    values = v_ref[...]
    sources, rows = q_ref.shape[0], q_ref.shape[1]
    width = out_ref.shape[2]
    group = max(1, min(sources, 256 // rows))
    visible = lax.broadcasted_iota(jnp.int32, (1, keys.shape[0]), 1) < live
    bias = jnp.where(visible, 0.0, -jnp.inf).astype(jnp.float32)
    log_rows = {src: [] for src in range(sources)}
    for first in range(0, sources, group):
        members = list(range(first, min(first + group, sources)))
        for h in range(q_ref.shape[2] // HD):
            q = jnp.concatenate([q_ref[src, :, h * HD:(h + 1) * HD] for src in members], axis=0)
            scores = lax.dot_general(
                q, keys, (((1,), (1,)), ((), ())), preferred_element_type=jnp.float32
            ) * HD ** (-0.5) + bias
            highest = jnp.max(scores, axis=-1, keepdims=True)
            weights = jnp.exp(scores - highest)
            totals = jnp.sum(weights, axis=-1, keepdims=True)
            part = jnp.dot(weights.astype(jnp.bfloat16), values, preferred_element_type=jnp.float32)
            normalized = (part / totals).astype(out_ref.dtype)
            log_totals = highest + jnp.log(totals)
            for i, src in enumerate(members):
                out_ref[src, :rows, h * HD:(h + 1) * HD] = normalized[i * rows:(i + 1) * rows]
                log_col = jnp.broadcast_to(log_totals[i * rows:(i + 1) * rows], (rows, HD))
                rest = jnp.transpose(log_col)[0:1, :]
                for _ in range(3):
                    piece = rest.astype(jnp.bfloat16).astype(jnp.float32)
                    log_rows[src].append(piece)
                    rest = rest - piece
    for src in range(sources):
        rows_here = log_rows[src]
        if rows < width:
            rows_here = [jnp.concatenate([r, jnp.zeros((1, width - rows), jnp.float32)], axis=1) for r in rows_here]
        rows_here = rows_here + [jnp.zeros((1, width), jnp.float32)] * (out_ref.shape[1] - rows - len(rows_here))
        out_ref[src, rows:, :] = jnp.concatenate(rows_here, axis=0).astype(out_ref.dtype)


LOG_ROWS = 8


def cache_attention(live, every_query, cached_keys, cached_values):
    sources, span_rows, width = every_query.shape
    kv_heads = cached_keys.shape[1] // HD
    per_head = sources // kv_heads
    rows = cached_keys.shape[0]
    grid_spec = pltpu.PrefetchScalarGridSpec(
        num_scalar_prefetch=1,
        grid=(kv_heads,),
        in_specs=[
            pl.BlockSpec((per_head, span_rows, width), lambda g, live: (g, 0, 0)),
            pl.BlockSpec((rows, HD), lambda g, live: (0, g)),
            pl.BlockSpec((rows, HD), lambda g, live: (0, g)),
        ],
        out_specs=pl.BlockSpec((per_head, span_rows + LOG_ROWS, width), lambda g, live: (g, 0, 0)),
    )
    return pl.pallas_call(
        cache_kernel,
        grid_spec=grid_spec,
        out_shape=jax.ShapeDtypeStruct((sources, span_rows + LOG_ROWS, width), jnp.bfloat16),
    )(live, every_query, cached_keys, cached_values)


def combine_kernel(*refs):
    parts_refs = refs[:-5]
    own_out_ref, own_log_ref, weight_ref, out_ref, attended_ref = refs[-5:]

    @pl.when(pl.program_id(0) == 0)
    def _():
        rows = own_out_ref.shape[0] // len(parts_refs)
        for i, parts_ref in enumerate(parts_refs):
            combine_into(
                parts_ref,
                own_out_ref.at[pl.ds(i * rows, rows), :],
                own_log_ref.at[:, pl.ds(i * rows, rows)],
                attended_ref.at[pl.ds(i * rows, rows), :],
            )

    out_ref[...] = jnp.dot(
        attended_ref[...], weight_ref[...], preferred_element_type=jnp.float32
    ).astype(out_ref.dtype)


def combine_into(parts_ref, own_out_ref, own_log_ref, out_ref):
    sources = parts_ref.shape[0]
    rows = out_ref.shape[0]
    heads_here = out_ref.shape[1] // HD
    logs = [[] for _ in range(heads_here)]
    for b in range(sources):
        packed = parts_ref[b, rows:rows + LOG_ROWS, :rows].astype(jnp.float32)
        for h in range(heads_here):
            logs[h].append((packed[3 * h + 2:3 * h + 3] + packed[3 * h + 1:3 * h + 2]) + packed[3 * h:3 * h + 1])
    own_logs = own_log_ref[...]
    table_rows = []
    for h in range(heads_here):
        own_log = own_logs[h:h + 1]
        ceiling = own_log
        for lg in logs[h]:
            ceiling = jnp.maximum(ceiling, lg)
        own_factor = jnp.exp(own_log - ceiling)
        factors = [jnp.exp(lg - ceiling) for lg in logs[h]]
        total = own_factor
        for factor in factors:
            total = total + factor
        table_rows += [own_factor] + factors + [total]
    size = 128 * pl.cdiv(len(table_rows), 128)
    which = lax.broadcasted_iota(jnp.int32, (size, rows), 0)
    table = jnp.zeros((size, rows), jnp.float32)
    for j, row in enumerate(table_rows):
        table = jnp.where(which == j, jnp.broadcast_to(row, (size, rows)), table)
    columns = jnp.transpose(table)
    for h in range(heads_here):
        base = h * (sources + 2)
        weighted = columns[:, base:base + 1] * own_out_ref[:, h * HD:(h + 1) * HD].astype(jnp.float32)
        for b in range(sources):
            weighted = weighted + columns[:, base + 1 + b:base + 2 + b] * parts_ref[
                b, :rows, h * HD:(h + 1) * HD
            ].astype(jnp.float32)
        total = columns[:, base + sources + 1:base + sources + 2]
        out_ref[:, h * HD:(h + 1) * HD] = (weighted / total).astype(out_ref.dtype)


COLUMN_BLOCK = 4096


def combine(arrived_halves, own_out, own_log, out_weight):
    sources, packed_rows, width = arrived_halves[0].shape
    rows = own_out.shape[0]
    columns = out_weight.shape[1]
    return pl.pallas_call(
        combine_kernel,
        grid=(columns // COLUMN_BLOCK,),
        in_specs=[pl.BlockSpec((sources, packed_rows, width), lambda j: (0, 0, 0)) for _ in arrived_halves]
        + [
            pl.BlockSpec(own_out.shape, lambda j: (0, 0)),
            pl.BlockSpec(own_log.shape, lambda j: (0, 0)),
            pl.BlockSpec((out_weight.shape[0], COLUMN_BLOCK), lambda j: (0, j)),
        ],
        out_specs=pl.BlockSpec((rows, COLUMN_BLOCK), lambda j: (0, j)),
        out_shape=jax.ShapeDtypeStruct((rows, columns), jnp.bfloat16),
        scratch_shapes=[pltpu.VMEM(own_out.shape, jnp.bfloat16)],
        compiler_params=pltpu.CompilerParams(dimension_semantics=("arbitrary",)),
    )(*arrived_halves, own_out, own_log, out_weight)


def residual_kernel(position_ref, terms_ref, current_ref, out_ref):
    total = terms_ref[0].astype(jnp.float32)
    for n in range(1, terms_ref.shape[0]):
        total = total + terms_ref[n].astype(jnp.float32)
    mixed = (current_ref[...].astype(jnp.float32) + total).astype(out_ref.dtype)
    for n in range(out_ref.shape[0]):
        out_ref[n] = mixed


def residual(position, gathered_terms, current):
    sources, chunk, width = gathered_terms.shape
    grid_spec = pltpu.PrefetchScalarGridSpec(
        num_scalar_prefetch=1,
        grid=(1,),
        in_specs=[
            pl.BlockSpec((sources, chunk, width), lambda i, pos: (0, 0, 0)),
            pl.BlockSpec((chunk, width), lambda i, pos: (pos[0], 0)),
        ],
        out_specs=pl.BlockSpec((sources, chunk, width), lambda i, pos: (0, 0, 0)),
    )
    return pl.pallas_call(
        residual_kernel,
        grid_spec=grid_spec,
        out_shape=jax.ShapeDtypeStruct((sources, chunk, width), jnp.bfloat16),
    )(position, gathered_terms, current)


def shards(
    fresh,
    previous,
    span_index,
    cache_counts,
    norm_gain,
    w_query,
    w_keyval,
    w_out,
    cache_keys,
    cache_values,
):
    blocks = lax.axis_size("blk")
    position = lax.axis_index("blk")
    span_rows = fresh.shape[0]
    first_span = span_index[0]
    heads_here = w_query.shape[2] // HD
    odd_member = position % 2 == 1
    live = cache_counts[0, position].reshape(1)
    arrived = passed_along(previous[0], "segment", 1)
    current = jnp.where(lax.axis_index("segment") == 0, fresh, arrived)
    widened = current.astype(jnp.float32)
    normed = (
        widened
        * lax.rsqrt(jnp.mean(widened * widened, axis=-1, keepdims=True) + EPSILON)
        * norm_gain[0]
    ).astype(jnp.bfloat16)
    queries = jnp.dot(normed, w_query[0], preferred_element_type=jnp.float32).reshape(
        span_rows, heads_here, HD
    )
    queries = rotate(queries, first_span).astype(jnp.bfloat16).reshape(span_rows, heads_here * HD)
    projected = jnp.dot(normed, w_keyval[0], preferred_element_type=jnp.float32)
    as_key = rotate(projected[:, None, :], first_span)[:, 0, :].astype(jnp.bfloat16)
    mine = jnp.where(odd_member, projected.astype(jnp.bfloat16), as_key)
    partner = swapped(mine, "blk", 0)
    own_keys = jnp.where(odd_member, partner, mine)
    own_values = jnp.where(odd_member, mine, partner)
    partner, queries = lax.optimization_barrier((partner, queries))
    halves = 2
    half_rows = span_rows // halves
    arrived_halves = []
    for i in range(halves):
        half = queries[i * half_rows:(i + 1) * half_rows]
        every_query = lax.all_to_all(
            jnp.broadcast_to(half[None], (blocks,) + half.shape), "blk", 0, 0, tiled=True
        )
        held = cache_attention(live, every_query, cache_keys[0], cache_values[0])
        arrived_halves.append(lax.all_to_all(held, "blk", split_axis=0, concat_axis=0, tiled=True))
    query_rows = queries.reshape(span_rows * heads_here, HD)
    row_tokens = jnp.arange(span_rows * heads_here, dtype=jnp.int32) // heads_here
    causal = row_tokens[:, None] >= jnp.arange(span_rows, dtype=jnp.int32)[None, :]
    own_out, own_log = attend_rows(query_rows, own_keys, own_values, causal)
    own_out = own_out.reshape(span_rows, heads_here * HD)
    own_log = own_log.reshape(span_rows, heads_here).T
    head_terms = combine(arrived_halves, own_out, own_log, w_out[0])
    chunk = span_rows // blocks
    gathered_terms = lax.all_to_all(
        head_terms.reshape(blocks, chunk, -1), "blk", 0, 0, tiled=True
    )
    spread = residual(position.reshape(1), gathered_terms, current)
    mixed = lax.all_to_all(spread, "blk", 0, 0, tiled=True).reshape(span_rows, -1)
    return mixed[None]


def solution(mesh):
    placed = (
        P(),
        P("segment", None, None),
        P("segment"),
        P("segment", None),
        P("segment", None),
        P("segment", None, "blk"),
        P("segment", None, "blk"),
        P("segment", "blk", None),
        P("segment", "blk", None),
        P("segment", "blk", None),
    )
    return jax.shard_map(
        shards, mesh=mesh, in_specs=placed, out_specs=P("segment", None, None), check_vma=False
    )
```
